256 devices in a mesh: blk: 32 (over z, x_lo, core), col: 8 (over x_hi, y).
Axes of the slice: x: 4 (x_hi: 2, x_lo: 2; x = x_hi * 2 + x_lo), y: 4, z: 8, core: 2. Of those that a mesh axis runs over, the one named last changes fastest.
Arguments:
- feat1: bfloat16 [128, 384, 256], P('blk', 'col'), may hold values from -40 to 40
- feat2: bfloat16 [128, 384, 256], P('blk', 'col'), may hold values from -40 to 40
Outputs:
- flow: float32 [2, 128, 384], P(None, 'blk', 'col')
- grad_flow: float32 [2, 128, 384], P(None, 'blk', 'col')
- grad_warped: float32 [128, 384, 256], P('blk', 'col')
The draws below stay inside these ranges and needn't reach their ends.
All inputs are finite; a program needn't handle non-finite values.
Results may differ from the reference program's by a relative error of at most 0.0075.
Values may be sent and summed in bfloat16 or wider, within the bound.
No kernel may reach another device: no remote copies, remote signals or barrier semaphores. Data moves between devices by JAX's collectives and lax.ppermute only.
A program may use at most 64 MiB of HBM per device.

```python
import math
import jax
import jax.numpy as jnp
from jax import lax

C = 256
H = 128
W = 384


def make_pair(key):
    count = H * W
    base_two = jnp.clip(jax.random.normal(jax.random.fold_in(key, 11), (count, C), jnp.float32), -5.0, 5.0)
    base_one = jnp.clip(jax.random.normal(jax.random.fold_in(key, 12), (count, C), jnp.float32), -5.0, 5.0)
    target = base_two
    source = base_one
    return (source.reshape(H, W, C), target.reshape(H, W, C))


def draw_feat1(key, part):
    return make_pair(key)[0].astype(jnp.bfloat16)


def draw_feat2(key, part):
    return make_pair(key)[1].astype(jnp.bfloat16)


def setup_inputs(seed: int = 0) -> dict:
    streams_of = jax.random.split(jax.random.key(seed), 3)
    feat1 = draw_feat1(jax.random.fold_in(streams_of[2], 71), 0)
    feat2 = draw_feat2(jax.random.fold_in(streams_of[2], 71), 0)
    return dict(feat1=feat1, feat2=feat2)


ssim_one = 0.01
ssim_two = 0.03
charb_sq = 0.0001

def box_valid(padded):
    rows_out = padded.shape[0] - 2
    cols_out = padded.shape[1] - 2
    total = jnp.zeros((rows_out, cols_out) + padded.shape[2:], padded.dtype)
    for offset_r in range(3):
        for offset_c in range(3):
            total = total + padded[offset_r:offset_r + rows_out, offset_c:offset_c + cols_out]
    return total / 9.0

def box_zero(values):
    return box_valid(jnp.pad(values, ((1, 1), (1, 1), (0, 0))))

def ssim_loss(mean_y, var_y, cov_xy, mean_x, var_x):
    top = (2.0 * mean_x * mean_y + ssim_one) * (2.0 * cov_xy + ssim_two)
    bottom = (mean_x * mean_x + mean_y * mean_y + ssim_one) * (var_x + var_y + ssim_two)
    return jnp.sum((1.0 - top / bottom) * 0.5)

def local_terms(xpad, ypad):
    mean_x = box_valid(xpad)
    mean_y = box_valid(ypad)
    var_x = box_valid(xpad * xpad) - mean_x * mean_x
    var_y = box_valid(ypad * ypad) - mean_y * mean_y
    cov_xy = box_valid(xpad * ypad) - mean_x * mean_y
    loss, pull = jax.vjp(lambda one, two, three: ssim_loss(one, two, three, mean_x, var_x), mean_y, var_y, cov_xy)
    grad_mean, grad_var, grad_cov = pull(jnp.ones_like(loss))
    first = grad_mean - 2.0 * grad_var * mean_y - grad_cov * mean_x
    return (first, grad_var, grad_cov)

def edge_weight(lower, upper):
    return jnp.exp(-lax.optimization_barrier(jnp.mean(jnp.abs(upper - lower), axis=-1)))

def charbonnier(weight, delta):
    return weight * delta / jnp.sqrt(delta * delta + charb_sq)

def reference(feat1, feat2):
    count = H * W
    queries = feat1.reshape(count, C)
    keys = feat2.reshape(count, C)
    where_at = jnp.arange(count, dtype=jnp.int32)
    coord_y = ((where_at // W).astype(jnp.float32) + 0.5) * (2.0 / H) - 1.0
    coord_x = ((where_at % W).astype(jnp.float32) + 0.5) * (2.0 / W) - 1.0
    scale = 1.0 / math.sqrt(C)
    block = math.gcd(count, 2048)

    def match(query_block):
        score = jnp.dot(query_block, keys.T, preferred_element_type=jnp.float32) * scale
        top = lax.optimization_barrier(jnp.max(score, axis=1, keepdims=True))
        expo = jnp.exp(score - top)
        total = lax.optimization_barrier(jnp.sum(expo, axis=1))
        mixed = jnp.dot(expo.astype(jnp.bfloat16), keys, preferred_element_type=jnp.float32) / total[:, None]
        along_y = lax.optimization_barrier(jnp.sum(expo * coord_y[None, :], axis=1)) / total
        along_x = lax.optimization_barrier(jnp.sum(expo * coord_x[None, :], axis=1)) / total
        return (mixed, along_y, along_x)
    mixed, along_y, along_x = lax.map(match, queries.reshape(count // block, block, C))
    warped = mixed.reshape(H, W, C).astype(jnp.bfloat16)
    flow = jnp.stack([along_y.reshape(count) - coord_y, along_x.reshape(count) - coord_x]).reshape(2, H, W)
    xval = feat1.astype(jnp.float32)
    yval = warped.astype(jnp.float32)
    pad_x = jnp.pad(xval, ((1, 1), (1, 1), (0, 0)))
    pad_y = jnp.pad(yval, ((1, 1), (1, 1), (0, 0)))
    first, grad_var, grad_cov = local_terms(pad_x, pad_y)
    grad_warped = box_zero(first) + 2.0 * yval * box_zero(grad_var) + xval * box_zero(grad_cov)
    weight_y = edge_weight(xval[:-1], xval[1:])
    delta_y = flow[:, 1:, :] - flow[:, :-1, :]
    push_y = charbonnier(weight_y[None], delta_y)
    weight_x = edge_weight(xval[:, :-1], xval[:, 1:])
    delta_x = flow[:, :, 1:] - flow[:, :, :-1]
    push_x = charbonnier(weight_x[None], delta_x)
    grad_flow = jnp.pad(push_y, ((0, 0), (1, 0), (0, 0))) - jnp.pad(push_y, ((0, 0), (0, 1), (0, 0)))
    grad_flow = grad_flow + jnp.pad(push_x, ((0, 0), (0, 0), (1, 0))) - jnp.pad(push_x, ((0, 0), (0, 0), (0, 1)))
    return (flow, grad_flow, grad_warped)
```

```python
import math

import jax
import jax.numpy as jnp
from jax import lax
from jax.sharding import Mesh
from jax.sharding import PartitionSpec as P

ssim_one = 0.01
ssim_two = 0.03
charb_sq = 0.0001

FINE = ("z", "xl", "c", "xh", "y")
BLK = ("z", "xl", "c")
COL = ("xh", "y")
GATHER_ORDER = ("z", ("xh", "xl"), "y", "c")


def with_halo(value, sides, width):
    for axis, dim in sides:
        count, length = (lax.axis_size(axis), value.shape[dim])
        up = [(i, (i + 1) % count) for i in range(count - 1)]
        down = [(j, i) for i, j in up]
        last = lax.slice_in_dim(value, length - width, length, axis=dim)
        first = lax.slice_in_dim(value, 0, width, axis=dim)
        before = lax.ppermute(last, axis, up)
        after = lax.ppermute(first, axis, down)
        value = jnp.concatenate([before, value, after], axis=dim)
    return value


def box_valid(padded):
    rows_out = padded.shape[0] - 2
    cols_out = padded.shape[1] - 2
    total = jnp.zeros((rows_out, cols_out) + padded.shape[2:], padded.dtype)
    for offset_r in range(3):
        for offset_c in range(3):
            total = total + padded[offset_r : offset_r + rows_out, offset_c : offset_c + cols_out]
    return total / 9.0


def ssim_loss(mean_y, var_y, cov_xy, mean_x, var_x):
    top = (2.0 * mean_x * mean_y + ssim_one) * (2.0 * cov_xy + ssim_two)
    bottom = (mean_x * mean_x + mean_y * mean_y + ssim_one) * (var_x + var_y + ssim_two)
    return jnp.sum((1.0 - top / bottom) * 0.5)


def local_terms(xpad, ypad):
    mean_x = box_valid(xpad)
    mean_y = box_valid(ypad)
    var_x = box_valid(xpad * xpad) - mean_x * mean_x
    var_y = box_valid(ypad * ypad) - mean_y * mean_y
    cov_xy = box_valid(xpad * ypad) - mean_x * mean_y
    loss, pull = jax.vjp(
        lambda one, two, three: ssim_loss(one, two, three, mean_x, var_x), mean_y, var_y, cov_xy
    )
    grad_mean, grad_var, grad_cov = pull(jnp.ones_like(loss))
    first = grad_mean - 2.0 * grad_var * mean_y - grad_cov * mean_x
    return (first, grad_var, grad_cov)


def edge_weight(lower, upper):
    return jnp.exp(-jnp.mean(jnp.abs(upper - lower), axis=-1))


def charbonnier(weight, delta):
    return weight * delta / jnp.sqrt(delta * delta + charb_sq)


def absorb(carry, queries, keys, key_y, key_x, scale):
    total_keys = keys.shape[0]
    width = keys.shape[1]
    step = min(total_keys, 2048)
    while total_keys % step != 0:
        step = step - 1
    blocks = total_keys // step

    def visit(state, item):
        top, total, acc, along_y, along_x = state
        key_block, block_y, block_x = item
        score = (
            lax.dot_general(
                queries, key_block, (((1,), (1,)), ((), ())), preferred_element_type=jnp.float32
            )
            * scale
        )
        new_top = jnp.maximum(top, jnp.max(score, axis=1))
        shrink = jnp.exp(top - new_top)
        expo = jnp.exp(score - new_top[:, None])
        total = total * shrink + jnp.sum(expo, axis=1)
        acc = acc * shrink[:, None] + jnp.dot(
            expo.astype(jnp.bfloat16), key_block, preferred_element_type=jnp.float32
        )
        along_y = along_y * shrink + jnp.sum(expo * block_y[None, :], axis=1)
        along_x = along_x * shrink + jnp.sum(expo * block_x[None, :], axis=1)
        return ((new_top, total, acc, along_y, along_x), None)

    items = (
        keys.reshape(blocks, step, width),
        key_y.reshape(blocks, step),
        key_x.reshape(blocks, step),
    )
    carry, unused = lax.scan(visit, carry, items)
    return carry


def body(feat1, feat2):
    rows, cols, width = feat1.shape
    ncol = lax.axis_size(COL)
    full_rows = rows * lax.axis_size(BLK)
    full_cols = cols * ncol
    row_start = lax.axis_index(BLK) * rows
    col_start = lax.axis_index(COL) * cols
    scale = 1.0 / math.sqrt(width)
    tokens = rows * cols
    queries = feat1.reshape(tokens, width)
    init = (
        jnp.full((tokens,), -1e30, jnp.float32),
        jnp.zeros((tokens,), jnp.float32),
        jnp.zeros((tokens, width), jnp.float32),
        jnp.zeros((tokens,), jnp.float32),
        jnp.zeros((tokens,), jnp.float32),
    )

    def norm_y(index):
        return (index.astype(jnp.float32) + 0.5) * (2.0 / full_rows) - 1.0

    def norm_x(index):
        return (index.astype(jnp.float32) + 0.5) * (2.0 / full_cols) - 1.0

    piece = feat2
    for axis in GATHER_ORDER:
        piece = lax.all_gather(piece, axis, axis=0, tiled=True)
    count = piece.shape[0]
    gathered = jnp.arange(count, dtype=jnp.int32)
    rest = gathered // rows
    place = {}
    for axis in GATHER_ORDER:
        size = lax.axis_size(axis)
        place[axis] = rest % size
        rest = rest // size
    sz, sxl, sc, sxh, sy = (lax.axis_size(a) for a in FINE)
    x_full = place[("xh", "xl")]
    blk_of = (place["z"] * sxl + x_full % sxl) * sc + place["c"]
    col_of = (x_full // sxl) * sy + place["y"]
    tile_y = blk_of * rows + gathered % rows
    tile_x = col_of * cols
    grid_y = jnp.broadcast_to(tile_y[:, None], (count, cols))
    grid_x = tile_x[:, None] + jnp.arange(cols, dtype=jnp.int32)[None, :]
    carry = absorb(
        init,
        queries,
        piece.reshape(count * cols, width),
        norm_y(grid_y).reshape(-1),
        norm_x(grid_x).reshape(-1),
        scale,
    )
    top, total, acc, along_y, along_x = carry
    warped = (acc / total[:, None]).astype(jnp.bfloat16).reshape(rows, cols, width)
    own_y = norm_y(row_start + jnp.arange(rows, dtype=jnp.int32))
    own_x = norm_x(col_start + jnp.arange(cols, dtype=jnp.int32))
    flow = jnp.stack(
        [
            (along_y / total).reshape(rows, cols) - own_y[:, None],
            (along_x / total).reshape(rows, cols) - own_x[None, :],
        ]
    )
    pair = jnp.stack([feat1, warped])
    xval = feat1.astype(jnp.float32)
    yval = warped.astype(jnp.float32)
    margin = 1
    padded = with_halo(pair, ((BLK, 1), (COL, 2)), 1)
    xpad = padded[0].astype(jnp.float32)
    ypad = padded[1].astype(jnp.float32)
    first, grad_var, grad_cov = local_terms(xpad, ypad)
    maps = jnp.stack([first, grad_var, grad_cov])
    beside_all = with_halo(maps.astype(jnp.bfloat16), ((BLK, 1), (COL, 2)), 1).astype(
        maps.dtype
    )
    spread_first = box_valid(beside_all[0])
    spread_var = box_valid(beside_all[1])
    spread_cov = box_valid(beside_all[2])
    grad_warped = spread_first + 2.0 * yval * spread_var + xval * spread_cov
    flow_pad = with_halo(flow, ((BLK, 1), (COL, 2)), 1)
    x_rows = xpad[margin - 1 : margin + rows + 1, margin : margin + cols]
    x_cols = xpad[margin : margin + rows, margin - 1 : margin + cols + 1]
    edge_y = row_start - 1 + jnp.arange(rows + 1, dtype=jnp.int32)
    valid_y = (edge_y >= 0) & (edge_y <= full_rows - 2)
    edge_x = col_start - 1 + jnp.arange(cols + 1, dtype=jnp.int32)
    valid_x = (edge_x >= 0) & (edge_x <= full_cols - 2)
    delta_y = flow_pad[:, 1:, 1:-1] - flow_pad[:, :-1, 1:-1]
    push_y = jnp.where(
        valid_y[None, :, None],
        charbonnier(edge_weight(x_rows[:-1], x_rows[1:])[None], delta_y),
        0.0,
    )
    delta_x = flow_pad[:, 1:-1, 1:] - flow_pad[:, 1:-1, :-1]
    push_x = jnp.where(
        valid_x[None, None, :],
        charbonnier(edge_weight(x_cols[:, :-1], x_cols[:, 1:])[None], delta_x),
        0.0,
    )
    grad_flow = push_y[:, :rows] - push_y[:, 1:] + push_x[:, :, :cols] - push_x[:, :, 1:]
    return (flow, grad_flow, grad_warped)


def solution(mesh):
    blk, col = mesh.devices.shape
    fine = mesh.devices.reshape(blk // 4, 2, 2, 2, col // 2)
    fine_mesh = Mesh(fine, FINE)
    placed = (P(BLK, COL, None), P(BLK, COL, None))
    return jax.shard_map(
        body,
        mesh=fine_mesh,
        in_specs=placed,
        out_specs=(P(None, BLK, COL), P(None, BLK, COL), P(BLK, COL, None)),
        check_vma=False,
    )
```

```python
import math

import jax
import jax.numpy as jnp
from jax import lax
from jax.sharding import Mesh
from jax.sharding import PartitionSpec as P

ssim_one = 0.01
ssim_two = 0.03
charb_sq = 0.0001

FINE = ("z", "xl", "c", "xh", "y")
BLK = ("z", "xl", "c")
COL = ("xh", "y")
KEY_AXES = ("z", ("xh", "xl"))
QUERY_AXES = ("y", "c")


def with_halo(value, sides, width):
    for axis, dim in sides:
        count, length = (lax.axis_size(axis), value.shape[dim])
        up = [(i, (i + 1) % count) for i in range(count - 1)]
        down = [(j, i) for i, j in up]
        last = lax.slice_in_dim(value, length - width, length, axis=dim)
        first = lax.slice_in_dim(value, 0, width, axis=dim)
        before = lax.ppermute(last, axis, up)
        after = lax.ppermute(first, axis, down)
        value = jnp.concatenate([before, value, after], axis=dim)
    return value


def box_valid(padded):
    rows_out = padded.shape[0] - 2
    cols_out = padded.shape[1] - 2
    total = jnp.zeros((rows_out, cols_out) + padded.shape[2:], padded.dtype)
    for offset_r in range(3):
        for offset_c in range(3):
            total = total + padded[offset_r : offset_r + rows_out, offset_c : offset_c + cols_out]
    return total / 9.0


def ssim_loss(mean_y, var_y, cov_xy, mean_x, var_x):
    top = (2.0 * mean_x * mean_y + ssim_one) * (2.0 * cov_xy + ssim_two)
    bottom = (mean_x * mean_x + mean_y * mean_y + ssim_one) * (var_x + var_y + ssim_two)
    return jnp.sum((1.0 - top / bottom) * 0.5)


def local_terms(xpad, ypad):
    mean_x = box_valid(xpad)
    mean_y = box_valid(ypad)
    var_x = box_valid(xpad * xpad) - mean_x * mean_x
    var_y = box_valid(ypad * ypad) - mean_y * mean_y
    cov_xy = box_valid(xpad * ypad) - mean_x * mean_y
    loss, pull = jax.vjp(
        lambda one, two, three: ssim_loss(one, two, three, mean_x, var_x), mean_y, var_y, cov_xy
    )
    grad_mean, grad_var, grad_cov = pull(jnp.ones_like(loss))
    first = grad_mean - 2.0 * grad_var * mean_y - grad_cov * mean_x
    return (first, grad_var, grad_cov)


def edge_weight(lower, upper):
    return jnp.exp(-jnp.mean(jnp.abs(upper - lower), axis=-1))


def charbonnier(weight, delta):
    return weight * delta / jnp.sqrt(delta * delta + charb_sq)


def absorb(carry, queries, keys, key_y, key_x, scale):
    total_keys = keys.shape[0]
    width = keys.shape[1]
    step = min(total_keys, 2048)
    while total_keys % step != 0:
        step = step - 1
    blocks = total_keys // step

    def visit(state, item):
        top, total, acc, along_y, along_x = state
        key_block, block_y, block_x = item
        score = (
            lax.dot_general(
                queries, key_block, (((1,), (1,)), ((), ())), preferred_element_type=jnp.float32
            )
            * scale
        )
        new_top = jnp.maximum(top, jnp.max(score, axis=1))
        shrink = jnp.exp(top - new_top)
        expo = jnp.exp(score - new_top[:, None])
        total = total * shrink + jnp.sum(expo, axis=1)
        acc = acc * shrink[:, None] + jnp.dot(
            expo.astype(jnp.bfloat16), key_block, preferred_element_type=jnp.float32
        )
        along_y = along_y * shrink + jnp.sum(expo * block_y[None, :], axis=1)
        along_x = along_x * shrink + jnp.sum(expo * block_x[None, :], axis=1)
        return ((new_top, total, acc, along_y, along_x), None)

    items = (
        keys.reshape(blocks, step, width),
        key_y.reshape(blocks, step),
        key_x.reshape(blocks, step),
    )
    carry, unused = lax.scan(visit, carry, items)
    return carry


def body(feat1, feat2):
    rows, cols, width = feat1.shape
    ncol = lax.axis_size(COL)
    full_rows = rows * lax.axis_size(BLK)
    full_cols = cols * ncol
    row_start = lax.axis_index(BLK) * rows
    col_start = lax.axis_index(COL) * cols
    scale = 1.0 / math.sqrt(width)
    tokens = rows * cols
    queries = lax.all_gather(feat1.reshape(tokens, width), QUERY_AXES, axis=0, tiled=True)
    group = queries.shape[0]
    init = (
        jnp.full((group,), -1e30, jnp.float32),
        jnp.zeros((group,), jnp.float32),
        jnp.zeros((group, width), jnp.float32),
        jnp.zeros((group,), jnp.float32),
        jnp.zeros((group,), jnp.float32),
    )

    def norm_y(index):
        return (index.astype(jnp.float32) + 0.5) * (2.0 / full_rows) - 1.0

    def norm_x(index):
        return (index.astype(jnp.float32) + 0.5) * (2.0 / full_cols) - 1.0

    piece = feat2
    for axis in KEY_AXES:
        piece = lax.all_gather(piece, axis, axis=0, tiled=True)
    count = piece.shape[0]
    gathered = jnp.arange(count, dtype=jnp.int32)
    rest = gathered // rows
    place = {}
    for axis in KEY_AXES:
        size = lax.axis_size(axis)
        place[axis] = rest % size
        rest = rest // size
    sz, sxl, sc, sxh, sy = (lax.axis_size(a) for a in FINE)
    x_full = place[("xh", "xl")]
    blk_of = (place["z"] * sxl + x_full % sxl) * sc + lax.axis_index("c")
    col_of = (x_full // sxl) * sy + lax.axis_index("y")
    tile_y = blk_of * rows + gathered % rows
    tile_x = col_of * cols
    grid_y = jnp.broadcast_to(tile_y[:, None], (count, cols))
    grid_x = tile_x[:, None] + jnp.arange(cols, dtype=jnp.int32)[None, :]
    carry = absorb(
        init,
        queries,
        piece.reshape(count * cols, width),
        norm_y(grid_y).reshape(-1),
        norm_x(grid_x).reshape(-1),
        scale,
    )
    top, total, acc, along_y, along_x = carry
    peak = lax.pmax(top, QUERY_AXES)
    factor = jnp.exp(top - peak)
    acc = lax.psum_scatter(acc * factor[:, None], QUERY_AXES, scatter_dimension=0, tiled=True)
    stats = jnp.stack([total * factor, along_y * factor, along_x * factor])
    stats = lax.psum_scatter(stats, QUERY_AXES, scatter_dimension=1, tiled=True)
    total, along_y, along_x = stats[0], stats[1], stats[2]
    warped = (acc / total[:, None]).astype(jnp.bfloat16).reshape(rows, cols, width)
    own_y = norm_y(row_start + jnp.arange(rows, dtype=jnp.int32))
    own_x = norm_x(col_start + jnp.arange(cols, dtype=jnp.int32))
    flow = jnp.stack(
        [
            (along_y / total).reshape(rows, cols) - own_y[:, None],
            (along_x / total).reshape(rows, cols) - own_x[None, :],
        ]
    )
    pair = jnp.stack([feat1, warped])
    xval = feat1.astype(jnp.float32)
    yval = warped.astype(jnp.float32)
    margin = 1
    padded = with_halo(pair, ((BLK, 1), (COL, 2)), 1)
    xpad = padded[0].astype(jnp.float32)
    ypad = padded[1].astype(jnp.float32)
    first, grad_var, grad_cov = local_terms(xpad, ypad)
    maps = jnp.stack([first, grad_var, grad_cov])
    beside_all = with_halo(maps.astype(jnp.bfloat16), ((BLK, 1), (COL, 2)), 1).astype(
        maps.dtype
    )
    spread_first = box_valid(beside_all[0])
    spread_var = box_valid(beside_all[1])
    spread_cov = box_valid(beside_all[2])
    grad_warped = spread_first + 2.0 * yval * spread_var + xval * spread_cov
    flow_pad = with_halo(flow, ((BLK, 1), (COL, 2)), 1)
    x_rows = xpad[margin - 1 : margin + rows + 1, margin : margin + cols]
    x_cols = xpad[margin : margin + rows, margin - 1 : margin + cols + 1]
    edge_y = row_start - 1 + jnp.arange(rows + 1, dtype=jnp.int32)
    valid_y = (edge_y >= 0) & (edge_y <= full_rows - 2)
    edge_x = col_start - 1 + jnp.arange(cols + 1, dtype=jnp.int32)
    valid_x = (edge_x >= 0) & (edge_x <= full_cols - 2)
    delta_y = flow_pad[:, 1:, 1:-1] - flow_pad[:, :-1, 1:-1]
    push_y = jnp.where(
        valid_y[None, :, None],
        charbonnier(edge_weight(x_rows[:-1], x_rows[1:])[None], delta_y),
        0.0,
    )
    delta_x = flow_pad[:, 1:-1, 1:] - flow_pad[:, 1:-1, :-1]
    push_x = jnp.where(
        valid_x[None, None, :],
        charbonnier(edge_weight(x_cols[:, :-1], x_cols[:, 1:])[None], delta_x),
        0.0,
    )
    grad_flow = push_y[:, :rows] - push_y[:, 1:] + push_x[:, :, :cols] - push_x[:, :, 1:]
    return (flow, grad_flow, grad_warped)


def solution(mesh):
    blk, col = mesh.devices.shape
    fine = mesh.devices.reshape(blk // 4, 2, 2, 2, col // 2)
    fine_mesh = Mesh(fine, FINE)
    placed = (P(BLK, COL, None), P(BLK, COL, None))
    return jax.shard_map(
        body,
        mesh=fine_mesh,
        in_specs=placed,
        out_specs=(P(None, BLK, COL), P(None, BLK, COL), P(BLK, COL, None)),
        check_vma=False,
    )
```

```python
import math

import jax
import jax.numpy as jnp
from jax import lax
from jax.sharding import Mesh
from jax.sharding import PartitionSpec as P

ssim_one = 0.01
ssim_two = 0.03
charb_sq = 0.0001

FINE = ("z", "xl", "c", "xh", "y")
BLK = ("z", "xl", "c")
COL = ("xh", "y")
KEY_AXES = ("z", ("xh", "xl"))
QUERY_AXES = ("y", "c")


def with_halo(value, sides, width):
    for axis, dim in sides:
        count, length = (lax.axis_size(axis), value.shape[dim])
        up = [(i, (i + 1) % count) for i in range(count - 1)]
        down = [(j, i) for i, j in up]
        last = lax.slice_in_dim(value, length - width, length, axis=dim)
        first = lax.slice_in_dim(value, 0, width, axis=dim)
        before = lax.ppermute(last, axis, up)
        after = lax.ppermute(first, axis, down)
        value = jnp.concatenate([before, value, after], axis=dim)
    return value


def box_valid(padded):
    rows_out = padded.shape[0] - 2
    cols_out = padded.shape[1] - 2
    total = jnp.zeros((rows_out, cols_out) + padded.shape[2:], padded.dtype)
    for offset_r in range(3):
        for offset_c in range(3):
            total = total + padded[offset_r : offset_r + rows_out, offset_c : offset_c + cols_out]
    return total / 9.0


def ssim_loss(mean_y, var_y, cov_xy, mean_x, var_x):
    top = (2.0 * mean_x * mean_y + ssim_one) * (2.0 * cov_xy + ssim_two)
    bottom = (mean_x * mean_x + mean_y * mean_y + ssim_one) * (var_x + var_y + ssim_two)
    return jnp.sum((1.0 - top / bottom) * 0.5)


def local_terms(xpad, ypad):
    mean_x = box_valid(xpad)
    mean_y = box_valid(ypad)
    var_x = box_valid(xpad * xpad) - mean_x * mean_x
    var_y = box_valid(ypad * ypad) - mean_y * mean_y
    cov_xy = box_valid(xpad * ypad) - mean_x * mean_y
    loss, pull = jax.vjp(
        lambda one, two, three: ssim_loss(one, two, three, mean_x, var_x), mean_y, var_y, cov_xy
    )
    grad_mean, grad_var, grad_cov = pull(jnp.ones_like(loss))
    first = grad_mean - 2.0 * grad_var * mean_y - grad_cov * mean_x
    return (first, grad_var, grad_cov)


def edge_weight(lower, upper):
    return jnp.exp(-jnp.mean(jnp.abs(upper - lower), axis=-1))


def charbonnier(weight, delta):
    return weight * delta / jnp.sqrt(delta * delta + charb_sq)


def absorb(carry, queries, keys, key_y, key_x, scale):
    total_keys = keys.shape[0]
    width = keys.shape[1]
    step = min(total_keys, 2048)
    while total_keys % step != 0:
        step = step - 1
    blocks = total_keys // step

    def visit(state, item):
        top, total, acc, along_y, along_x = state
        key_block, block_y, block_x = item
        score = (
            lax.dot_general(
                queries, key_block, (((1,), (1,)), ((), ())), preferred_element_type=jnp.float32
            )
            * scale
        )
        new_top = jnp.maximum(top, jnp.max(score, axis=1))
        shrink = jnp.exp(top - new_top)
        expo = jnp.exp(score - new_top[:, None])
        total = total * shrink + jnp.sum(expo, axis=1)
        acc = acc * shrink[:, None] + jnp.dot(
            expo.astype(jnp.bfloat16), key_block, preferred_element_type=jnp.float32
        )
        along_y = along_y * shrink + jnp.sum(expo * block_y[None, :], axis=1)
        along_x = along_x * shrink + jnp.sum(expo * block_x[None, :], axis=1)
        return ((new_top, total, acc, along_y, along_x), None)

    items = (
        keys.reshape(blocks, step, width),
        key_y.reshape(blocks, step),
        key_x.reshape(blocks, step),
    )
    carry, unused = lax.scan(visit, carry, items)
    return carry


def body(feat1, feat2):
    rows, cols, width = feat1.shape
    ncol = lax.axis_size(COL)
    full_rows = rows * lax.axis_size(BLK)
    full_cols = cols * ncol
    row_start = lax.axis_index(BLK) * rows
    col_start = lax.axis_index(COL) * cols
    scale = 1.0 / math.sqrt(width)
    tokens = rows * cols
    queries = lax.all_gather(feat1.reshape(tokens, width), QUERY_AXES, axis=0, tiled=True)
    group = queries.shape[0]
    init = (
        jnp.full((group,), -1e30, jnp.float32),
        jnp.zeros((group,), jnp.float32),
        jnp.zeros((group, width), jnp.float32),
        jnp.zeros((group,), jnp.float32),
        jnp.zeros((group,), jnp.float32),
    )

    def norm_y(index):
        return (index.astype(jnp.float32) + 0.5) * (2.0 / full_rows) - 1.0

    def norm_x(index):
        return (index.astype(jnp.float32) + 0.5) * (2.0 / full_cols) - 1.0

    piece = feat2
    for axis in KEY_AXES:
        piece = lax.all_gather(piece, axis, axis=0, tiled=True)
    count = piece.shape[0]
    gathered = jnp.arange(count, dtype=jnp.int32)
    rest = gathered // rows
    place = {}
    for axis in KEY_AXES:
        size = lax.axis_size(axis)
        place[axis] = rest % size
        rest = rest // size
    sz, sxl, sc, sxh, sy = (lax.axis_size(a) for a in FINE)
    x_full = place[("xh", "xl")]
    blk_of = (place["z"] * sxl + x_full % sxl) * sc + lax.axis_index("c")
    col_of = (x_full // sxl) * sy + lax.axis_index("y")
    tile_y = blk_of * rows + gathered % rows
    tile_x = col_of * cols
    grid_y = jnp.broadcast_to(tile_y[:, None], (count, cols))
    grid_x = tile_x[:, None] + jnp.arange(cols, dtype=jnp.int32)[None, :]
    carry = absorb(
        init,
        queries,
        piece.reshape(count * cols, width),
        norm_y(grid_y).reshape(-1),
        norm_x(grid_x).reshape(-1),
        scale,
    )
    top, total, acc, along_y, along_x = carry
    parts = lax.axis_size(QUERY_AXES)
    stats = jnp.stack([top, total, along_y, along_x]).reshape(4, parts, tokens)
    stats = jnp.pad(stats.transpose(1, 0, 2), ((0, 0), (0, 0), (0, width - tokens)))
    packed = jnp.concatenate([acc.reshape(parts, tokens, width), stats], axis=1)
    packed = lax.all_to_all(packed, QUERY_AXES, 0, 0, tiled=True)
    tops = packed[:, tokens, :tokens]
    peak = jnp.max(tops, axis=0)
    factor = jnp.exp(tops - peak[None])
    acc = jnp.sum(packed[:, :tokens, :] * factor[:, :, None], axis=0)
    total = jnp.sum(packed[:, tokens + 1, :tokens] * factor, axis=0)
    along_y = jnp.sum(packed[:, tokens + 2, :tokens] * factor, axis=0)
    along_x = jnp.sum(packed[:, tokens + 3, :tokens] * factor, axis=0)
    warped = (acc / total[:, None]).astype(jnp.bfloat16).reshape(rows, cols, width)
    own_y = norm_y(row_start + jnp.arange(rows, dtype=jnp.int32))
    own_x = norm_x(col_start + jnp.arange(cols, dtype=jnp.int32))
    flow = jnp.stack(
        [
            (along_y / total).reshape(rows, cols) - own_y[:, None],
            (along_x / total).reshape(rows, cols) - own_x[None, :],
        ]
    )
    pair = jnp.stack([feat1, warped])
    xval = feat1.astype(jnp.float32)
    yval = warped.astype(jnp.float32)
    margin = 1
    padded = with_halo(pair, ((BLK, 1), (COL, 2)), 1)
    xpad = padded[0].astype(jnp.float32)
    ypad = padded[1].astype(jnp.float32)
    first, grad_var, grad_cov = local_terms(xpad, ypad)
    maps = jnp.stack([first, grad_var, grad_cov])
    beside_all = with_halo(maps.astype(jnp.bfloat16), ((BLK, 1), (COL, 2)), 1).astype(
        maps.dtype
    )
    spread_first = box_valid(beside_all[0])
    spread_var = box_valid(beside_all[1])
    spread_cov = box_valid(beside_all[2])
    grad_warped = spread_first + 2.0 * yval * spread_var + xval * spread_cov
    flow_pad = with_halo(flow, ((BLK, 1), (COL, 2)), 1)
    x_rows = xpad[margin - 1 : margin + rows + 1, margin : margin + cols]
    x_cols = xpad[margin : margin + rows, margin - 1 : margin + cols + 1]
    edge_y = row_start - 1 + jnp.arange(rows + 1, dtype=jnp.int32)
    valid_y = (edge_y >= 0) & (edge_y <= full_rows - 2)
    edge_x = col_start - 1 + jnp.arange(cols + 1, dtype=jnp.int32)
    valid_x = (edge_x >= 0) & (edge_x <= full_cols - 2)
    delta_y = flow_pad[:, 1:, 1:-1] - flow_pad[:, :-1, 1:-1]
    push_y = jnp.where(
        valid_y[None, :, None],
        charbonnier(edge_weight(x_rows[:-1], x_rows[1:])[None], delta_y),
        0.0,
    )
    delta_x = flow_pad[:, 1:-1, 1:] - flow_pad[:, 1:-1, :-1]
    push_x = jnp.where(
        valid_x[None, None, :],
        charbonnier(edge_weight(x_cols[:, :-1], x_cols[:, 1:])[None], delta_x),
        0.0,
    )
    grad_flow = push_y[:, :rows] - push_y[:, 1:] + push_x[:, :, :cols] - push_x[:, :, 1:]
    return (flow, grad_flow, grad_warped)


def solution(mesh):
    blk, col = mesh.devices.shape
    fine = mesh.devices.reshape(blk // 4, 2, 2, 2, col // 2)
    fine_mesh = Mesh(fine, FINE)
    placed = (P(BLK, COL, None), P(BLK, COL, None))
    return jax.shard_map(
        body,
        mesh=fine_mesh,
        in_specs=placed,
        out_specs=(P(None, BLK, COL), P(None, BLK, COL), P(BLK, COL, None)),
        check_vma=False,
    )
```

```python
import math

import jax
import jax.numpy as jnp
from jax import lax
from jax.experimental import pallas as pl
from jax.experimental.pallas import tpu as pltpu
from jax.sharding import Mesh
from jax.sharding import PartitionSpec as P

ssim_one = 0.01
ssim_two = 0.03
charb_sq = 0.0001

FINE = ("z", "xl", "c", "xh", "y")
BLK = ("z", "xl", "c")
COL = ("xh", "y")
KEY_AXES = ("z", ("xh", "xl"))
QUERY_AXES = ("y", "c")
BLOCK_Q = 512
BLOCK_K = 1024


def with_halo(value, sides, width):
    for axis, dim in sides:
        count, length = (lax.axis_size(axis), value.shape[dim])
        up = [(i, (i + 1) % count) for i in range(count - 1)]
        down = [(j, i) for i, j in up]
        last = lax.slice_in_dim(value, length - width, length, axis=dim)
        first = lax.slice_in_dim(value, 0, width, axis=dim)
        before = lax.ppermute(last, axis, up)
        after = lax.ppermute(first, axis, down)
        value = jnp.concatenate([before, value, after], axis=dim)
    return value


def box_valid(padded):
    rows_out = padded.shape[0] - 2
    cols_out = padded.shape[1] - 2
    total = jnp.zeros((rows_out, cols_out) + padded.shape[2:], padded.dtype)
    for offset_r in range(3):
        for offset_c in range(3):
            total = total + padded[offset_r : offset_r + rows_out, offset_c : offset_c + cols_out]
    return total / 9.0


def ssim_loss(mean_y, var_y, cov_xy, mean_x, var_x):
    top = (2.0 * mean_x * mean_y + ssim_one) * (2.0 * cov_xy + ssim_two)
    bottom = (mean_x * mean_x + mean_y * mean_y + ssim_one) * (var_x + var_y + ssim_two)
    return jnp.sum((1.0 - top / bottom) * 0.5)


def local_terms(xpad, ypad):
    mean_x = box_valid(xpad)
    mean_y = box_valid(ypad)
    var_x = box_valid(xpad * xpad) - mean_x * mean_x
    var_y = box_valid(ypad * ypad) - mean_y * mean_y
    cov_xy = box_valid(xpad * ypad) - mean_x * mean_y
    loss, pull = jax.vjp(
        lambda one, two, three: ssim_loss(one, two, three, mean_x, var_x), mean_y, var_y, cov_xy
    )
    grad_mean, grad_var, grad_cov = pull(jnp.ones_like(loss))
    first = grad_mean - 2.0 * grad_var * mean_y - grad_cov * mean_x
    return (first, grad_var, grad_cov)


def edge_weight(lower, upper):
    return jnp.exp(-jnp.mean(jnp.abs(upper - lower), axis=-1))


def charbonnier(weight, delta):
    return weight * delta / jnp.sqrt(delta * delta + charb_sq)


def flash_partials(queries, keys, key_y, key_x, scale, block_q, block_k):
    nq, width = queries.shape
    nk = keys.shape[0]
    grid = (nq // block_q, nk // block_k)
    last = grid[1] - 1

    def kernel(q_ref, k_ref, y_ref, x_ref, top_ref, total_ref, acc_ref, ay_ref, ax_ref,
               m_sc, l_sc, acc_sc, ay_sc, ax_sc):
        step = pl.program_id(1)

        @pl.when(step == 0)
        def _():
            m_sc[...] = jnp.full(m_sc.shape, -1e30, jnp.float32)
            l_sc[...] = jnp.zeros(l_sc.shape, jnp.float32)
            acc_sc[...] = jnp.zeros(acc_sc.shape, jnp.float32)
            ay_sc[...] = jnp.zeros(ay_sc.shape, jnp.float32)
            ax_sc[...] = jnp.zeros(ax_sc.shape, jnp.float32)

        k = k_ref[...]
        score = lax.dot_general(q_ref[...], k, (((1,), (1,)), ((), ())),
                                preferred_element_type=jnp.float32) * scale
        m_prev = m_sc[...]
        m_new = jnp.maximum(m_prev, jnp.max(score, axis=1, keepdims=True))
        shrink = jnp.exp(m_prev - m_new)
        expo = jnp.exp(score - m_new)
        l_sc[...] = l_sc[...] * shrink + jnp.sum(expo, axis=1, keepdims=True)
        ay_sc[...] = ay_sc[...] * shrink + jnp.sum(expo * y_ref[...], axis=1, keepdims=True)
        ax_sc[...] = ax_sc[...] * shrink + jnp.sum(expo * x_ref[...], axis=1, keepdims=True)
        acc_sc[...] = acc_sc[...] * shrink + jnp.dot(expo.astype(jnp.bfloat16), k,
                                                     preferred_element_type=jnp.float32)
        m_sc[...] = m_new

        @pl.when(step == last)
        def _():
            top_ref[...] = m_sc[...]
            total_ref[...] = l_sc[...]
            acc_ref[...] = acc_sc[...]
            ay_ref[...] = ay_sc[...]
            ax_ref[...] = ax_sc[...]

    col = pl.BlockSpec((block_q, 1), lambda i, j: (i, 0))
    outs = pl.pallas_call(
        kernel,
        grid=grid,
        in_specs=[
            pl.BlockSpec((block_q, width), lambda i, j: (i, 0)),
            pl.BlockSpec((block_k, width), lambda i, j: (j, 0)),
            pl.BlockSpec((1, block_k), lambda i, j: (0, j)),
            pl.BlockSpec((1, block_k), lambda i, j: (0, j)),
        ],
        out_specs=[col, col, pl.BlockSpec((block_q, width), lambda i, j: (i, 0)), col, col],
        out_shape=[
            jax.ShapeDtypeStruct((nq, 1), jnp.float32),
            jax.ShapeDtypeStruct((nq, 1), jnp.float32),
            jax.ShapeDtypeStruct((nq, width), jnp.float32),
            jax.ShapeDtypeStruct((nq, 1), jnp.float32),
            jax.ShapeDtypeStruct((nq, 1), jnp.float32),
        ],
        scratch_shapes=[
            pltpu.VMEM((block_q, 1), jnp.float32),
            pltpu.VMEM((block_q, 1), jnp.float32),
            pltpu.VMEM((block_q, width), jnp.float32),
            pltpu.VMEM((block_q, 1), jnp.float32),
            pltpu.VMEM((block_q, 1), jnp.float32),
        ],
        compiler_params=pltpu.CompilerParams(dimension_semantics=("arbitrary", "arbitrary")),
    )(queries, keys, key_y.reshape(1, nk), key_x.reshape(1, nk))
    top, total, acc, ay, ax = outs
    return top[:, 0], total[:, 0], acc, ay[:, 0], ax[:, 0]


def body(feat1, feat2):
    rows, cols, width = feat1.shape
    ncol = lax.axis_size(COL)
    full_rows = rows * lax.axis_size(BLK)
    full_cols = cols * ncol
    row_start = lax.axis_index(BLK) * rows
    col_start = lax.axis_index(COL) * cols
    scale = 1.0 / math.sqrt(width)
    tokens = rows * cols
    queries = lax.all_gather(feat1.reshape(tokens, width), QUERY_AXES, axis=0, tiled=True)

    def norm_y(index):
        return (index.astype(jnp.float32) + 0.5) * (2.0 / full_rows) - 1.0

    def norm_x(index):
        return (index.astype(jnp.float32) + 0.5) * (2.0 / full_cols) - 1.0

    piece = feat2
    for axis in KEY_AXES:
        piece = lax.all_gather(piece, axis, axis=0, tiled=True)
    count = piece.shape[0]
    gathered = jnp.arange(count, dtype=jnp.int32)
    rest = gathered // rows
    place = {}
    for axis in KEY_AXES:
        size = lax.axis_size(axis)
        place[axis] = rest % size
        rest = rest // size
    sz, sxl, sc, sxh, sy = (lax.axis_size(a) for a in FINE)
    x_full = place[("xh", "xl")]
    blk_of = (place["z"] * sxl + x_full % sxl) * sc + lax.axis_index("c")
    col_of = (x_full // sxl) * sy + lax.axis_index("y")
    tile_y = blk_of * rows + gathered % rows
    tile_x = col_of * cols
    grid_y = jnp.broadcast_to(tile_y[:, None], (count, cols))
    grid_x = tile_x[:, None] + jnp.arange(cols, dtype=jnp.int32)[None, :]
    carry = flash_partials(
        queries,
        piece.reshape(count * cols, width),
        norm_y(grid_y).reshape(-1),
        norm_x(grid_x).reshape(-1),
        scale,
        BLOCK_Q,
        BLOCK_K,
    )
    top, total, acc, along_y, along_x = carry
    parts = lax.axis_size(QUERY_AXES)
    stats = jnp.stack([top, total, along_y, along_x]).reshape(4, parts, tokens)
    stats = jnp.pad(stats.transpose(1, 0, 2), ((0, 0), (0, 0), (0, width - tokens)))
    packed = jnp.concatenate([acc.reshape(parts, tokens, width), stats], axis=1)
    packed = lax.all_to_all(packed, QUERY_AXES, 0, 0, tiled=True)
    tops = packed[:, tokens, :tokens]
    peak = jnp.max(tops, axis=0)
    factor = jnp.exp(tops - peak[None])
    acc = jnp.sum(packed[:, :tokens, :] * factor[:, :, None], axis=0)
    total = jnp.sum(packed[:, tokens + 1, :tokens] * factor, axis=0)
    along_y = jnp.sum(packed[:, tokens + 2, :tokens] * factor, axis=0)
    along_x = jnp.sum(packed[:, tokens + 3, :tokens] * factor, axis=0)
    warped = (acc / total[:, None]).astype(jnp.bfloat16).reshape(rows, cols, width)
    own_y = norm_y(row_start + jnp.arange(rows, dtype=jnp.int32))
    own_x = norm_x(col_start + jnp.arange(cols, dtype=jnp.int32))
    flow = jnp.stack(
        [
            (along_y / total).reshape(rows, cols) - own_y[:, None],
            (along_x / total).reshape(rows, cols) - own_x[None, :],
        ]
    )
    pair = jnp.stack([feat1, warped])
    xval = feat1.astype(jnp.float32)
    yval = warped.astype(jnp.float32)
    margin = 1
    padded = with_halo(pair, ((BLK, 1), (COL, 2)), 1)
    xpad = padded[0].astype(jnp.float32)
    ypad = padded[1].astype(jnp.float32)
    first, grad_var, grad_cov = local_terms(xpad, ypad)
    maps = jnp.stack([first, grad_var, grad_cov])
    beside_all = with_halo(maps.astype(jnp.bfloat16), ((BLK, 1), (COL, 2)), 1).astype(
        maps.dtype
    )
    spread_first = box_valid(beside_all[0])
    spread_var = box_valid(beside_all[1])
    spread_cov = box_valid(beside_all[2])
    grad_warped = spread_first + 2.0 * yval * spread_var + xval * spread_cov
    flow_pad = with_halo(flow, ((BLK, 1), (COL, 2)), 1)
    x_rows = xpad[margin - 1 : margin + rows + 1, margin : margin + cols]
    x_cols = xpad[margin : margin + rows, margin - 1 : margin + cols + 1]
    edge_y = row_start - 1 + jnp.arange(rows + 1, dtype=jnp.int32)
    valid_y = (edge_y >= 0) & (edge_y <= full_rows - 2)
    edge_x = col_start - 1 + jnp.arange(cols + 1, dtype=jnp.int32)
    valid_x = (edge_x >= 0) & (edge_x <= full_cols - 2)
    delta_y = flow_pad[:, 1:, 1:-1] - flow_pad[:, :-1, 1:-1]
    push_y = jnp.where(
        valid_y[None, :, None],
        charbonnier(edge_weight(x_rows[:-1], x_rows[1:])[None], delta_y),
        0.0,
    )
    delta_x = flow_pad[:, 1:-1, 1:] - flow_pad[:, 1:-1, :-1]
    push_x = jnp.where(
        valid_x[None, None, :],
        charbonnier(edge_weight(x_cols[:, :-1], x_cols[:, 1:])[None], delta_x),
        0.0,
    )
    grad_flow = push_y[:, :rows] - push_y[:, 1:] + push_x[:, :, :cols] - push_x[:, :, 1:]
    return (flow, grad_flow, grad_warped)


def solution(mesh):
    blk, col = mesh.devices.shape
    fine = mesh.devices.reshape(blk // 4, 2, 2, 2, col // 2)
    fine_mesh = Mesh(fine, FINE)
    placed = (P(BLK, COL, None), P(BLK, COL, None))
    return jax.shard_map(
        body,
        mesh=fine_mesh,
        in_specs=placed,
        out_specs=(P(None, BLK, COL), P(None, BLK, COL), P(BLK, COL, None)),
        check_vma=False,
    )
```

```python
import math

import jax
import jax.numpy as jnp
from jax import lax
from jax.experimental import pallas as pl
from jax.experimental.pallas import tpu as pltpu
from jax.sharding import Mesh
from jax.sharding import PartitionSpec as P

ssim_one = 0.01
ssim_two = 0.03
charb_sq = 0.0001

FINE = ("z", "xl", "c", "xh", "y")
BLK = ("z", "xl", "c")
COL = ("xh", "y")
KEY_AXES = ("z", ("xh", "xl"))
QUERY_AXES = ("y", "c")
BLOCK_Q = 512
BLOCK_K = 1024


def with_halo(value, sides, width):
    for axis, dim in sides:
        count, length = (lax.axis_size(axis), value.shape[dim])
        up = [(i, (i + 1) % count) for i in range(count - 1)]
        down = [(j, i) for i, j in up]
        last = lax.slice_in_dim(value, length - width, length, axis=dim)
        first = lax.slice_in_dim(value, 0, width, axis=dim)
        before = lax.ppermute(last, axis, up)
        after = lax.ppermute(first, axis, down)
        value = jnp.concatenate([before, value, after], axis=dim)
    return value


def box_valid(padded):
    rows_out = padded.shape[0] - 2
    cols_out = padded.shape[1] - 2
    total = jnp.zeros((rows_out, cols_out) + padded.shape[2:], padded.dtype)
    for offset_r in range(3):
        for offset_c in range(3):
            total = total + padded[offset_r : offset_r + rows_out, offset_c : offset_c + cols_out]
    return total / 9.0


def ssim_loss(mean_y, var_y, cov_xy, mean_x, var_x):
    top = (2.0 * mean_x * mean_y + ssim_one) * (2.0 * cov_xy + ssim_two)
    bottom = (mean_x * mean_x + mean_y * mean_y + ssim_one) * (var_x + var_y + ssim_two)
    return jnp.sum((1.0 - top / bottom) * 0.5)


def local_terms(xpad, ypad):
    mean_x = box_valid(xpad)
    mean_y = box_valid(ypad)
    var_x = box_valid(xpad * xpad) - mean_x * mean_x
    var_y = box_valid(ypad * ypad) - mean_y * mean_y
    cov_xy = box_valid(xpad * ypad) - mean_x * mean_y
    loss, pull = jax.vjp(
        lambda one, two, three: ssim_loss(one, two, three, mean_x, var_x), mean_y, var_y, cov_xy
    )
    grad_mean, grad_var, grad_cov = pull(jnp.ones_like(loss))
    first = grad_mean - 2.0 * grad_var * mean_y - grad_cov * mean_x
    return (first, grad_var, grad_cov)


def edge_weight(lower, upper):
    return jnp.exp(-jnp.mean(jnp.abs(upper - lower), axis=-1))


def charbonnier(weight, delta):
    return weight * delta / jnp.sqrt(delta * delta + charb_sq)


def flash_partials(queries, keys, key_y, key_x, scale, block_q, block_k):
    nq, width = queries.shape
    nk = keys.shape[0]
    grid = (nq // block_q, nk // block_k)
    last = grid[1] - 1

    def kernel(q_ref, k_ref, y_ref, x_ref, top_ref, total_ref, acc_ref, ay_ref, ax_ref,
               m_sc, l_sc, acc_sc, ay_sc, ax_sc):
        step = pl.program_id(1)

        @pl.when(step == 0)
        def _():
            m_sc[...] = jnp.full(m_sc.shape, -1e30, jnp.float32)
            l_sc[...] = jnp.zeros(l_sc.shape, jnp.float32)
            acc_sc[...] = jnp.zeros(acc_sc.shape, jnp.float32)
            ay_sc[...] = jnp.zeros(ay_sc.shape, jnp.float32)
            ax_sc[...] = jnp.zeros(ax_sc.shape, jnp.float32)

        k = k_ref[...]
        score = lax.dot_general(q_ref[...], k, (((1,), (1,)), ((), ())),
                                preferred_element_type=jnp.float32) * scale
        m_prev = m_sc[...]
        m_new = jnp.maximum(m_prev, jnp.max(score, axis=1, keepdims=True))
        shrink = jnp.exp(m_prev - m_new)
        expo = jnp.exp(score - m_new)
        l_sc[...] = l_sc[...] * shrink + jnp.sum(expo, axis=1, keepdims=True)
        ay_sc[...] = ay_sc[...] * shrink + jnp.sum(expo * y_ref[...], axis=1, keepdims=True)
        ax_sc[...] = ax_sc[...] * shrink + jnp.sum(expo * x_ref[...], axis=1, keepdims=True)
        acc_sc[...] = acc_sc[...] * shrink + jnp.dot(expo.astype(jnp.bfloat16), k,
                                                     preferred_element_type=jnp.float32)
        m_sc[...] = m_new

        @pl.when(step == last)
        def _():
            top_ref[...] = m_sc[...]
            total_ref[...] = l_sc[...]
            acc_ref[...] = acc_sc[...]
            ay_ref[...] = ay_sc[...]
            ax_ref[...] = ax_sc[...]

    col = pl.BlockSpec((block_q, 1), lambda i, j: (i, 0))
    outs = pl.pallas_call(
        kernel,
        grid=grid,
        in_specs=[
            pl.BlockSpec((block_q, width), lambda i, j: (i, 0)),
            pl.BlockSpec((block_k, width), lambda i, j: (j, 0)),
            pl.BlockSpec((1, block_k), lambda i, j: (0, j)),
            pl.BlockSpec((1, block_k), lambda i, j: (0, j)),
        ],
        out_specs=[col, col, pl.BlockSpec((block_q, width), lambda i, j: (i, 0)), col, col],
        out_shape=[
            jax.ShapeDtypeStruct((nq, 1), jnp.float32),
            jax.ShapeDtypeStruct((nq, 1), jnp.float32),
            jax.ShapeDtypeStruct((nq, width), jnp.float32),
            jax.ShapeDtypeStruct((nq, 1), jnp.float32),
            jax.ShapeDtypeStruct((nq, 1), jnp.float32),
        ],
        scratch_shapes=[
            pltpu.VMEM((block_q, 1), jnp.float32),
            pltpu.VMEM((block_q, 1), jnp.float32),
            pltpu.VMEM((block_q, width), jnp.float32),
            pltpu.VMEM((block_q, 1), jnp.float32),
            pltpu.VMEM((block_q, 1), jnp.float32),
        ],
        compiler_params=pltpu.CompilerParams(dimension_semantics=("arbitrary", "arbitrary")),
    )(queries, keys, key_y.reshape(1, nk), key_x.reshape(1, nk))
    top, total, acc, ay, ax = outs
    return top[:, 0], total[:, 0], acc, ay[:, 0], ax[:, 0]


def body(feat1, feat2):
    rows, cols, width = feat1.shape
    ncol = lax.axis_size(COL)
    full_rows = rows * lax.axis_size(BLK)
    full_cols = cols * ncol
    row_start = lax.axis_index(BLK) * rows
    col_start = lax.axis_index(COL) * cols
    scale = 1.0 / math.sqrt(width)
    tokens = rows * cols
    queries = lax.all_gather(feat1.reshape(tokens, width), QUERY_AXES, axis=0, tiled=True)

    def norm_y(index):
        return (index.astype(jnp.float32) + 0.5) * (2.0 / full_rows) - 1.0

    def norm_x(index):
        return (index.astype(jnp.float32) + 0.5) * (2.0 / full_cols) - 1.0

    piece = feat2
    for axis in KEY_AXES:
        piece = lax.all_gather(piece, axis, axis=0, tiled=True)
    count = piece.shape[0]
    gathered = jnp.arange(count, dtype=jnp.int32)
    rest = gathered // rows
    place = {}
    for axis in KEY_AXES:
        size = lax.axis_size(axis)
        place[axis] = rest % size
        rest = rest // size
    sz, sxl, sc, sxh, sy = (lax.axis_size(a) for a in FINE)
    x_full = place[("xh", "xl")]
    blk_of = (place["z"] * sxl + x_full % sxl) * sc + lax.axis_index("c")
    col_of = (x_full // sxl) * sy + lax.axis_index("y")
    tile_y = blk_of * rows + gathered % rows
    tile_x = col_of * cols
    grid_y = jnp.broadcast_to(tile_y[:, None], (count, cols))
    grid_x = tile_x[:, None] + jnp.arange(cols, dtype=jnp.int32)[None, :]
    carry = flash_partials(
        queries,
        piece.reshape(count * cols, width),
        norm_y(grid_y).reshape(-1),
        norm_x(grid_x).reshape(-1),
        scale,
        BLOCK_Q,
        BLOCK_K,
    )
    top, total, acc, along_y, along_x = carry
    parts = lax.axis_size(QUERY_AXES)
    stats = jnp.stack([top, total, along_y, along_x]).reshape(4, parts, tokens)
    stats = jnp.pad(stats.transpose(1, 0, 2), ((0, 0), (0, 0), (0, width - tokens)))
    packed = jnp.concatenate([acc.reshape(parts, tokens, width), stats], axis=1)
    packed = lax.all_to_all(packed, QUERY_AXES, 0, 0, tiled=True)
    tops = packed[:, tokens, :tokens]
    peak = jnp.max(tops, axis=0)
    factor = jnp.exp(tops - peak[None])
    acc = jnp.sum(packed[:, :tokens, :] * factor[:, :, None], axis=0)
    total = jnp.sum(packed[:, tokens + 1, :tokens] * factor, axis=0)
    along_y = jnp.sum(packed[:, tokens + 2, :tokens] * factor, axis=0)
    along_x = jnp.sum(packed[:, tokens + 3, :tokens] * factor, axis=0)
    warped = (acc / total[:, None]).astype(jnp.bfloat16).reshape(rows, cols, width)
    own_y = norm_y(row_start + jnp.arange(rows, dtype=jnp.int32))
    own_x = norm_x(col_start + jnp.arange(cols, dtype=jnp.int32))
    flow = jnp.stack(
        [
            (along_y / total).reshape(rows, cols) - own_y[:, None],
            (along_x / total).reshape(rows, cols) - own_x[None, :],
        ]
    )
    xval = feat1.astype(jnp.float32)
    yval = warped.astype(jnp.float32)
    margin = 2
    xpad = with_halo(feat1, ((BLK, 0), (COL, 1)), margin).astype(jnp.float32)
    ypad = with_halo(warped, ((BLK, 0), (COL, 1)), margin).astype(jnp.float32)
    flow_pad = with_halo(flow, ((BLK, 1), (COL, 2)), 1)
    first, grad_var, grad_cov = local_terms(xpad, ypad)
    cell_y = row_start - 1 + jnp.arange(rows + 2, dtype=jnp.int32)
    cell_x = col_start - 1 + jnp.arange(cols + 2, dtype=jnp.int32)
    inside = ((cell_y >= 0) & (cell_y < full_rows))[:, None] & ((cell_x >= 0) & (cell_x < full_cols))[None, :]
    inside = inside[:, :, None]
    spread_first = box_valid(jnp.where(inside, first, 0.0))
    spread_var = box_valid(jnp.where(inside, grad_var, 0.0))
    spread_cov = box_valid(jnp.where(inside, grad_cov, 0.0))
    grad_warped = spread_first + 2.0 * yval * spread_var + xval * spread_cov
    x_rows = xpad[margin - 1 : margin + rows + 1, margin : margin + cols]
    x_cols = xpad[margin : margin + rows, margin - 1 : margin + cols + 1]
    edge_y = row_start - 1 + jnp.arange(rows + 1, dtype=jnp.int32)
    valid_y = (edge_y >= 0) & (edge_y <= full_rows - 2)
    edge_x = col_start - 1 + jnp.arange(cols + 1, dtype=jnp.int32)
    valid_x = (edge_x >= 0) & (edge_x <= full_cols - 2)
    delta_y = flow_pad[:, 1:, 1:-1] - flow_pad[:, :-1, 1:-1]
    push_y = jnp.where(
        valid_y[None, :, None],
        charbonnier(edge_weight(x_rows[:-1], x_rows[1:])[None], delta_y),
        0.0,
    )
    delta_x = flow_pad[:, 1:-1, 1:] - flow_pad[:, 1:-1, :-1]
    push_x = jnp.where(
        valid_x[None, None, :],
        charbonnier(edge_weight(x_cols[:, :-1], x_cols[:, 1:])[None], delta_x),
        0.0,
    )
    grad_flow = push_y[:, :rows] - push_y[:, 1:] + push_x[:, :, :cols] - push_x[:, :, 1:]
    return (flow, grad_flow, grad_warped)


def solution(mesh):
    blk, col = mesh.devices.shape
    fine = mesh.devices.reshape(blk // 4, 2, 2, 2, col // 2)
    fine_mesh = Mesh(fine, FINE)
    placed = (P(BLK, COL, None), P(BLK, COL, None))
    return jax.shard_map(
        body,
        mesh=fine_mesh,
        in_specs=placed,
        out_specs=(P(None, BLK, COL), P(None, BLK, COL), P(BLK, COL, None)),
        check_vma=False,
    )
```

```python
import math

import jax
import jax.numpy as jnp
from jax import lax
from jax.experimental import pallas as pl
from jax.experimental.pallas import tpu as pltpu
from jax.sharding import Mesh
from jax.sharding import PartitionSpec as P

ssim_one = 0.01
ssim_two = 0.03
charb_sq = 0.0001

FINE = ("z", "xl", "c", "xh", "y")
BLK = ("z", "xl", "c")
COL = ("xh", "y")
QUERY_AXES = ("y", "c")
BLOCK_Q = 512
BLOCK_K = 1024


def with_halo(value, sides, width):
    for axis, dim in sides:
        count, length = (lax.axis_size(axis), value.shape[dim])
        up = [(i, (i + 1) % count) for i in range(count - 1)]
        down = [(j, i) for i, j in up]
        last = lax.slice_in_dim(value, length - width, length, axis=dim)
        first = lax.slice_in_dim(value, 0, width, axis=dim)
        before = lax.ppermute(last, axis, up)
        after = lax.ppermute(first, axis, down)
        value = jnp.concatenate([before, value, after], axis=dim)
    return value


def box_valid(padded):
    rows_out = padded.shape[0] - 2
    cols_out = padded.shape[1] - 2
    total = jnp.zeros((rows_out, cols_out) + padded.shape[2:], padded.dtype)
    for offset_r in range(3):
        for offset_c in range(3):
            total = total + padded[offset_r : offset_r + rows_out, offset_c : offset_c + cols_out]
    return total / 9.0


def ssim_loss(mean_y, var_y, cov_xy, mean_x, var_x):
    top = (2.0 * mean_x * mean_y + ssim_one) * (2.0 * cov_xy + ssim_two)
    bottom = (mean_x * mean_x + mean_y * mean_y + ssim_one) * (var_x + var_y + ssim_two)
    return jnp.sum((1.0 - top / bottom) * 0.5)


def local_terms(xpad, ypad):
    mean_x = box_valid(xpad)
    mean_y = box_valid(ypad)
    var_x = box_valid(xpad * xpad) - mean_x * mean_x
    var_y = box_valid(ypad * ypad) - mean_y * mean_y
    cov_xy = box_valid(xpad * ypad) - mean_x * mean_y
    loss, pull = jax.vjp(
        lambda one, two, three: ssim_loss(one, two, three, mean_x, var_x), mean_y, var_y, cov_xy
    )
    grad_mean, grad_var, grad_cov = pull(jnp.ones_like(loss))
    first = grad_mean - 2.0 * grad_var * mean_y - grad_cov * mean_x
    return (first, grad_var, grad_cov)


def edge_weight(lower, upper):
    return jnp.exp(-jnp.mean(jnp.abs(upper - lower), axis=-1))


def charbonnier(weight, delta):
    return weight * delta / jnp.sqrt(delta * delta + charb_sq)


def flash_partials(queries, keys, key_y, key_x, scale, block_q, block_k):
    nq, width = queries.shape
    nk = keys.shape[0]
    grid = (nq // block_q, nk // block_k)
    last = grid[1] - 1

    def kernel(q_ref, k_ref, y_ref, x_ref, top_ref, total_ref, acc_ref, ay_ref, ax_ref,
               m_sc, l_sc, acc_sc, ay_sc, ax_sc):
        step = pl.program_id(1)

        @pl.when(step == 0)
        def _():
            m_sc[...] = jnp.full(m_sc.shape, -1e30, jnp.float32)
            l_sc[...] = jnp.zeros(l_sc.shape, jnp.float32)
            acc_sc[...] = jnp.zeros(acc_sc.shape, jnp.float32)
            ay_sc[...] = jnp.zeros(ay_sc.shape, jnp.float32)
            ax_sc[...] = jnp.zeros(ax_sc.shape, jnp.float32)

        k = k_ref[...]
        score = lax.dot_general(q_ref[...], k, (((1,), (1,)), ((), ())),
                                preferred_element_type=jnp.float32) * scale
        m_prev = m_sc[...]
        m_new = jnp.maximum(m_prev, jnp.max(score, axis=1, keepdims=True))
        shrink = jnp.exp(m_prev - m_new)
        expo = jnp.exp(score - m_new)
        l_sc[...] = l_sc[...] * shrink + jnp.sum(expo, axis=1, keepdims=True)
        ay_sc[...] = ay_sc[...] * shrink + jnp.sum(expo * y_ref[...], axis=1, keepdims=True)
        ax_sc[...] = ax_sc[...] * shrink + jnp.sum(expo * x_ref[...], axis=1, keepdims=True)
        acc_sc[...] = acc_sc[...] * shrink + jnp.dot(expo.astype(jnp.bfloat16), k,
                                                     preferred_element_type=jnp.float32)
        m_sc[...] = m_new

        @pl.when(step == last)
        def _():
            top_ref[...] = m_sc[...]
            total_ref[...] = l_sc[...]
            acc_ref[...] = acc_sc[...]
            ay_ref[...] = ay_sc[...]
            ax_ref[...] = ax_sc[...]

    col = pl.BlockSpec((block_q, 1), lambda i, j: (i, 0))
    outs = pl.pallas_call(
        kernel,
        grid=grid,
        in_specs=[
            pl.BlockSpec((block_q, width), lambda i, j: (i, 0)),
            pl.BlockSpec((block_k, width), lambda i, j: (j, 0)),
            pl.BlockSpec((1, block_k), lambda i, j: (0, j)),
            pl.BlockSpec((1, block_k), lambda i, j: (0, j)),
        ],
        out_specs=[col, col, pl.BlockSpec((block_q, width), lambda i, j: (i, 0)), col, col],
        out_shape=[
            jax.ShapeDtypeStruct((nq, 1), jnp.float32),
            jax.ShapeDtypeStruct((nq, 1), jnp.float32),
            jax.ShapeDtypeStruct((nq, width), jnp.float32),
            jax.ShapeDtypeStruct((nq, 1), jnp.float32),
            jax.ShapeDtypeStruct((nq, 1), jnp.float32),
        ],
        scratch_shapes=[
            pltpu.VMEM((block_q, 1), jnp.float32),
            pltpu.VMEM((block_q, 1), jnp.float32),
            pltpu.VMEM((block_q, width), jnp.float32),
            pltpu.VMEM((block_q, 1), jnp.float32),
            pltpu.VMEM((block_q, 1), jnp.float32),
        ],
        compiler_params=pltpu.CompilerParams(dimension_semantics=("arbitrary", "arbitrary")),
    )(queries, keys, key_y.reshape(1, nk), key_x.reshape(1, nk))
    top, total, acc, ay, ax = outs
    return top[:, 0], total[:, 0], acc, ay[:, 0], ax[:, 0]


def body(feat1, feat2):
    rows, cols, width = feat1.shape
    ncol = lax.axis_size(COL)
    full_rows = rows * lax.axis_size(BLK)
    full_cols = cols * ncol
    row_start = lax.axis_index(BLK) * rows
    col_start = lax.axis_index(COL) * cols
    scale = 1.0 / math.sqrt(width)
    tokens = rows * cols
    queries = lax.all_gather(feat1.reshape(tokens, width), QUERY_AXES, axis=0, tiled=True)

    def norm_y(index):
        return (index.astype(jnp.float32) + 0.5) * (2.0 / full_rows) - 1.0

    def norm_x(index):
        return (index.astype(jnp.float32) + 0.5) * (2.0 / full_cols) - 1.0

    sz, sxl, sc, sxh, sy = (lax.axis_size(a) for a in FINE)
    blocks = [feat2]
    for shift in range(1, sz):
        ring = [(i, (i + shift) % sz) for i in range(sz)]
        blocks.append(lax.ppermute(feat2, "z", ring))
    piece = lax.all_gather(jnp.concatenate(blocks, axis=0), ("xh", "xl"), axis=0, tiled=True)
    count = piece.shape[0]
    gathered = jnp.arange(count, dtype=jnp.int32)
    rest = gathered // rows
    z_from = (lax.axis_index("z") - rest % sz) % sz
    x_full = rest // sz
    blk_of = (z_from * sxl + x_full % sxl) * sc + lax.axis_index("c")
    col_of = (x_full // sxl) * sy + lax.axis_index("y")
    tile_y = blk_of * rows + gathered % rows
    tile_x = col_of * cols
    grid_y = jnp.broadcast_to(tile_y[:, None], (count, cols))
    grid_x = tile_x[:, None] + jnp.arange(cols, dtype=jnp.int32)[None, :]
    carry = flash_partials(
        queries,
        piece.reshape(count * cols, width),
        norm_y(grid_y).reshape(-1),
        norm_x(grid_x).reshape(-1),
        scale,
        BLOCK_Q,
        BLOCK_K,
    )
    top, total, acc, along_y, along_x = carry
    parts = lax.axis_size(QUERY_AXES)
    stats = jnp.stack([top, total, along_y, along_x]).reshape(4, parts, tokens)
    stats = jnp.pad(stats.transpose(1, 0, 2), ((0, 0), (0, 0), (0, width - tokens)))
    packed = jnp.concatenate([acc.reshape(parts, tokens, width), stats], axis=1)
    packed = lax.all_to_all(packed, QUERY_AXES, 0, 0, tiled=True)
    tops = packed[:, tokens, :tokens]
    peak = jnp.max(tops, axis=0)
    factor = jnp.exp(tops - peak[None])
    acc = jnp.sum(packed[:, :tokens, :] * factor[:, :, None], axis=0)
    total = jnp.sum(packed[:, tokens + 1, :tokens] * factor, axis=0)
    along_y = jnp.sum(packed[:, tokens + 2, :tokens] * factor, axis=0)
    along_x = jnp.sum(packed[:, tokens + 3, :tokens] * factor, axis=0)
    warped = (acc / total[:, None]).astype(jnp.bfloat16).reshape(rows, cols, width)
    own_y = norm_y(row_start + jnp.arange(rows, dtype=jnp.int32))
    own_x = norm_x(col_start + jnp.arange(cols, dtype=jnp.int32))
    flow = jnp.stack(
        [
            (along_y / total).reshape(rows, cols) - own_y[:, None],
            (along_x / total).reshape(rows, cols) - own_x[None, :],
        ]
    )
    xval = feat1.astype(jnp.float32)
    yval = warped.astype(jnp.float32)
    margin = 2
    xpad = with_halo(feat1, ((BLK, 0), (COL, 1)), margin).astype(jnp.float32)
    ypad = with_halo(warped, ((BLK, 0), (COL, 1)), margin).astype(jnp.float32)
    flow_pad = with_halo(flow, ((BLK, 1), (COL, 2)), 1)
    first, grad_var, grad_cov = local_terms(xpad, ypad)
    cell_y = row_start - 1 + jnp.arange(rows + 2, dtype=jnp.int32)
    cell_x = col_start - 1 + jnp.arange(cols + 2, dtype=jnp.int32)
    inside = ((cell_y >= 0) & (cell_y < full_rows))[:, None] & ((cell_x >= 0) & (cell_x < full_cols))[None, :]
    inside = inside[:, :, None]
    spread_first = box_valid(jnp.where(inside, first, 0.0))
    spread_var = box_valid(jnp.where(inside, grad_var, 0.0))
    spread_cov = box_valid(jnp.where(inside, grad_cov, 0.0))
    grad_warped = spread_first + 2.0 * yval * spread_var + xval * spread_cov
    x_rows = xpad[margin - 1 : margin + rows + 1, margin : margin + cols]
    x_cols = xpad[margin : margin + rows, margin - 1 : margin + cols + 1]
    edge_y = row_start - 1 + jnp.arange(rows + 1, dtype=jnp.int32)
    valid_y = (edge_y >= 0) & (edge_y <= full_rows - 2)
    edge_x = col_start - 1 + jnp.arange(cols + 1, dtype=jnp.int32)
    valid_x = (edge_x >= 0) & (edge_x <= full_cols - 2)
    delta_y = flow_pad[:, 1:, 1:-1] - flow_pad[:, :-1, 1:-1]
    push_y = jnp.where(
        valid_y[None, :, None],
        charbonnier(edge_weight(x_rows[:-1], x_rows[1:])[None], delta_y),
        0.0,
    )
    delta_x = flow_pad[:, 1:-1, 1:] - flow_pad[:, 1:-1, :-1]
    push_x = jnp.where(
        valid_x[None, None, :],
        charbonnier(edge_weight(x_cols[:, :-1], x_cols[:, 1:])[None], delta_x),
        0.0,
    )
    grad_flow = push_y[:, :rows] - push_y[:, 1:] + push_x[:, :, :cols] - push_x[:, :, 1:]
    return (flow, grad_flow, grad_warped)


def solution(mesh):
    blk, col = mesh.devices.shape
    fine = mesh.devices.reshape(blk // 4, 2, 2, 2, col // 2)
    fine_mesh = Mesh(fine, FINE)
    placed = (P(BLK, COL, None), P(BLK, COL, None))
    return jax.shard_map(
        body,
        mesh=fine_mesh,
        in_specs=placed,
        out_specs=(P(None, BLK, COL), P(None, BLK, COL), P(BLK, COL, None)),
        check_vma=False,
    )
```

```python
import math

import jax
import jax.numpy as jnp
from jax import lax
from jax.experimental import pallas as pl
from jax.experimental.pallas import tpu as pltpu
from jax.sharding import Mesh
from jax.sharding import PartitionSpec as P

ssim_one = 0.01
ssim_two = 0.03
charb_sq = 0.0001

FINE = ("z", "xl", "c", "xh", "y")
BLK = ("z", "xl", "c")
COL = ("xh", "y")
QUERY_AXES = ("c", "y")
BLOCK_Q = 512
BLOCK_K = 1024


def with_halo(value, sides, width):
    for axis, dim in sides:
        count, length = (lax.axis_size(axis), value.shape[dim])
        up = [(i, (i + 1) % count) for i in range(count - 1)]
        down = [(j, i) for i, j in up]
        last = lax.slice_in_dim(value, length - width, length, axis=dim)
        first = lax.slice_in_dim(value, 0, width, axis=dim)
        before = lax.ppermute(last, axis, up)
        after = lax.ppermute(first, axis, down)
        value = jnp.concatenate([before, value, after], axis=dim)
    return value


def box_valid(padded):
    rows_out = padded.shape[0] - 2
    cols_out = padded.shape[1] - 2
    total = jnp.zeros((rows_out, cols_out) + padded.shape[2:], padded.dtype)
    for offset_r in range(3):
        for offset_c in range(3):
            total = total + padded[offset_r : offset_r + rows_out, offset_c : offset_c + cols_out]
    return total / 9.0


def ssim_loss(mean_y, var_y, cov_xy, mean_x, var_x):
    top = (2.0 * mean_x * mean_y + ssim_one) * (2.0 * cov_xy + ssim_two)
    bottom = (mean_x * mean_x + mean_y * mean_y + ssim_one) * (var_x + var_y + ssim_two)
    return jnp.sum((1.0 - top / bottom) * 0.5)


def local_terms(xpad, ypad):
    mean_x = box_valid(xpad)
    mean_y = box_valid(ypad)
    var_x = box_valid(xpad * xpad) - mean_x * mean_x
    var_y = box_valid(ypad * ypad) - mean_y * mean_y
    cov_xy = box_valid(xpad * ypad) - mean_x * mean_y
    loss, pull = jax.vjp(
        lambda one, two, three: ssim_loss(one, two, three, mean_x, var_x), mean_y, var_y, cov_xy
    )
    grad_mean, grad_var, grad_cov = pull(jnp.ones_like(loss))
    first = grad_mean - 2.0 * grad_var * mean_y - grad_cov * mean_x
    return (first, grad_var, grad_cov)


def edge_weight(lower, upper):
    return jnp.exp(-jnp.mean(jnp.abs(upper - lower), axis=-1))


def charbonnier(weight, delta):
    return weight * delta / jnp.sqrt(delta * delta + charb_sq)


def flash_partials(queries, keys, key_y, key_x, scale, block_q, block_k):
    nq, width = queries.shape
    nk = keys.shape[0]
    grid = (nq // block_q, nk // block_k)
    last = grid[1] - 1

    def kernel(q_ref, k_ref, y_ref, x_ref, top_ref, total_ref, acc_ref, ay_ref, ax_ref,
               m_sc, l_sc, acc_sc, ay_sc, ax_sc):
        step = pl.program_id(1)

        @pl.when(step == 0)
        def _():
            m_sc[...] = jnp.full(m_sc.shape, -1e30, jnp.float32)
            l_sc[...] = jnp.zeros(l_sc.shape, jnp.float32)
            acc_sc[...] = jnp.zeros(acc_sc.shape, jnp.float32)
            ay_sc[...] = jnp.zeros(ay_sc.shape, jnp.float32)
            ax_sc[...] = jnp.zeros(ax_sc.shape, jnp.float32)

        k = k_ref[...]
        score = lax.dot_general(q_ref[...], k, (((1,), (1,)), ((), ())),
                                preferred_element_type=jnp.float32) * scale
        m_prev = m_sc[...]
        m_new = jnp.maximum(m_prev, jnp.max(score, axis=1, keepdims=True))
        shrink = jnp.exp(m_prev - m_new)
        expo = jnp.exp(score - m_new)
        l_sc[...] = l_sc[...] * shrink + jnp.sum(expo, axis=1, keepdims=True)
        ay_sc[...] = ay_sc[...] * shrink + jnp.sum(expo * y_ref[...], axis=1, keepdims=True)
        ax_sc[...] = ax_sc[...] * shrink + jnp.sum(expo * x_ref[...], axis=1, keepdims=True)
        acc_sc[...] = acc_sc[...] * shrink + jnp.dot(expo.astype(jnp.bfloat16), k,
                                                     preferred_element_type=jnp.float32)
        m_sc[...] = m_new

        @pl.when(step == last)
        def _():
            top_ref[...] = m_sc[...]
            total_ref[...] = l_sc[...]
            acc_ref[...] = acc_sc[...]
            ay_ref[...] = ay_sc[...]
            ax_ref[...] = ax_sc[...]

    col = pl.BlockSpec((block_q, 1), lambda i, j: (i, 0))
    outs = pl.pallas_call(
        kernel,
        grid=grid,
        in_specs=[
            pl.BlockSpec((block_q, width), lambda i, j: (i, 0)),
            pl.BlockSpec((block_k, width), lambda i, j: (j, 0)),
            pl.BlockSpec((1, block_k), lambda i, j: (0, j)),
            pl.BlockSpec((1, block_k), lambda i, j: (0, j)),
        ],
        out_specs=[col, col, pl.BlockSpec((block_q, width), lambda i, j: (i, 0)), col, col],
        out_shape=[
            jax.ShapeDtypeStruct((nq, 1), jnp.float32),
            jax.ShapeDtypeStruct((nq, 1), jnp.float32),
            jax.ShapeDtypeStruct((nq, width), jnp.float32),
            jax.ShapeDtypeStruct((nq, 1), jnp.float32),
            jax.ShapeDtypeStruct((nq, 1), jnp.float32),
        ],
        scratch_shapes=[
            pltpu.VMEM((block_q, 1), jnp.float32),
            pltpu.VMEM((block_q, 1), jnp.float32),
            pltpu.VMEM((block_q, width), jnp.float32),
            pltpu.VMEM((block_q, 1), jnp.float32),
            pltpu.VMEM((block_q, 1), jnp.float32),
        ],
        compiler_params=pltpu.CompilerParams(dimension_semantics=("arbitrary", "arbitrary")),
    )(queries, keys, key_y.reshape(1, nk), key_x.reshape(1, nk))
    top, total, acc, ay, ax = outs
    return top[:, 0], total[:, 0], acc, ay[:, 0], ax[:, 0]


def body(feat1, feat2):
    rows, cols, width = feat1.shape
    ncol = lax.axis_size(COL)
    full_rows = rows * lax.axis_size(BLK)
    full_cols = cols * ncol
    row_start = lax.axis_index(BLK) * rows
    col_start = lax.axis_index(COL) * cols
    scale = 1.0 / math.sqrt(width)
    tokens = rows * cols
    parts = lax.axis_size(QUERY_AXES)
    mine = feat1.reshape(tokens, width)
    arrived = [mine]
    for shift in range(1, parts):
        ring = [(i, (i + shift) % parts) for i in range(parts)]
        arrived.append(lax.ppermute(mine, QUERY_AXES, ring))
    order = (lax.axis_index(QUERY_AXES) - jnp.arange(parts, dtype=jnp.int32)) % parts
    queries = jnp.take(jnp.stack(arrived), order, axis=0).reshape(parts * tokens, width)

    def norm_y(index):
        return (index.astype(jnp.float32) + 0.5) * (2.0 / full_rows) - 1.0

    def norm_x(index):
        return (index.astype(jnp.float32) + 0.5) * (2.0 / full_cols) - 1.0

    sz, sxl, sc, sxh, sy = (lax.axis_size(a) for a in FINE)
    blocks = [feat2]
    for shift in range(1, sz):
        ring = [(i, (i + shift) % sz) for i in range(sz)]
        blocks.append(lax.ppermute(feat2, "z", ring))
    piece = lax.all_gather(jnp.concatenate(blocks, axis=0), ("xh", "xl"), axis=0, tiled=True)
    count = piece.shape[0]
    gathered = jnp.arange(count, dtype=jnp.int32)
    rest = gathered // rows
    z_from = (lax.axis_index("z") - rest % sz) % sz
    x_full = rest // sz
    blk_of = (z_from * sxl + x_full % sxl) * sc + lax.axis_index("c")
    col_of = (x_full // sxl) * sy + lax.axis_index("y")
    tile_y = blk_of * rows + gathered % rows
    tile_x = col_of * cols
    grid_y = jnp.broadcast_to(tile_y[:, None], (count, cols))
    grid_x = tile_x[:, None] + jnp.arange(cols, dtype=jnp.int32)[None, :]
    carry = flash_partials(
        queries,
        piece.reshape(count * cols, width),
        norm_y(grid_y).reshape(-1),
        norm_x(grid_x).reshape(-1),
        scale,
        BLOCK_Q,
        BLOCK_K,
    )
    top, total, acc, along_y, along_x = carry
    stats = jnp.stack([top, total, along_y, along_x]).reshape(4, parts, tokens)
    stats = jnp.pad(stats.transpose(1, 0, 2), ((0, 0), (0, 0), (0, width - tokens)))
    packed = jnp.concatenate([acc.reshape(parts, tokens, width), stats], axis=1)
    packed = lax.all_to_all(packed, QUERY_AXES, 0, 0, tiled=True)
    tops = packed[:, tokens, :tokens]
    peak = jnp.max(tops, axis=0)
    factor = jnp.exp(tops - peak[None])
    acc = jnp.sum(packed[:, :tokens, :] * factor[:, :, None], axis=0)
    total = jnp.sum(packed[:, tokens + 1, :tokens] * factor, axis=0)
    along_y = jnp.sum(packed[:, tokens + 2, :tokens] * factor, axis=0)
    along_x = jnp.sum(packed[:, tokens + 3, :tokens] * factor, axis=0)
    warped = (acc / total[:, None]).astype(jnp.bfloat16).reshape(rows, cols, width)
    own_y = norm_y(row_start + jnp.arange(rows, dtype=jnp.int32))
    own_x = norm_x(col_start + jnp.arange(cols, dtype=jnp.int32))
    flow = jnp.stack(
        [
            (along_y / total).reshape(rows, cols) - own_y[:, None],
            (along_x / total).reshape(rows, cols) - own_x[None, :],
        ]
    )
    xval = feat1.astype(jnp.float32)
    yval = warped.astype(jnp.float32)
    margin = 2
    xpad = with_halo(feat1, ((BLK, 0), (COL, 1)), margin).astype(jnp.float32)
    ypad = with_halo(warped, ((BLK, 0), (COL, 1)), margin).astype(jnp.float32)
    flow_pad = with_halo(flow, ((BLK, 1), (COL, 2)), 1)
    first, grad_var, grad_cov = local_terms(xpad, ypad)
    cell_y = row_start - 1 + jnp.arange(rows + 2, dtype=jnp.int32)
    cell_x = col_start - 1 + jnp.arange(cols + 2, dtype=jnp.int32)
    inside = ((cell_y >= 0) & (cell_y < full_rows))[:, None] & ((cell_x >= 0) & (cell_x < full_cols))[None, :]
    inside = inside[:, :, None]
    spread_first = box_valid(jnp.where(inside, first, 0.0))
    spread_var = box_valid(jnp.where(inside, grad_var, 0.0))
    spread_cov = box_valid(jnp.where(inside, grad_cov, 0.0))
    grad_warped = spread_first + 2.0 * yval * spread_var + xval * spread_cov
    x_rows = xpad[margin - 1 : margin + rows + 1, margin : margin + cols]
    x_cols = xpad[margin : margin + rows, margin - 1 : margin + cols + 1]
    edge_y = row_start - 1 + jnp.arange(rows + 1, dtype=jnp.int32)
    valid_y = (edge_y >= 0) & (edge_y <= full_rows - 2)
    edge_x = col_start - 1 + jnp.arange(cols + 1, dtype=jnp.int32)
    valid_x = (edge_x >= 0) & (edge_x <= full_cols - 2)
    delta_y = flow_pad[:, 1:, 1:-1] - flow_pad[:, :-1, 1:-1]
    push_y = jnp.where(
        valid_y[None, :, None],
        charbonnier(edge_weight(x_rows[:-1], x_rows[1:])[None], delta_y),
        0.0,
    )
    delta_x = flow_pad[:, 1:-1, 1:] - flow_pad[:, 1:-1, :-1]
    push_x = jnp.where(
        valid_x[None, None, :],
        charbonnier(edge_weight(x_cols[:, :-1], x_cols[:, 1:])[None], delta_x),
        0.0,
    )
    grad_flow = push_y[:, :rows] - push_y[:, 1:] + push_x[:, :, :cols] - push_x[:, :, 1:]
    return (flow, grad_flow, grad_warped)


def solution(mesh):
    blk, col = mesh.devices.shape
    fine = mesh.devices.reshape(blk // 4, 2, 2, 2, col // 2)
    fine_mesh = Mesh(fine, FINE)
    placed = (P(BLK, COL, None), P(BLK, COL, None))
    return jax.shard_map(
        body,
        mesh=fine_mesh,
        in_specs=placed,
        out_specs=(P(None, BLK, COL), P(None, BLK, COL), P(BLK, COL, None)),
        check_vma=False,
    )
```

```python
import math

import jax
import jax.numpy as jnp
from jax import lax
from jax.experimental import pallas as pl
from jax.experimental.pallas import tpu as pltpu
from jax.sharding import Mesh
from jax.sharding import PartitionSpec as P

ssim_one = 0.01
ssim_two = 0.03
charb_sq = 0.0001

FINE = ("z", "xl", "c", "xh", "y")
BLK = ("z", "xl", "c")
COL = ("xh", "y")
QUERY_AXES = ("c", "y")
BLOCK_Q = 512
BLOCK_K = 768


def with_halo(value, sides, width):
    for axis, dim in sides:
        count, length = (lax.axis_size(axis), value.shape[dim])
        up = [(i, (i + 1) % count) for i in range(count - 1)]
        down = [(j, i) for i, j in up]
        last = lax.slice_in_dim(value, length - width, length, axis=dim)
        first = lax.slice_in_dim(value, 0, width, axis=dim)
        before = lax.ppermute(last, axis, up)
        after = lax.ppermute(first, axis, down)
        value = jnp.concatenate([before, value, after], axis=dim)
    return value


def box_valid(padded):
    rows_out = padded.shape[0] - 2
    cols_out = padded.shape[1] - 2
    total = jnp.zeros((rows_out, cols_out) + padded.shape[2:], padded.dtype)
    for offset_r in range(3):
        for offset_c in range(3):
            total = total + padded[offset_r : offset_r + rows_out, offset_c : offset_c + cols_out]
    return total / 9.0


def ssim_loss(mean_y, var_y, cov_xy, mean_x, var_x):
    top = (2.0 * mean_x * mean_y + ssim_one) * (2.0 * cov_xy + ssim_two)
    bottom = (mean_x * mean_x + mean_y * mean_y + ssim_one) * (var_x + var_y + ssim_two)
    return jnp.sum((1.0 - top / bottom) * 0.5)


def local_terms(xpad, ypad):
    mean_x = box_valid(xpad)
    mean_y = box_valid(ypad)
    var_x = box_valid(xpad * xpad) - mean_x * mean_x
    var_y = box_valid(ypad * ypad) - mean_y * mean_y
    cov_xy = box_valid(xpad * ypad) - mean_x * mean_y
    loss, pull = jax.vjp(
        lambda one, two, three: ssim_loss(one, two, three, mean_x, var_x), mean_y, var_y, cov_xy
    )
    grad_mean, grad_var, grad_cov = pull(jnp.ones_like(loss))
    first = grad_mean - 2.0 * grad_var * mean_y - grad_cov * mean_x
    return (first, grad_var, grad_cov)


def edge_weight(lower, upper):
    return jnp.exp(-jnp.mean(jnp.abs(upper - lower), axis=-1))


def charbonnier(weight, delta):
    return weight * delta / jnp.sqrt(delta * delta + charb_sq)


def flash_partials(queries, keys, key_y, key_x, carry, scale, block_q, block_k):
    nq, width = queries.shape
    nk = keys.shape[0]
    grid = (nq // block_q, nk // block_k)
    last = grid[1] - 1

    def kernel(q_ref, k_ref, y_ref, x_ref, top_in, total_in, acc_in, ay_in, ax_in,
               top_ref, total_ref, acc_ref, ay_ref, ax_ref, m_sc, l_sc, acc_sc, ay_sc, ax_sc):
        step = pl.program_id(1)

        @pl.when(step == 0)
        def _():
            m_sc[...] = top_in[...]
            l_sc[...] = total_in[...]
            acc_sc[...] = acc_in[...]
            ay_sc[...] = ay_in[...]
            ax_sc[...] = ax_in[...]

        k = k_ref[...]
        score = lax.dot_general(q_ref[...], k, (((1,), (1,)), ((), ())),
                                preferred_element_type=jnp.float32) * scale
        m_prev = m_sc[...]
        m_new = jnp.maximum(m_prev, jnp.max(score, axis=1, keepdims=True))
        shrink = jnp.exp(m_prev - m_new)
        expo = jnp.exp(score - m_new)
        l_sc[...] = l_sc[...] * shrink + jnp.sum(expo, axis=1, keepdims=True)
        ay_sc[...] = ay_sc[...] * shrink + jnp.sum(expo * y_ref[...], axis=1, keepdims=True)
        ax_sc[...] = ax_sc[...] * shrink + jnp.sum(expo * x_ref[...], axis=1, keepdims=True)
        acc_sc[...] = acc_sc[...] * shrink + jnp.dot(expo.astype(jnp.bfloat16), k,
                                                     preferred_element_type=jnp.float32)
        m_sc[...] = m_new

        @pl.when(step == last)
        def _():
            top_ref[...] = m_sc[...]
            total_ref[...] = l_sc[...]
            acc_ref[...] = acc_sc[...]
            ay_ref[...] = ay_sc[...]
            ax_ref[...] = ax_sc[...]

    col = pl.BlockSpec((block_q, 1), lambda i, j: (i, 0))
    top, total, acc, ay, ax = carry
    outs = pl.pallas_call(
        kernel,
        grid=grid,
        in_specs=[
            pl.BlockSpec((block_q, width), lambda i, j: (i, 0)),
            pl.BlockSpec((block_k, width), lambda i, j: (j, 0)),
            pl.BlockSpec((1, block_k), lambda i, j: (0, j)),
            pl.BlockSpec((1, block_k), lambda i, j: (0, j)),
            col,
            col,
            pl.BlockSpec((block_q, width), lambda i, j: (i, 0)),
            col,
            col,
        ],
        out_specs=[col, col, pl.BlockSpec((block_q, width), lambda i, j: (i, 0)), col, col],
        out_shape=[
            jax.ShapeDtypeStruct((nq, 1), jnp.float32),
            jax.ShapeDtypeStruct((nq, 1), jnp.float32),
            jax.ShapeDtypeStruct((nq, width), jnp.float32),
            jax.ShapeDtypeStruct((nq, 1), jnp.float32),
            jax.ShapeDtypeStruct((nq, 1), jnp.float32),
        ],
        scratch_shapes=[
            pltpu.VMEM((block_q, 1), jnp.float32),
            pltpu.VMEM((block_q, 1), jnp.float32),
            pltpu.VMEM((block_q, width), jnp.float32),
            pltpu.VMEM((block_q, 1), jnp.float32),
            pltpu.VMEM((block_q, 1), jnp.float32),
        ],
        compiler_params=pltpu.CompilerParams(dimension_semantics=("arbitrary", "arbitrary")),
        cost_estimate=pl.CostEstimate(
            flops=4 * nq * nk * width,
            transcendentals=nq * nk,
            bytes_accessed=2 * nq * width + 2 * nk * width * grid[0] + 8 * nq * width,
        ),
    )(queries, keys, key_y.reshape(1, nk), key_x.reshape(1, nk), top, total, acc, ay, ax)
    return tuple(outs)


def body(feat1, feat2):
    rows, cols, width = feat1.shape
    ncol = lax.axis_size(COL)
    full_rows = rows * lax.axis_size(BLK)
    full_cols = cols * ncol
    row_start = lax.axis_index(BLK) * rows
    col_start = lax.axis_index(COL) * cols
    scale = 1.0 / math.sqrt(width)
    tokens = rows * cols
    parts = lax.axis_size(QUERY_AXES)
    mine = feat1.reshape(tokens, width)
    arrived = [mine]
    for shift in range(1, parts):
        ring = [(i, (i + shift) % parts) for i in range(parts)]
        arrived.append(lax.ppermute(mine, QUERY_AXES, ring))
    order = (lax.axis_index(QUERY_AXES) - jnp.arange(parts, dtype=jnp.int32)) % parts
    queries = jnp.take(jnp.stack(arrived), order, axis=0).reshape(parts * tokens, width)

    def norm_y(index):
        return (index.astype(jnp.float32) + 0.5) * (2.0 / full_rows) - 1.0

    def norm_x(index):
        return (index.astype(jnp.float32) + 0.5) * (2.0 / full_cols) - 1.0

    sz, sxl, sc, sxh, sy = (lax.axis_size(a) for a in FINE)
    blocks = [feat2]
    for shift in range(1, sz):
        ring = [(i, (i + shift) % sz) for i in range(sz)]
        blocks.append(lax.ppermute(feat2, "z", ring))
    zpiece = jnp.concatenate(blocks, axis=0)
    count = zpiece.shape[0]
    gathered = jnp.arange(count, dtype=jnp.int32)
    z_from = (lax.axis_index("z") - gathered // rows) % sz
    nx = sxl * sxh
    my_x = lax.axis_index("xh") * sxl + lax.axis_index("xl")
    group = queries.shape[0]
    carry = (
        jnp.full((group, 1), -1e30, jnp.float32),
        jnp.zeros((group, 1), jnp.float32),
        jnp.zeros((group, width), jnp.float32),
        jnp.zeros((group, 1), jnp.float32),
        jnp.zeros((group, 1), jnp.float32),
    )
    for shift in range(nx):
        if shift == 0:
            keys = zpiece
        else:
            pairs = []
            for xl in range(sxl):
                for xh in range(sxh):
                    there = (xh * sxl + xl + shift) % nx
                    pairs.append((xl * sxh + xh, (there % sxl) * sxh + there // sxl))
            keys = lax.ppermute(zpiece, ("xl", "xh"), pairs)
        x_from = (my_x - shift) % nx
        blk_of = (z_from * sxl + x_from % sxl) * sc + lax.axis_index("c")
        col_of = (x_from // sxl) * sy + lax.axis_index("y")
        tile_y = blk_of * rows + gathered % rows
        grid_y = jnp.broadcast_to(tile_y[:, None], (count, cols))
        grid_x = col_of * cols + jnp.broadcast_to(jnp.arange(cols, dtype=jnp.int32)[None, :], (count, cols))
        carry = flash_partials(
            queries,
            keys.reshape(count * cols, width),
            norm_y(grid_y).reshape(-1),
            norm_x(grid_x).reshape(-1),
            carry,
            scale,
            BLOCK_Q,
            BLOCK_K,
        )
    top, total, acc, along_y, along_x = (part[:, 0] if part.shape[1] == 1 else part for part in carry)
    stats = jnp.stack([top, total, along_y, along_x]).reshape(4, parts, tokens)
    stats = jnp.pad(stats.transpose(1, 0, 2), ((0, 0), (0, 0), (0, width - tokens)))
    packed = jnp.concatenate([acc.reshape(parts, tokens, width), stats], axis=1)
    packed = lax.all_to_all(packed, QUERY_AXES, 0, 0, tiled=True)
    tops = packed[:, tokens, :tokens]
    peak = jnp.max(tops, axis=0)
    factor = jnp.exp(tops - peak[None])
    acc = jnp.sum(packed[:, :tokens, :] * factor[:, :, None], axis=0)
    total = jnp.sum(packed[:, tokens + 1, :tokens] * factor, axis=0)
    along_y = jnp.sum(packed[:, tokens + 2, :tokens] * factor, axis=0)
    along_x = jnp.sum(packed[:, tokens + 3, :tokens] * factor, axis=0)
    warped = (acc / total[:, None]).astype(jnp.bfloat16).reshape(rows, cols, width)
    own_y = norm_y(row_start + jnp.arange(rows, dtype=jnp.int32))
    own_x = norm_x(col_start + jnp.arange(cols, dtype=jnp.int32))
    flow = jnp.stack(
        [
            (along_y / total).reshape(rows, cols) - own_y[:, None],
            (along_x / total).reshape(rows, cols) - own_x[None, :],
        ]
    )
    xval = feat1.astype(jnp.float32)
    yval = warped.astype(jnp.float32)
    margin = 2
    xpad = with_halo(feat1, ((BLK, 0), (COL, 1)), margin).astype(jnp.float32)
    ypad = with_halo(warped, ((BLK, 0), (COL, 1)), margin).astype(jnp.float32)
    flow_pad = with_halo(flow, ((BLK, 1), (COL, 2)), 1)
    first, grad_var, grad_cov = local_terms(xpad, ypad)
    cell_y = row_start - 1 + jnp.arange(rows + 2, dtype=jnp.int32)
    cell_x = col_start - 1 + jnp.arange(cols + 2, dtype=jnp.int32)
    inside = ((cell_y >= 0) & (cell_y < full_rows))[:, None] & ((cell_x >= 0) & (cell_x < full_cols))[None, :]
    inside = inside[:, :, None]
    spread_first = box_valid(jnp.where(inside, first, 0.0))
    spread_var = box_valid(jnp.where(inside, grad_var, 0.0))
    spread_cov = box_valid(jnp.where(inside, grad_cov, 0.0))
    grad_warped = spread_first + 2.0 * yval * spread_var + xval * spread_cov
    x_rows = xpad[margin - 1 : margin + rows + 1, margin : margin + cols]
    x_cols = xpad[margin : margin + rows, margin - 1 : margin + cols + 1]
    edge_y = row_start - 1 + jnp.arange(rows + 1, dtype=jnp.int32)
    valid_y = (edge_y >= 0) & (edge_y <= full_rows - 2)
    edge_x = col_start - 1 + jnp.arange(cols + 1, dtype=jnp.int32)
    valid_x = (edge_x >= 0) & (edge_x <= full_cols - 2)
    delta_y = flow_pad[:, 1:, 1:-1] - flow_pad[:, :-1, 1:-1]
    push_y = jnp.where(
        valid_y[None, :, None],
        charbonnier(edge_weight(x_rows[:-1], x_rows[1:])[None], delta_y),
        0.0,
    )
    delta_x = flow_pad[:, 1:-1, 1:] - flow_pad[:, 1:-1, :-1]
    push_x = jnp.where(
        valid_x[None, None, :],
        charbonnier(edge_weight(x_cols[:, :-1], x_cols[:, 1:])[None], delta_x),
        0.0,
    )
    grad_flow = push_y[:, :rows] - push_y[:, 1:] + push_x[:, :, :cols] - push_x[:, :, 1:]
    return (flow, grad_flow, grad_warped)


def solution(mesh):
    blk, col = mesh.devices.shape
    fine = mesh.devices.reshape(blk // 4, 2, 2, 2, col // 2)
    fine_mesh = Mesh(fine, FINE)
    placed = (P(BLK, COL, None), P(BLK, COL, None))
    return jax.shard_map(
        body,
        mesh=fine_mesh,
        in_specs=placed,
        out_specs=(P(None, BLK, COL), P(None, BLK, COL), P(BLK, COL, None)),
        check_vma=False,
    )
```

```python
import math

import jax
import jax.numpy as jnp
from jax import lax
from jax.experimental import pallas as pl
from jax.experimental.pallas import tpu as pltpu
from jax.sharding import Mesh
from jax.sharding import PartitionSpec as P

ssim_one = 0.01
ssim_two = 0.03
charb_sq = 0.0001

FINE = ("z", "xl", "c", "xh", "y")
BLK = ("z", "xl", "c")
COL = ("xh", "y")
QUERY_AXES = ("c", "y")
BLOCK_Q = 512
BLOCK_K = 1536


def with_halo(value, sides, width):
    for axis, dim in sides:
        count, length = (lax.axis_size(axis), value.shape[dim])
        up = [(i, (i + 1) % count) for i in range(count - 1)]
        down = [(j, i) for i, j in up]
        last = lax.slice_in_dim(value, length - width, length, axis=dim)
        first = lax.slice_in_dim(value, 0, width, axis=dim)
        before = lax.ppermute(last, axis, up)
        after = lax.ppermute(first, axis, down)
        value = jnp.concatenate([before, value, after], axis=dim)
    return value


def with_ring(value, width):
    nblk, ncol = lax.axis_size(BLK), lax.axis_size(COL)
    rows, cols = value.shape[0], value.shape[1]
    first_r, last_r = value[:width], value[rows - width :]

    def send(part, step_r, step_c):
        pairs = []
        for b in range(nblk):
            for c in range(ncol):
                tb, tc = b + step_r, c + step_c
                if 0 <= tb < nblk and 0 <= tc < ncol:
                    pairs.append((b * ncol + c, tb * ncol + tc))
        return lax.ppermute(part, FINE, pairs)

    def cut(part, side):
        return part[:, :width] if side == 0 else part[:, cols - width :]

    north = send(last_r, 1, 0)
    south = send(first_r, -1, 0)
    west = send(cut(value, 1), 0, 1)
    east = send(cut(value, 0), 0, -1)
    north_west = send(cut(last_r, 1), 1, 1)
    north_east = send(cut(last_r, 0), 1, -1)
    south_west = send(cut(first_r, 1), -1, 1)
    south_east = send(cut(first_r, 0), -1, -1)
    top = jnp.concatenate([north_west, north, north_east], axis=1)
    mid = jnp.concatenate([west, value, east], axis=1)
    bottom = jnp.concatenate([south_west, south, south_east], axis=1)
    return jnp.concatenate([top, mid, bottom], axis=0)


def box_valid(padded):
    rows_out = padded.shape[0] - 2
    cols_out = padded.shape[1] - 2
    total = jnp.zeros((rows_out, cols_out) + padded.shape[2:], padded.dtype)
    for offset_r in range(3):
        for offset_c in range(3):
            total = total + padded[offset_r : offset_r + rows_out, offset_c : offset_c + cols_out]
    return total / 9.0


def ssim_loss(mean_y, var_y, cov_xy, mean_x, var_x):
    top = (2.0 * mean_x * mean_y + ssim_one) * (2.0 * cov_xy + ssim_two)
    bottom = (mean_x * mean_x + mean_y * mean_y + ssim_one) * (var_x + var_y + ssim_two)
    return jnp.sum((1.0 - top / bottom) * 0.5)


def local_terms(xpad, ypad):
    mean_x = box_valid(xpad)
    mean_y = box_valid(ypad)
    var_x = box_valid(xpad * xpad) - mean_x * mean_x
    var_y = box_valid(ypad * ypad) - mean_y * mean_y
    cov_xy = box_valid(xpad * ypad) - mean_x * mean_y
    loss, pull = jax.vjp(
        lambda one, two, three: ssim_loss(one, two, three, mean_x, var_x), mean_y, var_y, cov_xy
    )
    grad_mean, grad_var, grad_cov = pull(jnp.ones_like(loss))
    first = grad_mean - 2.0 * grad_var * mean_y - grad_cov * mean_x
    return (first, grad_var, grad_cov)


def edge_weight(lower, upper):
    return jnp.exp(-jnp.mean(jnp.abs(upper - lower), axis=-1))


def charbonnier(weight, delta):
    return weight * delta / jnp.sqrt(delta * delta + charb_sq)


def flash_partials(queries, keys, key_y, key_x, carry, scale, block_q, block_k):
    nq, width = queries.shape
    nk = keys.shape[0]
    grid = (nq // block_q, nk // block_k)
    last = grid[1] - 1

    def kernel(q_ref, k_ref, y_ref, x_ref, top_in, total_in, acc_in, ay_in, ax_in,
               top_ref, total_ref, acc_ref, ay_ref, ax_ref, m_sc, l_sc, acc_sc, ay_sc, ax_sc):
        step = pl.program_id(1)

        @pl.when(step == 0)
        def _():
            m_sc[...] = top_in[...]
            l_sc[...] = total_in[...]
            acc_sc[...] = acc_in[...]
            ay_sc[...] = ay_in[...]
            ax_sc[...] = ax_in[...]

        k = k_ref[...]
        score = lax.dot_general(q_ref[...], k, (((1,), (1,)), ((), ())),
                                preferred_element_type=jnp.float32) * scale
        m_prev = m_sc[...]
        m_new = jnp.maximum(m_prev, jnp.max(score, axis=1, keepdims=True))
        shrink = jnp.exp(m_prev - m_new)
        expo = jnp.exp(score - m_new)
        l_sc[...] = l_sc[...] * shrink + jnp.sum(expo, axis=1, keepdims=True)
        ay_sc[...] = ay_sc[...] * shrink + jnp.sum(expo * y_ref[...], axis=1, keepdims=True)
        ax_sc[...] = ax_sc[...] * shrink + jnp.sum(expo * x_ref[...], axis=1, keepdims=True)
        acc_sc[...] = acc_sc[...] * shrink + jnp.dot(expo.astype(jnp.bfloat16), k,
                                                     preferred_element_type=jnp.float32)
        m_sc[...] = m_new

        @pl.when(step == last)
        def _():
            top_ref[...] = m_sc[...]
            total_ref[...] = l_sc[...]
            acc_ref[...] = acc_sc[...]
            ay_ref[...] = ay_sc[...]
            ax_ref[...] = ax_sc[...]

    col = pl.BlockSpec((block_q, 1), lambda i, j: (i, 0))
    top, total, acc, ay, ax = carry
    outs = pl.pallas_call(
        kernel,
        grid=grid,
        in_specs=[
            pl.BlockSpec((block_q, width), lambda i, j: (i, 0)),
            pl.BlockSpec((block_k, width), lambda i, j: (j, 0)),
            pl.BlockSpec((1, block_k), lambda i, j: (0, j)),
            pl.BlockSpec((1, block_k), lambda i, j: (0, j)),
            col,
            col,
            pl.BlockSpec((block_q, width), lambda i, j: (i, 0)),
            col,
            col,
        ],
        out_specs=[col, col, pl.BlockSpec((block_q, width), lambda i, j: (i, 0)), col, col],
        out_shape=[
            jax.ShapeDtypeStruct((nq, 1), jnp.float32),
            jax.ShapeDtypeStruct((nq, 1), jnp.float32),
            jax.ShapeDtypeStruct((nq, width), jnp.float32),
            jax.ShapeDtypeStruct((nq, 1), jnp.float32),
            jax.ShapeDtypeStruct((nq, 1), jnp.float32),
        ],
        scratch_shapes=[
            pltpu.VMEM((block_q, 1), jnp.float32),
            pltpu.VMEM((block_q, 1), jnp.float32),
            pltpu.VMEM((block_q, width), jnp.float32),
            pltpu.VMEM((block_q, 1), jnp.float32),
            pltpu.VMEM((block_q, 1), jnp.float32),
        ],
        compiler_params=pltpu.CompilerParams(dimension_semantics=("arbitrary", "arbitrary")),
        cost_estimate=pl.CostEstimate(
            flops=4 * nq * nk * width,
            transcendentals=nq * nk,
            bytes_accessed=2 * nq * width + 2 * nk * width * grid[0] + 8 * nq * width,
        ),
    )(queries, keys, key_y.reshape(1, nk), key_x.reshape(1, nk), top, total, acc, ay, ax)
    return tuple(outs)


def body(feat1, feat2):
    rows, cols, width = feat1.shape
    ncol = lax.axis_size(COL)
    full_rows = rows * lax.axis_size(BLK)
    full_cols = cols * ncol
    row_start = lax.axis_index(BLK) * rows
    col_start = lax.axis_index(COL) * cols
    scale = 1.0 / math.sqrt(width)
    tokens = rows * cols
    parts = lax.axis_size(QUERY_AXES)
    mine = feat1.reshape(tokens, width)
    arrived = [mine]
    for shift in range(1, parts):
        ring = [(i, (i + shift) % parts) for i in range(parts)]
        arrived.append(lax.ppermute(mine, QUERY_AXES, ring))
    order = (lax.axis_index(QUERY_AXES) - jnp.arange(parts, dtype=jnp.int32)) % parts
    queries = jnp.take(jnp.stack(arrived), order, axis=0).reshape(parts * tokens, width)

    def norm_y(index):
        return (index.astype(jnp.float32) + 0.5) * (2.0 / full_rows) - 1.0

    def norm_x(index):
        return (index.astype(jnp.float32) + 0.5) * (2.0 / full_cols) - 1.0

    sz, sxl, sc, sxh, sy = (lax.axis_size(a) for a in FINE)
    blocks = [feat2]
    for shift in range(1, sz):
        ring = [(i, (i + shift) % sz) for i in range(sz)]
        blocks.append(lax.ppermute(feat2, "z", ring))
    zpiece = jnp.concatenate(blocks, axis=0)
    count = zpiece.shape[0]
    gathered = jnp.arange(count, dtype=jnp.int32)
    z_from = (lax.axis_index("z") - gathered // rows) % sz
    nx = sxl * sxh
    my_x = lax.axis_index("xh") * sxl + lax.axis_index("xl")
    group = queries.shape[0]
    carry = (
        jnp.full((group, 1), -1e30, jnp.float32),
        jnp.zeros((group, 1), jnp.float32),
        jnp.zeros((group, width), jnp.float32),
        jnp.zeros((group, 1), jnp.float32),
        jnp.zeros((group, 1), jnp.float32),
    )
    for shift in range(nx):
        if shift == 0:
            keys = zpiece
        else:
            pairs = []
            for xl in range(sxl):
                for xh in range(sxh):
                    there = (xh * sxl + xl + shift) % nx
                    pairs.append((xl * sxh + xh, (there % sxl) * sxh + there // sxl))
            keys = lax.ppermute(zpiece, ("xl", "xh"), pairs)
        x_from = (my_x - shift) % nx
        blk_of = (z_from * sxl + x_from % sxl) * sc + lax.axis_index("c")
        col_of = (x_from // sxl) * sy + lax.axis_index("y")
        tile_y = blk_of * rows + gathered % rows
        grid_y = jnp.broadcast_to(tile_y[:, None], (count, cols))
        grid_x = col_of * cols + jnp.broadcast_to(jnp.arange(cols, dtype=jnp.int32)[None, :], (count, cols))
        carry = flash_partials(
            queries,
            keys.reshape(count * cols, width),
            norm_y(grid_y).reshape(-1),
            norm_x(grid_x).reshape(-1),
            carry,
            scale,
            BLOCK_Q,
            BLOCK_K,
        )
    top, total, acc, along_y, along_x = (part[:, 0] if part.shape[1] == 1 else part for part in carry)
    stats = jnp.stack([top, total, along_y, along_x]).reshape(4, parts, tokens)
    stats = jnp.pad(stats.transpose(1, 0, 2), ((0, 0), (0, 0), (0, width - tokens)))
    packed = jnp.concatenate([acc.reshape(parts, tokens, width), stats], axis=1)
    packed = lax.all_to_all(packed, QUERY_AXES, 0, 0, tiled=True)
    tops = packed[:, tokens, :tokens]
    peak = jnp.max(tops, axis=0)
    factor = jnp.exp(tops - peak[None])
    acc = jnp.sum(packed[:, :tokens, :] * factor[:, :, None], axis=0)
    total = jnp.sum(packed[:, tokens + 1, :tokens] * factor, axis=0)
    along_y = jnp.sum(packed[:, tokens + 2, :tokens] * factor, axis=0)
    along_x = jnp.sum(packed[:, tokens + 3, :tokens] * factor, axis=0)
    warped = (acc / total[:, None]).astype(jnp.bfloat16).reshape(rows, cols, width)
    own_y = norm_y(row_start + jnp.arange(rows, dtype=jnp.int32))
    own_x = norm_x(col_start + jnp.arange(cols, dtype=jnp.int32))
    flow = jnp.stack(
        [
            (along_y / total).reshape(rows, cols) - own_y[:, None],
            (along_x / total).reshape(rows, cols) - own_x[None, :],
        ]
    )
    xval = feat1.astype(jnp.float32)
    yval = warped.astype(jnp.float32)
    margin = 2
    xpad = with_ring(feat1, margin).astype(jnp.float32)
    both = jnp.concatenate([yval, flow.transpose(1, 2, 0)], axis=2)
    both = with_ring(both, margin)
    ypad = both[:, :, :width]
    flow_pad = both[margin - 1 : margin + rows + 1, margin - 1 : margin + cols + 1, width:].transpose(2, 0, 1)
    first, grad_var, grad_cov = local_terms(xpad, ypad)
    cell_y = row_start - 1 + jnp.arange(rows + 2, dtype=jnp.int32)
    cell_x = col_start - 1 + jnp.arange(cols + 2, dtype=jnp.int32)
    inside = ((cell_y >= 0) & (cell_y < full_rows))[:, None] & ((cell_x >= 0) & (cell_x < full_cols))[None, :]
    inside = inside[:, :, None]
    spread_first = box_valid(jnp.where(inside, first, 0.0))
    spread_var = box_valid(jnp.where(inside, grad_var, 0.0))
    spread_cov = box_valid(jnp.where(inside, grad_cov, 0.0))
    grad_warped = spread_first + 2.0 * yval * spread_var + xval * spread_cov
    x_rows = xpad[margin - 1 : margin + rows + 1, margin : margin + cols]
    x_cols = xpad[margin : margin + rows, margin - 1 : margin + cols + 1]
    edge_y = row_start - 1 + jnp.arange(rows + 1, dtype=jnp.int32)
    valid_y = (edge_y >= 0) & (edge_y <= full_rows - 2)
    edge_x = col_start - 1 + jnp.arange(cols + 1, dtype=jnp.int32)
    valid_x = (edge_x >= 0) & (edge_x <= full_cols - 2)
    delta_y = flow_pad[:, 1:, 1:-1] - flow_pad[:, :-1, 1:-1]
    push_y = jnp.where(
        valid_y[None, :, None],
        charbonnier(edge_weight(x_rows[:-1], x_rows[1:])[None], delta_y),
        0.0,
    )
    delta_x = flow_pad[:, 1:-1, 1:] - flow_pad[:, 1:-1, :-1]
    push_x = jnp.where(
        valid_x[None, None, :],
        charbonnier(edge_weight(x_cols[:, :-1], x_cols[:, 1:])[None], delta_x),
        0.0,
    )
    grad_flow = push_y[:, :rows] - push_y[:, 1:] + push_x[:, :, :cols] - push_x[:, :, 1:]
    return (flow, grad_flow, grad_warped)


def solution(mesh):
    blk, col = mesh.devices.shape
    fine = mesh.devices.reshape(blk // 4, 2, 2, 2, col // 2)
    fine_mesh = Mesh(fine, FINE)
    placed = (P(BLK, COL, None), P(BLK, COL, None))
    return jax.shard_map(
        body,
        mesh=fine_mesh,
        in_specs=placed,
        out_specs=(P(None, BLK, COL), P(None, BLK, COL), P(BLK, COL, None)),
        check_vma=False,
    )
```

```python
import math

import jax
import jax.numpy as jnp
from jax import lax
from jax.experimental import pallas as pl
from jax.experimental.pallas import tpu as pltpu
from jax.sharding import Mesh
from jax.sharding import PartitionSpec as P

ssim_one = 0.01
ssim_two = 0.03
charb_sq = 0.0001

FINE = ("z", "xl", "c", "xh", "y")
BLK = ("z", "xl", "c")
COL = ("xh", "y")
QUERY_AXES = ("c", "y")
BLOCK_Q = 512
BLOCK_K = 1536


def with_halo(value, sides, width):
    for axis, dim in sides:
        count, length = (lax.axis_size(axis), value.shape[dim])
        up = [(i, (i + 1) % count) for i in range(count - 1)]
        down = [(j, i) for i, j in up]
        last = lax.slice_in_dim(value, length - width, length, axis=dim)
        first = lax.slice_in_dim(value, 0, width, axis=dim)
        before = lax.ppermute(last, axis, up)
        after = lax.ppermute(first, axis, down)
        value = jnp.concatenate([before, value, after], axis=dim)
    return value


def box_valid(padded):
    rows_out = padded.shape[0] - 2
    cols_out = padded.shape[1] - 2
    total = jnp.zeros((rows_out, cols_out) + padded.shape[2:], padded.dtype)
    for offset_r in range(3):
        for offset_c in range(3):
            total = total + padded[offset_r : offset_r + rows_out, offset_c : offset_c + cols_out]
    return total / 9.0


def ssim_loss(mean_y, var_y, cov_xy, mean_x, var_x):
    top = (2.0 * mean_x * mean_y + ssim_one) * (2.0 * cov_xy + ssim_two)
    bottom = (mean_x * mean_x + mean_y * mean_y + ssim_one) * (var_x + var_y + ssim_two)
    return jnp.sum((1.0 - top / bottom) * 0.5)


def local_terms(xpad, ypad):
    mean_x = box_valid(xpad)
    mean_y = box_valid(ypad)
    var_x = box_valid(xpad * xpad) - mean_x * mean_x
    var_y = box_valid(ypad * ypad) - mean_y * mean_y
    cov_xy = box_valid(xpad * ypad) - mean_x * mean_y
    loss, pull = jax.vjp(
        lambda one, two, three: ssim_loss(one, two, three, mean_x, var_x), mean_y, var_y, cov_xy
    )
    grad_mean, grad_var, grad_cov = pull(jnp.ones_like(loss))
    first = grad_mean - 2.0 * grad_var * mean_y - grad_cov * mean_x
    return (first, grad_var, grad_cov)


def edge_weight(lower, upper):
    return jnp.exp(-jnp.mean(jnp.abs(upper - lower), axis=-1))


def charbonnier(weight, delta):
    return weight * delta / jnp.sqrt(delta * delta + charb_sq)


def flash_partials(queries, keys, key_y, key_x, carry, scale, block_q, block_k):
    nq, width = queries.shape
    nk = keys.shape[0]
    grid = (nq // block_q, nk // block_k)
    last = grid[1] - 1

    def kernel(q_ref, k_ref, y_ref, x_ref, top_in, total_in, acc_in, ay_in, ax_in,
               top_ref, total_ref, acc_ref, ay_ref, ax_ref, m_sc, l_sc, acc_sc, ay_sc, ax_sc):
        step = pl.program_id(1)

        @pl.when(step == 0)
        def _():
            m_sc[...] = top_in[...]
            l_sc[...] = total_in[...]
            acc_sc[...] = acc_in[...]
            ay_sc[...] = ay_in[...]
            ax_sc[...] = ax_in[...]

        k = k_ref[...]
        score = lax.dot_general(q_ref[...], k, (((1,), (1,)), ((), ())),
                                preferred_element_type=jnp.float32) * scale
        m_prev = m_sc[...]
        m_new = jnp.maximum(m_prev, jnp.max(score, axis=1, keepdims=True))
        shrink = jnp.exp(m_prev - m_new)
        expo = jnp.exp(score - m_new)
        l_sc[...] = l_sc[...] * shrink + jnp.sum(expo, axis=1, keepdims=True)
        ay_sc[...] = ay_sc[...] * shrink + jnp.sum(expo * y_ref[...], axis=1, keepdims=True)
        ax_sc[...] = ax_sc[...] * shrink + jnp.sum(expo * x_ref[...], axis=1, keepdims=True)
        acc_sc[...] = acc_sc[...] * shrink + jnp.dot(expo.astype(jnp.bfloat16), k,
                                                     preferred_element_type=jnp.float32)
        m_sc[...] = m_new

        @pl.when(step == last)
        def _():
            top_ref[...] = m_sc[...]
            total_ref[...] = l_sc[...]
            acc_ref[...] = acc_sc[...]
            ay_ref[...] = ay_sc[...]
            ax_ref[...] = ax_sc[...]

    col = pl.BlockSpec((block_q, 1), lambda i, j: (i, 0))
    top, total, acc, ay, ax = carry
    outs = pl.pallas_call(
        kernel,
        grid=grid,
        in_specs=[
            pl.BlockSpec((block_q, width), lambda i, j: (i, 0)),
            pl.BlockSpec((block_k, width), lambda i, j: (j, 0)),
            pl.BlockSpec((1, block_k), lambda i, j: (0, j)),
            pl.BlockSpec((1, block_k), lambda i, j: (0, j)),
            col,
            col,
            pl.BlockSpec((block_q, width), lambda i, j: (i, 0)),
            col,
            col,
        ],
        out_specs=[col, col, pl.BlockSpec((block_q, width), lambda i, j: (i, 0)), col, col],
        out_shape=[
            jax.ShapeDtypeStruct((nq, 1), jnp.float32),
            jax.ShapeDtypeStruct((nq, 1), jnp.float32),
            jax.ShapeDtypeStruct((nq, width), jnp.float32),
            jax.ShapeDtypeStruct((nq, 1), jnp.float32),
            jax.ShapeDtypeStruct((nq, 1), jnp.float32),
        ],
        scratch_shapes=[
            pltpu.VMEM((block_q, 1), jnp.float32),
            pltpu.VMEM((block_q, 1), jnp.float32),
            pltpu.VMEM((block_q, width), jnp.float32),
            pltpu.VMEM((block_q, 1), jnp.float32),
            pltpu.VMEM((block_q, 1), jnp.float32),
        ],
        compiler_params=pltpu.CompilerParams(dimension_semantics=("arbitrary", "arbitrary")),
        cost_estimate=pl.CostEstimate(
            flops=4 * nq * nk * width,
            transcendentals=nq * nk,
            bytes_accessed=2 * nq * width + 2 * nk * width * grid[0] + 8 * nq * width,
        ),
    )(queries, keys, key_y.reshape(1, nk), key_x.reshape(1, nk), top, total, acc, ay, ax)
    return tuple(outs)


def body(feat1, feat2):
    rows, cols, width = feat1.shape
    ncol = lax.axis_size(COL)
    full_rows = rows * lax.axis_size(BLK)
    full_cols = cols * ncol
    row_start = lax.axis_index(BLK) * rows
    col_start = lax.axis_index(COL) * cols
    scale = 1.0 / math.sqrt(width)
    tokens = rows * cols
    parts = lax.axis_size(QUERY_AXES)
    mine = feat1.reshape(tokens, width)
    arrived = [mine]
    for shift in range(1, parts):
        ring = [(i, (i + shift) % parts) for i in range(parts)]
        arrived.append(lax.ppermute(mine, QUERY_AXES, ring))
    order = (lax.axis_index(QUERY_AXES) - jnp.arange(parts, dtype=jnp.int32)) % parts
    queries = jnp.take(jnp.stack(arrived), order, axis=0).reshape(parts * tokens, width)

    def norm_y(index):
        return (index.astype(jnp.float32) + 0.5) * (2.0 / full_rows) - 1.0

    def norm_x(index):
        return (index.astype(jnp.float32) + 0.5) * (2.0 / full_cols) - 1.0

    sz, sxl, sc, sxh, sy = (lax.axis_size(a) for a in FINE)
    blocks = [feat2]
    for shift in range(1, sz):
        ring = [(i, (i + shift) % sz) for i in range(sz)]
        blocks.append(lax.ppermute(feat2, "z", ring))
    zpiece = jnp.concatenate(blocks, axis=0)
    count = zpiece.shape[0]
    gathered = jnp.arange(count, dtype=jnp.int32)
    z_from = (lax.axis_index("z") - gathered // rows) % sz
    nx = sxl * sxh
    my_x = lax.axis_index("xh") * sxl + lax.axis_index("xl")
    group = queries.shape[0]
    carry = (
        jnp.full((group, 1), -1e30, jnp.float32),
        jnp.zeros((group, 1), jnp.float32),
        jnp.zeros((group, width), jnp.float32),
        jnp.zeros((group, 1), jnp.float32),
        jnp.zeros((group, 1), jnp.float32),
    )
    for shift in range(nx):
        if shift == 0:
            keys = zpiece
        else:
            pairs = []
            for xl in range(sxl):
                for xh in range(sxh):
                    there = (xh * sxl + xl + shift) % nx
                    pairs.append((xl * sxh + xh, (there % sxl) * sxh + there // sxl))
            keys = lax.ppermute(zpiece, ("xl", "xh"), pairs)
        x_from = (my_x - shift) % nx
        blk_of = (z_from * sxl + x_from % sxl) * sc + lax.axis_index("c")
        col_of = (x_from // sxl) * sy + lax.axis_index("y")
        tile_y = blk_of * rows + gathered % rows
        grid_y = jnp.broadcast_to(tile_y[:, None], (count, cols))
        grid_x = col_of * cols + jnp.broadcast_to(jnp.arange(cols, dtype=jnp.int32)[None, :], (count, cols))
        carry = flash_partials(
            queries,
            keys.reshape(count * cols, width),
            norm_y(grid_y).reshape(-1),
            norm_x(grid_x).reshape(-1),
            carry,
            scale,
            BLOCK_Q,
            BLOCK_K,
        )
    top, total, acc, along_y, along_x = (part[:, 0] if part.shape[1] == 1 else part for part in carry)
    stats = jnp.stack([top, total, along_y, along_x]).reshape(4, parts, tokens)
    stats = jnp.pad(stats.transpose(1, 0, 2), ((0, 0), (0, 0), (0, width - tokens)))
    packed = jnp.concatenate([acc.reshape(parts, tokens, width), stats], axis=1)
    packed = lax.all_to_all(packed, QUERY_AXES, 0, 0, tiled=True)
    tops = packed[:, tokens, :tokens]
    peak = jnp.max(tops, axis=0)
    factor = jnp.exp(tops - peak[None])
    acc = jnp.sum(packed[:, :tokens, :] * factor[:, :, None], axis=0)
    total = jnp.sum(packed[:, tokens + 1, :tokens] * factor, axis=0)
    along_y = jnp.sum(packed[:, tokens + 2, :tokens] * factor, axis=0)
    along_x = jnp.sum(packed[:, tokens + 3, :tokens] * factor, axis=0)
    warped = (acc / total[:, None]).astype(jnp.bfloat16).reshape(rows, cols, width)
    own_y = norm_y(row_start + jnp.arange(rows, dtype=jnp.int32))
    own_x = norm_x(col_start + jnp.arange(cols, dtype=jnp.int32))
    flow = jnp.stack(
        [
            (along_y / total).reshape(rows, cols) - own_y[:, None],
            (along_x / total).reshape(rows, cols) - own_x[None, :],
        ]
    )
    xval = feat1.astype(jnp.float32)
    yval = warped.astype(jnp.float32)
    margin = 2
    xpad = with_halo(feat1, ((BLK, 0), (COL, 1)), margin).astype(jnp.float32)
    ypad = with_halo(warped, ((BLK, 0), (COL, 1)), margin).astype(jnp.float32)
    flow_pad = with_halo(flow, ((BLK, 1), (COL, 2)), 1)
    first, grad_var, grad_cov = local_terms(xpad, ypad)
    cell_y = row_start - 1 + jnp.arange(rows + 2, dtype=jnp.int32)
    cell_x = col_start - 1 + jnp.arange(cols + 2, dtype=jnp.int32)
    inside = ((cell_y >= 0) & (cell_y < full_rows))[:, None] & ((cell_x >= 0) & (cell_x < full_cols))[None, :]
    inside = inside[:, :, None]
    spread_first = box_valid(jnp.where(inside, first, 0.0))
    spread_var = box_valid(jnp.where(inside, grad_var, 0.0))
    spread_cov = box_valid(jnp.where(inside, grad_cov, 0.0))
    grad_warped = spread_first + 2.0 * yval * spread_var + xval * spread_cov
    x_rows = xpad[margin - 1 : margin + rows + 1, margin : margin + cols]
    x_cols = xpad[margin : margin + rows, margin - 1 : margin + cols + 1]
    edge_y = row_start - 1 + jnp.arange(rows + 1, dtype=jnp.int32)
    valid_y = (edge_y >= 0) & (edge_y <= full_rows - 2)
    edge_x = col_start - 1 + jnp.arange(cols + 1, dtype=jnp.int32)
    valid_x = (edge_x >= 0) & (edge_x <= full_cols - 2)
    delta_y = flow_pad[:, 1:, 1:-1] - flow_pad[:, :-1, 1:-1]
    push_y = jnp.where(
        valid_y[None, :, None],
        charbonnier(edge_weight(x_rows[:-1], x_rows[1:])[None], delta_y),
        0.0,
    )
    delta_x = flow_pad[:, 1:-1, 1:] - flow_pad[:, 1:-1, :-1]
    push_x = jnp.where(
        valid_x[None, None, :],
        charbonnier(edge_weight(x_cols[:, :-1], x_cols[:, 1:])[None], delta_x),
        0.0,
    )
    grad_flow = push_y[:, :rows] - push_y[:, 1:] + push_x[:, :, :cols] - push_x[:, :, 1:]
    return (flow, grad_flow, grad_warped)


def solution(mesh):
    blk, col = mesh.devices.shape
    fine = mesh.devices.reshape(blk // 4, 2, 2, 2, col // 2)
    fine_mesh = Mesh(fine, FINE)
    placed = (P(BLK, COL, None), P(BLK, COL, None))
    return jax.shard_map(
        body,
        mesh=fine_mesh,
        in_specs=placed,
        out_specs=(P(None, BLK, COL), P(None, BLK, COL), P(BLK, COL, None)),
        check_vma=False,
    )
```

```python
import math

import jax
import jax.numpy as jnp
from jax import lax
from jax.experimental import pallas as pl
from jax.experimental.pallas import tpu as pltpu
from jax.sharding import Mesh
from jax.sharding import PartitionSpec as P

ssim_one = 0.01
ssim_two = 0.03
charb_sq = 0.0001

FINE = ("z", "xl", "c", "xh", "y")
BLK = ("z", "xl", "c")
COL = ("xh", "y")
QUERY_AXES = ("c", "y")
BLOCK_Q = 512
BLOCK_K = 1536


def with_halo(value, sides, width):
    for axis, dim in sides:
        count, length = (lax.axis_size(axis), value.shape[dim])
        up = [(i, (i + 1) % count) for i in range(count - 1)]
        down = [(j, i) for i, j in up]
        last = lax.slice_in_dim(value, length - width, length, axis=dim)
        first = lax.slice_in_dim(value, 0, width, axis=dim)
        before = lax.ppermute(last, axis, up)
        after = lax.ppermute(first, axis, down)
        value = jnp.concatenate([before, value, after], axis=dim)
    return value


def box_valid(padded):
    rows_out = padded.shape[0] - 2
    cols_out = padded.shape[1] - 2
    total = jnp.zeros((rows_out, cols_out) + padded.shape[2:], padded.dtype)
    for offset_r in range(3):
        for offset_c in range(3):
            total = total + padded[offset_r : offset_r + rows_out, offset_c : offset_c + cols_out]
    return total / 9.0


def ssim_loss(mean_y, var_y, cov_xy, mean_x, var_x):
    top = (2.0 * mean_x * mean_y + ssim_one) * (2.0 * cov_xy + ssim_two)
    bottom = (mean_x * mean_x + mean_y * mean_y + ssim_one) * (var_x + var_y + ssim_two)
    return jnp.sum((1.0 - top / bottom) * 0.5)


def local_terms(xpad, ypad):
    mean_x = box_valid(xpad)
    mean_y = box_valid(ypad)
    var_x = box_valid(xpad * xpad) - mean_x * mean_x
    var_y = box_valid(ypad * ypad) - mean_y * mean_y
    cov_xy = box_valid(xpad * ypad) - mean_x * mean_y
    loss, pull = jax.vjp(
        lambda one, two, three: ssim_loss(one, two, three, mean_x, var_x), mean_y, var_y, cov_xy
    )
    grad_mean, grad_var, grad_cov = pull(jnp.ones_like(loss))
    first = grad_mean - 2.0 * grad_var * mean_y - grad_cov * mean_x
    return (first, grad_var, grad_cov)


def edge_weight(lower, upper):
    return jnp.exp(-jnp.mean(jnp.abs(upper - lower), axis=-1))


def charbonnier(weight, delta):
    return weight * delta / jnp.sqrt(delta * delta + charb_sq)


def flash_partials(queries, keys, key_y, key_x, carry, scale, block_q, block_k):
    nq, width = queries.shape
    nk = keys.shape[0]
    grid = (nq // block_q, nk // block_k)
    last = grid[1] - 1

    def kernel(q_ref, k_ref, y_ref, x_ref, top_in, total_in, acc_in, ay_in, ax_in,
               top_ref, total_ref, acc_ref, ay_ref, ax_ref, m_sc, l_sc, acc_sc, ay_sc, ax_sc):
        step = pl.program_id(1)

        @pl.when(step == 0)
        def _():
            m_sc[...] = top_in[...]
            l_sc[...] = total_in[...]
            acc_sc[...] = acc_in[...]
            ay_sc[...] = ay_in[...]
            ax_sc[...] = ax_in[...]

        k = k_ref[...]
        score = lax.dot_general(q_ref[...], k, (((1,), (1,)), ((), ())),
                                preferred_element_type=jnp.float32) * scale
        m_prev = m_sc[...]
        m_new = jnp.maximum(m_prev, jnp.max(score, axis=1, keepdims=True))
        shrink = jnp.exp(m_prev - m_new)
        expo = jnp.exp(score - m_new)
        l_sc[...] = l_sc[...] * shrink + jnp.sum(expo, axis=1, keepdims=True)
        ay_sc[...] = ay_sc[...] * shrink + jnp.sum(expo * y_ref[...], axis=1, keepdims=True)
        ax_sc[...] = ax_sc[...] * shrink + jnp.sum(expo * x_ref[...], axis=1, keepdims=True)
        acc_sc[...] = acc_sc[...] * shrink + jnp.dot(expo.astype(jnp.bfloat16), k,
                                                     preferred_element_type=jnp.float32)
        m_sc[...] = m_new

        @pl.when(step == last)
        def _():
            top_ref[...] = m_sc[...]
            total_ref[...] = l_sc[...]
            acc_ref[...] = acc_sc[...]
            ay_ref[...] = ay_sc[...]
            ax_ref[...] = ax_sc[...]

    col = pl.BlockSpec((block_q, 1), lambda i, j: (i, 0))
    top, total, acc, ay, ax = carry
    outs = pl.pallas_call(
        kernel,
        grid=grid,
        in_specs=[
            pl.BlockSpec((block_q, width), lambda i, j: (i, 0)),
            pl.BlockSpec((block_k, width), lambda i, j: (j, 0)),
            pl.BlockSpec((1, block_k), lambda i, j: (0, j)),
            pl.BlockSpec((1, block_k), lambda i, j: (0, j)),
            col,
            col,
            pl.BlockSpec((block_q, width), lambda i, j: (i, 0)),
            col,
            col,
        ],
        out_specs=[col, col, pl.BlockSpec((block_q, width), lambda i, j: (i, 0)), col, col],
        out_shape=[
            jax.ShapeDtypeStruct((nq, 1), jnp.float32),
            jax.ShapeDtypeStruct((nq, 1), jnp.float32),
            jax.ShapeDtypeStruct((nq, width), jnp.float32),
            jax.ShapeDtypeStruct((nq, 1), jnp.float32),
            jax.ShapeDtypeStruct((nq, 1), jnp.float32),
        ],
        scratch_shapes=[
            pltpu.VMEM((block_q, 1), jnp.float32),
            pltpu.VMEM((block_q, 1), jnp.float32),
            pltpu.VMEM((block_q, width), jnp.float32),
            pltpu.VMEM((block_q, 1), jnp.float32),
            pltpu.VMEM((block_q, 1), jnp.float32),
        ],
        compiler_params=pltpu.CompilerParams(dimension_semantics=("arbitrary", "arbitrary")),
        cost_estimate=pl.CostEstimate(
            flops=4 * nq * nk * width,
            transcendentals=nq * nk,
            bytes_accessed=2 * nq * width + 2 * nk * width * grid[0] + 8 * nq * width,
        ),
    )(queries, keys, key_y.reshape(1, nk), key_x.reshape(1, nk), top, total, acc, ay, ax)
    return tuple(outs)


def body(feat1, feat2):
    rows, cols, width = feat1.shape
    ncol = lax.axis_size(COL)
    full_rows = rows * lax.axis_size(BLK)
    full_cols = cols * ncol
    row_start = lax.axis_index(BLK) * rows
    col_start = lax.axis_index(COL) * cols
    scale = 1.0 / math.sqrt(width)
    tokens = rows * cols
    parts = lax.axis_size(QUERY_AXES)
    mine = feat1.reshape(tokens, width)
    arrived = [mine]
    for shift in range(1, parts):
        ring = [(i, (i + shift) % parts) for i in range(parts)]
        arrived.append(lax.ppermute(mine, QUERY_AXES, ring))
    order = (lax.axis_index(QUERY_AXES) - jnp.arange(parts, dtype=jnp.int32)) % parts
    queries = jnp.take(jnp.stack(arrived), order, axis=0).reshape(parts * tokens, width)

    def norm_y(index):
        return (index.astype(jnp.float32) + 0.5) * (2.0 / full_rows) - 1.0

    def norm_x(index):
        return (index.astype(jnp.float32) + 0.5) * (2.0 / full_cols) - 1.0

    sz, sxl, sc, sxh, sy = (lax.axis_size(a) for a in FINE)
    blocks = [feat2]
    for shift in range(1, sz):
        ring = [(i, (i + shift) % sz) for i in range(sz)]
        blocks.append(lax.ppermute(feat2, "z", ring))
    zpiece = jnp.concatenate(blocks, axis=0)
    count = zpiece.shape[0]
    gathered = jnp.arange(count, dtype=jnp.int32)
    z_from = (lax.axis_index("z") - gathered // rows) % sz
    nx = sxl * sxh
    my_x = lax.axis_index("xh") * sxl + lax.axis_index("xl")
    group = queries.shape[0]
    carry = (
        jnp.full((group, 1), -1e30, jnp.float32),
        jnp.zeros((group, 1), jnp.float32),
        jnp.zeros((group, width), jnp.float32),
        jnp.zeros((group, 1), jnp.float32),
        jnp.zeros((group, 1), jnp.float32),
    )
    for shift in range(nx):
        if shift == 0:
            keys = zpiece
        else:
            pairs = []
            for xl in range(sxl):
                for xh in range(sxh):
                    there = (xh * sxl + xl + shift) % nx
                    pairs.append((xl * sxh + xh, (there % sxl) * sxh + there // sxl))
            keys = lax.ppermute(zpiece, ("xl", "xh"), pairs)
        x_from = (my_x - shift) % nx
        blk_of = (z_from * sxl + x_from % sxl) * sc + lax.axis_index("c")
        col_of = (x_from // sxl) * sy + lax.axis_index("y")
        tile_y = blk_of * rows + gathered % rows
        grid_y = jnp.broadcast_to(tile_y[:, None], (count, cols))
        grid_x = col_of * cols + jnp.broadcast_to(jnp.arange(cols, dtype=jnp.int32)[None, :], (count, cols))
        carry = flash_partials(
            queries,
            keys.reshape(count * cols, width),
            norm_y(grid_y).reshape(-1),
            norm_x(grid_x).reshape(-1),
            carry,
            scale,
            BLOCK_Q,
            BLOCK_K,
        )
    top, total, acc, along_y, along_x = (part[:, 0] if part.shape[1] == 1 else part for part in carry)
    stats = jnp.stack([top, total, along_y, along_x]).reshape(4, parts, tokens)
    stats = jnp.pad(stats.transpose(1, 0, 2), ((0, 0), (0, 0), (0, width - tokens)))
    packed = jnp.concatenate([acc.reshape(parts, tokens, width), stats], axis=1)
    packed = lax.all_to_all(packed, QUERY_AXES, 0, 0, tiled=True)
    tops = packed[:, tokens, :tokens]
    peak = jnp.max(tops, axis=0)
    factor = jnp.exp(tops - peak[None])
    acc = jnp.sum(packed[:, :tokens, :] * factor[:, :, None], axis=0)
    total = jnp.sum(packed[:, tokens + 1, :tokens] * factor, axis=0)
    along_y = jnp.sum(packed[:, tokens + 2, :tokens] * factor, axis=0)
    along_x = jnp.sum(packed[:, tokens + 3, :tokens] * factor, axis=0)
    warped = (acc / total[:, None]).astype(jnp.bfloat16).reshape(rows, cols, width)
    own_y = norm_y(row_start + jnp.arange(rows, dtype=jnp.int32))
    own_x = norm_x(col_start + jnp.arange(cols, dtype=jnp.int32))
    flow = jnp.stack(
        [
            (along_y / total).reshape(rows, cols) - own_y[:, None],
            (along_x / total).reshape(rows, cols) - own_x[None, :],
        ]
    )
    xval = feat1.astype(jnp.float32)
    yval = warped.astype(jnp.float32)
    margin = 2
    xpad = with_halo(feat1, ((BLK, 0), (COL, 1)), margin).astype(jnp.float32)
    both = jnp.concatenate([yval, flow.transpose(1, 2, 0)], axis=2)
    both = with_halo(both, ((BLK, 0), (COL, 1)), margin)
    ypad = both[:, :, :width]
    flow_pad = both[margin - 1 : margin + rows + 1, margin - 1 : margin + cols + 1, width:].transpose(2, 0, 1)
    first, grad_var, grad_cov = local_terms(xpad, ypad)
    cell_y = row_start - 1 + jnp.arange(rows + 2, dtype=jnp.int32)
    cell_x = col_start - 1 + jnp.arange(cols + 2, dtype=jnp.int32)
    inside = ((cell_y >= 0) & (cell_y < full_rows))[:, None] & ((cell_x >= 0) & (cell_x < full_cols))[None, :]
    inside = inside[:, :, None]
    spread_first = box_valid(jnp.where(inside, first, 0.0))
    spread_var = box_valid(jnp.where(inside, grad_var, 0.0))
    spread_cov = box_valid(jnp.where(inside, grad_cov, 0.0))
    grad_warped = spread_first + 2.0 * yval * spread_var + xval * spread_cov
    x_rows = xpad[margin - 1 : margin + rows + 1, margin : margin + cols]
    x_cols = xpad[margin : margin + rows, margin - 1 : margin + cols + 1]
    edge_y = row_start - 1 + jnp.arange(rows + 1, dtype=jnp.int32)
    valid_y = (edge_y >= 0) & (edge_y <= full_rows - 2)
    edge_x = col_start - 1 + jnp.arange(cols + 1, dtype=jnp.int32)
    valid_x = (edge_x >= 0) & (edge_x <= full_cols - 2)
    delta_y = flow_pad[:, 1:, 1:-1] - flow_pad[:, :-1, 1:-1]
    push_y = jnp.where(
        valid_y[None, :, None],
        charbonnier(edge_weight(x_rows[:-1], x_rows[1:])[None], delta_y),
        0.0,
    )
    delta_x = flow_pad[:, 1:-1, 1:] - flow_pad[:, 1:-1, :-1]
    push_x = jnp.where(
        valid_x[None, None, :],
        charbonnier(edge_weight(x_cols[:, :-1], x_cols[:, 1:])[None], delta_x),
        0.0,
    )
    grad_flow = push_y[:, :rows] - push_y[:, 1:] + push_x[:, :, :cols] - push_x[:, :, 1:]
    return (flow, grad_flow, grad_warped)


def solution(mesh):
    blk, col = mesh.devices.shape
    fine = mesh.devices.reshape(blk // 4, 2, 2, 2, col // 2)
    fine_mesh = Mesh(fine, FINE)
    placed = (P(BLK, COL, None), P(BLK, COL, None))
    return jax.shard_map(
        body,
        mesh=fine_mesh,
        in_specs=placed,
        out_specs=(P(None, BLK, COL), P(None, BLK, COL), P(BLK, COL, None)),
        check_vma=False,
    )
```

```python
import math

import jax
import jax.numpy as jnp
from jax import lax
from jax.experimental import pallas as pl
from jax.experimental.pallas import tpu as pltpu
from jax.sharding import Mesh
from jax.sharding import PartitionSpec as P

ssim_one = 0.01
ssim_two = 0.03
charb_sq = 0.0001

FINE = ("z", "xl", "c", "xh", "y")
BLK = ("z", "xl", "c")
COL = ("xh", "y")
QUERY_AXES = ("c", "y")
BLOCK_Q = 512
BLOCK_K = 1536


def with_halo(value, sides, width):
    for axis, dim in sides:
        count, length = (lax.axis_size(axis), value.shape[dim])
        up = [(i, (i + 1) % count) for i in range(count - 1)]
        down = [(j, i) for i, j in up]
        last = lax.slice_in_dim(value, length - width, length, axis=dim)
        first = lax.slice_in_dim(value, 0, width, axis=dim)
        before = lax.ppermute(last, axis, up)
        after = lax.ppermute(first, axis, down)
        value = jnp.concatenate([before, value, after], axis=dim)
    return value


def box_valid(padded):
    rows_out = padded.shape[0] - 2
    cols_out = padded.shape[1] - 2
    total = jnp.zeros((rows_out, cols_out) + padded.shape[2:], padded.dtype)
    for offset_r in range(3):
        for offset_c in range(3):
            total = total + padded[offset_r : offset_r + rows_out, offset_c : offset_c + cols_out]
    return total / 9.0


def ssim_loss(mean_y, var_y, cov_xy, mean_x, var_x):
    top = (2.0 * mean_x * mean_y + ssim_one) * (2.0 * cov_xy + ssim_two)
    bottom = (mean_x * mean_x + mean_y * mean_y + ssim_one) * (var_x + var_y + ssim_two)
    return jnp.sum((1.0 - top / bottom) * 0.5)


def local_terms(xpad, ypad):
    mean_x = box_valid(xpad)
    mean_y = box_valid(ypad)
    var_x = box_valid(xpad * xpad) - mean_x * mean_x
    var_y = box_valid(ypad * ypad) - mean_y * mean_y
    cov_xy = box_valid(xpad * ypad) - mean_x * mean_y
    loss, pull = jax.vjp(
        lambda one, two, three: ssim_loss(one, two, three, mean_x, var_x), mean_y, var_y, cov_xy
    )
    grad_mean, grad_var, grad_cov = pull(jnp.ones_like(loss))
    first = grad_mean - 2.0 * grad_var * mean_y - grad_cov * mean_x
    return (first, grad_var, grad_cov)


def edge_weight(lower, upper):
    return jnp.exp(-jnp.mean(jnp.abs(upper - lower), axis=-1))


def charbonnier(weight, delta):
    return weight * delta / jnp.sqrt(delta * delta + charb_sq)


def flash_partials(queries, keys, key_y, key_x, carry, scale, block_q, block_k):
    nq, width = queries.shape
    nk = keys.shape[0]
    grid = (nq // block_q, nk // block_k)
    last = grid[1] - 1

    def kernel(q_ref, k_ref, y_ref, x_ref, top_in, total_in, acc_in, ay_in, ax_in,
               top_ref, total_ref, acc_ref, ay_ref, ax_ref, m_sc, l_sc, acc_sc, ay_sc, ax_sc):
        step = pl.program_id(1)

        @pl.when(step == 0)
        def _():
            m_sc[...] = top_in[...]
            l_sc[...] = total_in[...]
            acc_sc[...] = acc_in[...]
            ay_sc[...] = ay_in[...]
            ax_sc[...] = ax_in[...]

        k = k_ref[...]
        score = lax.dot_general(q_ref[...], k, (((1,), (1,)), ((), ())),
                                preferred_element_type=jnp.float32) * scale
        m_prev = m_sc[...]
        m_new = jnp.maximum(m_prev, jnp.max(score, axis=1, keepdims=True))
        shrink = jnp.exp(m_prev - m_new)
        expo = jnp.exp(score - m_new)
        l_sc[...] = l_sc[...] * shrink + jnp.sum(expo, axis=1, keepdims=True)
        ay_sc[...] = ay_sc[...] * shrink + jnp.sum(expo * y_ref[...], axis=1, keepdims=True)
        ax_sc[...] = ax_sc[...] * shrink + jnp.sum(expo * x_ref[...], axis=1, keepdims=True)
        acc_sc[...] = acc_sc[...] * shrink + jnp.dot(expo.astype(jnp.bfloat16), k,
                                                     preferred_element_type=jnp.float32)
        m_sc[...] = m_new

        @pl.when(step == last)
        def _():
            top_ref[...] = m_sc[...]
            total_ref[...] = l_sc[...]
            acc_ref[...] = acc_sc[...]
            ay_ref[...] = ay_sc[...]
            ax_ref[...] = ax_sc[...]

    col = pl.BlockSpec((block_q, 1), lambda i, j: (i, 0))
    top, total, acc, ay, ax = carry
    outs = pl.pallas_call(
        kernel,
        grid=grid,
        in_specs=[
            pl.BlockSpec((block_q, width), lambda i, j: (i, 0)),
            pl.BlockSpec((block_k, width), lambda i, j: (j, 0)),
            pl.BlockSpec((1, block_k), lambda i, j: (0, j)),
            pl.BlockSpec((1, block_k), lambda i, j: (0, j)),
            col,
            col,
            pl.BlockSpec((block_q, width), lambda i, j: (i, 0)),
            col,
            col,
        ],
        out_specs=[col, col, pl.BlockSpec((block_q, width), lambda i, j: (i, 0)), col, col],
        out_shape=[
            jax.ShapeDtypeStruct((nq, 1), jnp.float32),
            jax.ShapeDtypeStruct((nq, 1), jnp.float32),
            jax.ShapeDtypeStruct((nq, width), jnp.float32),
            jax.ShapeDtypeStruct((nq, 1), jnp.float32),
            jax.ShapeDtypeStruct((nq, 1), jnp.float32),
        ],
        scratch_shapes=[
            pltpu.VMEM((block_q, 1), jnp.float32),
            pltpu.VMEM((block_q, 1), jnp.float32),
            pltpu.VMEM((block_q, width), jnp.float32),
            pltpu.VMEM((block_q, 1), jnp.float32),
            pltpu.VMEM((block_q, 1), jnp.float32),
        ],
        compiler_params=pltpu.CompilerParams(dimension_semantics=("arbitrary", "arbitrary")),
        cost_estimate=pl.CostEstimate(
            flops=4 * nq * nk * width,
            transcendentals=nq * nk,
            bytes_accessed=2 * nq * width + 2 * nk * width * grid[0] + 8 * nq * width,
        ),
    )(queries, keys, key_y.reshape(1, nk), key_x.reshape(1, nk), top, total, acc, ay, ax)
    return tuple(outs)


def body(feat1, feat2):
    rows, cols, width = feat1.shape
    ncol = lax.axis_size(COL)
    full_rows = rows * lax.axis_size(BLK)
    full_cols = cols * ncol
    row_start = lax.axis_index(BLK) * rows
    col_start = lax.axis_index(COL) * cols
    scale = 1.0 / math.sqrt(width)
    tokens = rows * cols
    parts = lax.axis_size(QUERY_AXES)
    mine = feat1.reshape(tokens, width)
    arrived = [mine]
    for shift in range(1, parts):
        ring = [(i, (i + shift) % parts) for i in range(parts)]
        arrived.append(lax.ppermute(mine, QUERY_AXES, ring))
    order = (lax.axis_index(QUERY_AXES) - jnp.arange(parts, dtype=jnp.int32)) % parts
    queries = jnp.take(jnp.stack(arrived), order, axis=0).reshape(parts * tokens, width)

    def norm_y(index):
        return (index.astype(jnp.float32) + 0.5) * (2.0 / full_rows) - 1.0

    def norm_x(index):
        return (index.astype(jnp.float32) + 0.5) * (2.0 / full_cols) - 1.0

    sz, sxl, sc, sxh, sy = (lax.axis_size(a) for a in FINE)
    blocks = [feat2]
    for shift in range(1, sz):
        ring = [(i, (i + shift) % sz) for i in range(sz)]
        blocks.append(lax.ppermute(feat2, "z", ring))
    zpiece = jnp.concatenate(blocks, axis=0)
    count = zpiece.shape[0]
    gathered = jnp.arange(count, dtype=jnp.int32)
    z_from = (lax.axis_index("z") - gathered // rows) % sz
    nx = sxl * sxh
    my_x = lax.axis_index("xh") * sxl + lax.axis_index("xl")
    group = queries.shape[0]
    carry = (
        jnp.full((group, 1), -1e30, jnp.float32),
        jnp.zeros((group, 1), jnp.float32),
        jnp.zeros((group, width), jnp.float32),
        jnp.zeros((group, 1), jnp.float32),
        jnp.zeros((group, 1), jnp.float32),
    )
    for shift in range(nx):
        if shift == 0:
            keys = zpiece
        else:
            pairs = []
            for xl in range(sxl):
                for xh in range(sxh):
                    there = (xh * sxl + xl + shift) % nx
                    pairs.append((xl * sxh + xh, (there % sxl) * sxh + there // sxl))
            keys = lax.ppermute(zpiece, ("xl", "xh"), pairs)
        x_from = (my_x - shift) % nx
        blk_of = (z_from * sxl + x_from % sxl) * sc + lax.axis_index("c")
        col_of = (x_from // sxl) * sy + lax.axis_index("y")
        tile_y = blk_of * rows + gathered % rows
        grid_y = jnp.broadcast_to(tile_y[:, None], (count, cols))
        grid_x = col_of * cols + jnp.broadcast_to(jnp.arange(cols, dtype=jnp.int32)[None, :], (count, cols))
        carry = flash_partials(
            queries,
            keys.reshape(count * cols, width),
            norm_y(grid_y).reshape(-1),
            norm_x(grid_x).reshape(-1),
            carry,
            scale,
            BLOCK_Q,
            BLOCK_K,
        )
    top, total, acc, along_y, along_x = (part[:, 0] if part.shape[1] == 1 else part for part in carry)
    stats = jnp.stack([top, total, along_y, along_x]).reshape(4, parts, tokens)
    stats = jnp.pad(stats.transpose(1, 0, 2), ((0, 0), (0, 0), (0, width - tokens)))
    packed = jnp.concatenate([acc.reshape(parts, tokens, width), stats], axis=1)
    me = lax.axis_index(QUERY_AXES)
    returned = [lax.dynamic_index_in_dim(packed, me, axis=0, keepdims=False)]
    for shift in range(1, parts):
        ring = [(i, (i + shift) % parts) for i in range(parts)]
        block = lax.dynamic_index_in_dim(packed, (me + shift) % parts, axis=0, keepdims=False)
        returned.append(lax.ppermute(block, QUERY_AXES, ring))
    packed = jnp.stack(returned)
    tops = packed[:, tokens, :tokens]
    peak = jnp.max(tops, axis=0)
    factor = jnp.exp(tops - peak[None])
    acc = jnp.sum(packed[:, :tokens, :] * factor[:, :, None], axis=0)
    total = jnp.sum(packed[:, tokens + 1, :tokens] * factor, axis=0)
    along_y = jnp.sum(packed[:, tokens + 2, :tokens] * factor, axis=0)
    along_x = jnp.sum(packed[:, tokens + 3, :tokens] * factor, axis=0)
    warped = (acc / total[:, None]).astype(jnp.bfloat16).reshape(rows, cols, width)
    own_y = norm_y(row_start + jnp.arange(rows, dtype=jnp.int32))
    own_x = norm_x(col_start + jnp.arange(cols, dtype=jnp.int32))
    flow = jnp.stack(
        [
            (along_y / total).reshape(rows, cols) - own_y[:, None],
            (along_x / total).reshape(rows, cols) - own_x[None, :],
        ]
    )
    xval = feat1.astype(jnp.float32)
    yval = warped.astype(jnp.float32)
    margin = 2
    xpad = with_halo(feat1, ((BLK, 0), (COL, 1)), margin).astype(jnp.float32)
    both = jnp.concatenate([yval, flow.transpose(1, 2, 0)], axis=2)
    both = with_halo(both, ((BLK, 0), (COL, 1)), margin)
    ypad = both[:, :, :width]
    flow_pad = both[margin - 1 : margin + rows + 1, margin - 1 : margin + cols + 1, width:].transpose(2, 0, 1)
    first, grad_var, grad_cov = local_terms(xpad, ypad)
    cell_y = row_start - 1 + jnp.arange(rows + 2, dtype=jnp.int32)
    cell_x = col_start - 1 + jnp.arange(cols + 2, dtype=jnp.int32)
    inside = ((cell_y >= 0) & (cell_y < full_rows))[:, None] & ((cell_x >= 0) & (cell_x < full_cols))[None, :]
    inside = inside[:, :, None]
    spread_first = box_valid(jnp.where(inside, first, 0.0))
    spread_var = box_valid(jnp.where(inside, grad_var, 0.0))
    spread_cov = box_valid(jnp.where(inside, grad_cov, 0.0))
    grad_warped = spread_first + 2.0 * yval * spread_var + xval * spread_cov
    x_rows = xpad[margin - 1 : margin + rows + 1, margin : margin + cols]
    x_cols = xpad[margin : margin + rows, margin - 1 : margin + cols + 1]
    edge_y = row_start - 1 + jnp.arange(rows + 1, dtype=jnp.int32)
    valid_y = (edge_y >= 0) & (edge_y <= full_rows - 2)
    edge_x = col_start - 1 + jnp.arange(cols + 1, dtype=jnp.int32)
    valid_x = (edge_x >= 0) & (edge_x <= full_cols - 2)
    delta_y = flow_pad[:, 1:, 1:-1] - flow_pad[:, :-1, 1:-1]
    push_y = jnp.where(
        valid_y[None, :, None],
        charbonnier(edge_weight(x_rows[:-1], x_rows[1:])[None], delta_y),
        0.0,
    )
    delta_x = flow_pad[:, 1:-1, 1:] - flow_pad[:, 1:-1, :-1]
    push_x = jnp.where(
        valid_x[None, None, :],
        charbonnier(edge_weight(x_cols[:, :-1], x_cols[:, 1:])[None], delta_x),
        0.0,
    )
    grad_flow = push_y[:, :rows] - push_y[:, 1:] + push_x[:, :, :cols] - push_x[:, :, 1:]
    return (flow, grad_flow, grad_warped)


def solution(mesh):
    blk, col = mesh.devices.shape
    fine = mesh.devices.reshape(blk // 4, 2, 2, 2, col // 2)
    fine_mesh = Mesh(fine, FINE)
    placed = (P(BLK, COL, None), P(BLK, COL, None))
    return jax.shard_map(
        body,
        mesh=fine_mesh,
        in_specs=placed,
        out_specs=(P(None, BLK, COL), P(None, BLK, COL), P(BLK, COL, None)),
        check_vma=False,
    )
```

```python
import math

import jax
import jax.numpy as jnp
from jax import lax
from jax.experimental import pallas as pl
from jax.experimental.pallas import tpu as pltpu
from jax.sharding import Mesh
from jax.sharding import PartitionSpec as P

ssim_one = 0.01
ssim_two = 0.03
charb_sq = 0.0001

FINE = ("z", "xl", "c", "xh", "y")
BLK = ("z", "xl", "c")
COL = ("xh", "y")
QUERY_AXES = ("c", "y")
BLOCK_Q = 512
BLOCK_K = 1536


def with_halo(value, sides, width):
    for axis, dim in sides:
        count, length = (lax.axis_size(axis), value.shape[dim])
        up = [(i, (i + 1) % count) for i in range(count - 1)]
        down = [(j, i) for i, j in up]
        last = lax.slice_in_dim(value, length - width, length, axis=dim)
        first = lax.slice_in_dim(value, 0, width, axis=dim)
        before = lax.ppermute(last, axis, up)
        after = lax.ppermute(first, axis, down)
        value = jnp.concatenate([before, value, after], axis=dim)
    return value


def box_valid(padded):
    rows_out = padded.shape[0] - 2
    cols_out = padded.shape[1] - 2
    total = jnp.zeros((rows_out, cols_out) + padded.shape[2:], padded.dtype)
    for offset_r in range(3):
        for offset_c in range(3):
            total = total + padded[offset_r : offset_r + rows_out, offset_c : offset_c + cols_out]
    return total / 9.0


def ssim_loss(mean_y, var_y, cov_xy, mean_x, var_x):
    top = (2.0 * mean_x * mean_y + ssim_one) * (2.0 * cov_xy + ssim_two)
    bottom = (mean_x * mean_x + mean_y * mean_y + ssim_one) * (var_x + var_y + ssim_two)
    return jnp.sum((1.0 - top / bottom) * 0.5)


def local_terms(xpad, ypad):
    mean_x = box_valid(xpad)
    mean_y = box_valid(ypad)
    var_x = box_valid(xpad * xpad) - mean_x * mean_x
    var_y = box_valid(ypad * ypad) - mean_y * mean_y
    cov_xy = box_valid(xpad * ypad) - mean_x * mean_y
    loss, pull = jax.vjp(
        lambda one, two, three: ssim_loss(one, two, three, mean_x, var_x), mean_y, var_y, cov_xy
    )
    grad_mean, grad_var, grad_cov = pull(jnp.ones_like(loss))
    first = grad_mean - 2.0 * grad_var * mean_y - grad_cov * mean_x
    return (first, grad_var, grad_cov)


def edge_weight(lower, upper):
    return jnp.exp(-jnp.mean(jnp.abs(upper - lower), axis=-1))


def charbonnier(weight, delta):
    return weight * delta / jnp.sqrt(delta * delta + charb_sq)


def flash_partials(queries, keys, key_y, key_x, carry, scale, block_q, block_k):
    nq, width = queries.shape
    nk = keys.shape[0]
    grid = (nq // block_q, nk // block_k)
    last = grid[1] - 1

    fresh = carry is None

    def kernel(q_ref, k_ref, y_ref, x_ref, *refs):
        if fresh:
            refs = (None,) * 5 + refs
        top_in, total_in, acc_in, ay_in, ax_in = refs[:5]
        top_ref, total_ref, acc_ref, ay_ref, ax_ref, m_sc, l_sc, acc_sc, ay_sc, ax_sc = refs[5:]
        step = pl.program_id(1)

        @pl.when(step == 0)
        def _():
            if fresh:
                m_sc[...] = jnp.full(m_sc.shape, -1e30, jnp.float32)
                l_sc[...] = jnp.zeros(l_sc.shape, jnp.float32)
                acc_sc[...] = jnp.zeros(acc_sc.shape, jnp.float32)
                ay_sc[...] = jnp.zeros(ay_sc.shape, jnp.float32)
                ax_sc[...] = jnp.zeros(ax_sc.shape, jnp.float32)
            else:
                m_sc[...] = top_in[...]
                l_sc[...] = total_in[...]
                acc_sc[...] = acc_in[...]
                ay_sc[...] = ay_in[...]
                ax_sc[...] = ax_in[...]

        k = k_ref[...]
        score = lax.dot_general(q_ref[...], k, (((1,), (1,)), ((), ())),
                                preferred_element_type=jnp.float32) * scale
        m_prev = m_sc[...]
        m_new = jnp.maximum(m_prev, jnp.max(score, axis=1, keepdims=True))
        shrink = jnp.exp(m_prev - m_new)
        expo = jnp.exp(score - m_new)
        l_sc[...] = l_sc[...] * shrink + jnp.sum(expo, axis=1, keepdims=True)
        ay_sc[...] = ay_sc[...] * shrink + jnp.sum(expo * y_ref[...], axis=1, keepdims=True)
        ax_sc[...] = ax_sc[...] * shrink + jnp.sum(expo * x_ref[...], axis=1, keepdims=True)
        acc_sc[...] = acc_sc[...] * shrink + jnp.dot(expo.astype(jnp.bfloat16), k,
                                                     preferred_element_type=jnp.float32)
        m_sc[...] = m_new

        @pl.when(step == last)
        def _():
            top_ref[...] = m_sc[...]
            total_ref[...] = l_sc[...]
            acc_ref[...] = acc_sc[...]
            ay_ref[...] = ay_sc[...]
            ax_ref[...] = ax_sc[...]

    col = pl.BlockSpec((block_q, 1), lambda i, j: (i, 0))
    extra = () if fresh else tuple(carry)
    outs = pl.pallas_call(
        kernel,
        grid=grid,
        in_specs=[
            pl.BlockSpec((block_q, width), lambda i, j: (i, 0)),
            pl.BlockSpec((block_k, width), lambda i, j: (j, 0)),
            pl.BlockSpec((1, block_k), lambda i, j: (0, j)),
            pl.BlockSpec((1, block_k), lambda i, j: (0, j)),
        ]
        + ([] if fresh else [col, col, pl.BlockSpec((block_q, width), lambda i, j: (i, 0)), col, col]),
        out_specs=[col, col, pl.BlockSpec((block_q, width), lambda i, j: (i, 0)), col, col],
        out_shape=[
            jax.ShapeDtypeStruct((nq, 1), jnp.float32),
            jax.ShapeDtypeStruct((nq, 1), jnp.float32),
            jax.ShapeDtypeStruct((nq, width), jnp.float32),
            jax.ShapeDtypeStruct((nq, 1), jnp.float32),
            jax.ShapeDtypeStruct((nq, 1), jnp.float32),
        ],
        scratch_shapes=[
            pltpu.VMEM((block_q, 1), jnp.float32),
            pltpu.VMEM((block_q, 1), jnp.float32),
            pltpu.VMEM((block_q, width), jnp.float32),
            pltpu.VMEM((block_q, 1), jnp.float32),
            pltpu.VMEM((block_q, 1), jnp.float32),
        ],
        compiler_params=pltpu.CompilerParams(dimension_semantics=("arbitrary", "arbitrary")),
        cost_estimate=pl.CostEstimate(
            flops=4 * nq * nk * width,
            transcendentals=nq * nk,
            bytes_accessed=2 * nq * width + 2 * nk * width * grid[0] + 8 * nq * width,
        ),
    )(queries, keys, key_y.reshape(1, nk), key_x.reshape(1, nk), *extra)
    return tuple(outs)


def body(feat1, feat2):
    rows, cols, width = feat1.shape
    ncol = lax.axis_size(COL)
    full_rows = rows * lax.axis_size(BLK)
    full_cols = cols * ncol
    row_start = lax.axis_index(BLK) * rows
    col_start = lax.axis_index(COL) * cols
    scale = 1.0 / math.sqrt(width)
    tokens = rows * cols
    parts = lax.axis_size(QUERY_AXES)
    mine = feat1.reshape(tokens, width)
    arrived = [mine]
    for shift in range(1, parts):
        ring = [(i, (i + shift) % parts) for i in range(parts)]
        arrived.append(lax.ppermute(mine, QUERY_AXES, ring))
    order = (lax.axis_index(QUERY_AXES) - jnp.arange(parts, dtype=jnp.int32)) % parts
    queries = jnp.take(jnp.stack(arrived), order, axis=0).reshape(parts * tokens, width)

    def norm_y(index):
        return (index.astype(jnp.float32) + 0.5) * (2.0 / full_rows) - 1.0

    def norm_x(index):
        return (index.astype(jnp.float32) + 0.5) * (2.0 / full_cols) - 1.0

    sz, sxl, sc, sxh, sy = (lax.axis_size(a) for a in FINE)
    blocks = [feat2]
    for shift in range(1, sz):
        ring = [(i, (i + shift) % sz) for i in range(sz)]
        blocks.append(lax.ppermute(feat2, "z", ring))
    zpiece = jnp.concatenate(blocks, axis=0)
    count = zpiece.shape[0]
    gathered = jnp.arange(count, dtype=jnp.int32)
    z_from = (lax.axis_index("z") - gathered // rows) % sz
    nx = sxl * sxh
    my_x = lax.axis_index("xh") * sxl + lax.axis_index("xl")
    carry = None
    for shift in range(nx):
        if shift == 0:
            keys = zpiece
        else:
            pairs = []
            for xl in range(sxl):
                for xh in range(sxh):
                    there = (xh * sxl + xl + shift) % nx
                    pairs.append((xl * sxh + xh, (there % sxl) * sxh + there // sxl))
            keys = lax.ppermute(zpiece, ("xl", "xh"), pairs)
        x_from = (my_x - shift) % nx
        blk_of = (z_from * sxl + x_from % sxl) * sc + lax.axis_index("c")
        col_of = (x_from // sxl) * sy + lax.axis_index("y")
        tile_y = blk_of * rows + gathered % rows
        grid_y = jnp.broadcast_to(tile_y[:, None], (count, cols))
        grid_x = col_of * cols + jnp.broadcast_to(jnp.arange(cols, dtype=jnp.int32)[None, :], (count, cols))
        carry = flash_partials(
            queries,
            keys.reshape(count * cols, width),
            norm_y(grid_y).reshape(-1),
            norm_x(grid_x).reshape(-1),
            carry,
            scale,
            BLOCK_Q,
            BLOCK_K,
        )
    top, total, acc, along_y, along_x = (part[:, 0] if part.shape[1] == 1 else part for part in carry)
    stats = jnp.stack([top, total, along_y, along_x]).reshape(4, parts, tokens)
    stats = jnp.pad(stats.transpose(1, 0, 2), ((0, 0), (0, 0), (0, width - tokens)))
    packed = jnp.concatenate([acc.reshape(parts, tokens, width), stats], axis=1)
    packed = lax.all_to_all(packed, QUERY_AXES, 0, 0, tiled=True)
    tops = packed[:, tokens, :tokens]
    peak = jnp.max(tops, axis=0)
    factor = jnp.exp(tops - peak[None])
    acc = jnp.sum(packed[:, :tokens, :] * factor[:, :, None], axis=0)
    total = jnp.sum(packed[:, tokens + 1, :tokens] * factor, axis=0)
    along_y = jnp.sum(packed[:, tokens + 2, :tokens] * factor, axis=0)
    along_x = jnp.sum(packed[:, tokens + 3, :tokens] * factor, axis=0)
    warped = (acc / total[:, None]).astype(jnp.bfloat16).reshape(rows, cols, width)
    own_y = norm_y(row_start + jnp.arange(rows, dtype=jnp.int32))
    own_x = norm_x(col_start + jnp.arange(cols, dtype=jnp.int32))
    flow = jnp.stack(
        [
            (along_y / total).reshape(rows, cols) - own_y[:, None],
            (along_x / total).reshape(rows, cols) - own_x[None, :],
        ]
    )
    xval = feat1.astype(jnp.float32)
    yval = warped.astype(jnp.float32)
    margin = 2
    xpad = with_halo(feat1, ((BLK, 0), (COL, 1)), margin).astype(jnp.float32)
    both = jnp.concatenate([yval, flow.transpose(1, 2, 0)], axis=2)
    both = with_halo(both, ((BLK, 0), (COL, 1)), margin)
    ypad = both[:, :, :width]
    flow_pad = both[margin - 1 : margin + rows + 1, margin - 1 : margin + cols + 1, width:].transpose(2, 0, 1)
    first, grad_var, grad_cov = local_terms(xpad, ypad)
    cell_y = row_start - 1 + jnp.arange(rows + 2, dtype=jnp.int32)
    cell_x = col_start - 1 + jnp.arange(cols + 2, dtype=jnp.int32)
    inside = ((cell_y >= 0) & (cell_y < full_rows))[:, None] & ((cell_x >= 0) & (cell_x < full_cols))[None, :]
    inside = inside[:, :, None]
    spread_first = box_valid(jnp.where(inside, first, 0.0))
    spread_var = box_valid(jnp.where(inside, grad_var, 0.0))
    spread_cov = box_valid(jnp.where(inside, grad_cov, 0.0))
    grad_warped = spread_first + 2.0 * yval * spread_var + xval * spread_cov
    x_rows = xpad[margin - 1 : margin + rows + 1, margin : margin + cols]
    x_cols = xpad[margin : margin + rows, margin - 1 : margin + cols + 1]
    edge_y = row_start - 1 + jnp.arange(rows + 1, dtype=jnp.int32)
    valid_y = (edge_y >= 0) & (edge_y <= full_rows - 2)
    edge_x = col_start - 1 + jnp.arange(cols + 1, dtype=jnp.int32)
    valid_x = (edge_x >= 0) & (edge_x <= full_cols - 2)
    delta_y = flow_pad[:, 1:, 1:-1] - flow_pad[:, :-1, 1:-1]
    push_y = jnp.where(
        valid_y[None, :, None],
        charbonnier(edge_weight(x_rows[:-1], x_rows[1:])[None], delta_y),
        0.0,
    )
    delta_x = flow_pad[:, 1:-1, 1:] - flow_pad[:, 1:-1, :-1]
    push_x = jnp.where(
        valid_x[None, None, :],
        charbonnier(edge_weight(x_cols[:, :-1], x_cols[:, 1:])[None], delta_x),
        0.0,
    )
    grad_flow = push_y[:, :rows] - push_y[:, 1:] + push_x[:, :, :cols] - push_x[:, :, 1:]
    return (flow, grad_flow, grad_warped)


def solution(mesh):
    blk, col = mesh.devices.shape
    fine = mesh.devices.reshape(blk // 4, 2, 2, 2, col // 2)
    fine_mesh = Mesh(fine, FINE)
    placed = (P(BLK, COL, None), P(BLK, COL, None))
    return jax.shard_map(
        body,
        mesh=fine_mesh,
        in_specs=placed,
        out_specs=(P(None, BLK, COL), P(None, BLK, COL), P(BLK, COL, None)),
        check_vma=False,
    )
```

```python
import math

import jax
import jax.numpy as jnp
from jax import lax
from jax.experimental import pallas as pl
from jax.experimental.pallas import tpu as pltpu
from jax.sharding import Mesh
from jax.sharding import PartitionSpec as P

ssim_one = 0.01
ssim_two = 0.03
charb_sq = 0.0001

FINE = ("z", "xl", "c", "xh", "y")
BLK = ("z", "xl", "c")
COL = ("xh", "y")
QUERY_AXES = ("c", "y")
BLOCK_Q = 512
BLOCK_K = 1536


def with_halo(value, sides, width):
    for axis, dim in sides:
        count, length = (lax.axis_size(axis), value.shape[dim])
        up = [(i, (i + 1) % count) for i in range(count - 1)]
        down = [(j, i) for i, j in up]
        last = lax.slice_in_dim(value, length - width, length, axis=dim)
        first = lax.slice_in_dim(value, 0, width, axis=dim)
        before = lax.ppermute(last, axis, up)
        after = lax.ppermute(first, axis, down)
        value = jnp.concatenate([before, value, after], axis=dim)
    return value


def box_valid(padded):
    rows_out = padded.shape[0] - 2
    cols_out = padded.shape[1] - 2
    total = jnp.zeros((rows_out, cols_out) + padded.shape[2:], padded.dtype)
    for offset_r in range(3):
        for offset_c in range(3):
            total = total + padded[offset_r : offset_r + rows_out, offset_c : offset_c + cols_out]
    return total / 9.0


def ssim_loss(mean_y, var_y, cov_xy, mean_x, var_x):
    top = (2.0 * mean_x * mean_y + ssim_one) * (2.0 * cov_xy + ssim_two)
    bottom = (mean_x * mean_x + mean_y * mean_y + ssim_one) * (var_x + var_y + ssim_two)
    return jnp.sum((1.0 - top / bottom) * 0.5)


def local_terms(xpad, ypad):
    mean_x = box_valid(xpad)
    mean_y = box_valid(ypad)
    var_x = box_valid(xpad * xpad) - mean_x * mean_x
    var_y = box_valid(ypad * ypad) - mean_y * mean_y
    cov_xy = box_valid(xpad * ypad) - mean_x * mean_y
    loss, pull = jax.vjp(
        lambda one, two, three: ssim_loss(one, two, three, mean_x, var_x), mean_y, var_y, cov_xy
    )
    grad_mean, grad_var, grad_cov = pull(jnp.ones_like(loss))
    first = grad_mean - 2.0 * grad_var * mean_y - grad_cov * mean_x
    return (first, grad_var, grad_cov)


def edge_weight(lower, upper):
    return jnp.exp(-jnp.mean(jnp.abs(upper - lower), axis=-1))


def charbonnier(weight, delta):
    return weight * delta / jnp.sqrt(delta * delta + charb_sq)


def flash_partials(queries, keys, key_y, key_x, carry, scale, block_q, block_k):
    nq, width = queries.shape
    nk = keys.shape[0]
    grid = (nq // block_q, nk // block_k)
    last = grid[1] - 1

    fresh = carry is None

    def kernel(q_ref, k_ref, y_ref, x_ref, *refs):
        if fresh:
            refs = (None,) * 5 + refs
        top_in, total_in, acc_in, ay_in, ax_in = refs[:5]
        top_ref, total_ref, acc_ref, ay_ref, ax_ref, m_sc, l_sc, acc_sc, ay_sc, ax_sc = refs[5:]
        step = pl.program_id(1)

        @pl.when(step == 0)
        def _():
            if fresh:
                m_sc[...] = jnp.full(m_sc.shape, -1e30, jnp.float32)
                l_sc[...] = jnp.zeros(l_sc.shape, jnp.float32)
                acc_sc[...] = jnp.zeros(acc_sc.shape, jnp.float32)
                ay_sc[...] = jnp.zeros(ay_sc.shape, jnp.float32)
                ax_sc[...] = jnp.zeros(ax_sc.shape, jnp.float32)
            else:
                m_sc[...] = top_in[...]
                l_sc[...] = total_in[...]
                acc_sc[...] = acc_in[...]
                ay_sc[...] = ay_in[...]
                ax_sc[...] = ax_in[...]

        k = k_ref[...]
        score = lax.dot_general(q_ref[...], k, (((1,), (1,)), ((), ())),
                                preferred_element_type=jnp.float32) * scale
        m_prev = m_sc[...]
        m_new = jnp.maximum(m_prev, jnp.max(score, axis=1, keepdims=True))
        shrink = jnp.exp(m_prev - m_new)
        expo = jnp.exp(score - m_new)
        l_sc[...] = l_sc[...] * shrink + jnp.sum(expo, axis=1, keepdims=True)
        ay_sc[...] = ay_sc[...] * shrink + jnp.sum(expo * y_ref[...], axis=1, keepdims=True)
        ax_sc[...] = ax_sc[...] * shrink + jnp.sum(expo * x_ref[...], axis=1, keepdims=True)
        acc_sc[...] = acc_sc[...] * shrink + jnp.dot(expo.astype(jnp.bfloat16), k,
                                                     preferred_element_type=jnp.float32)
        m_sc[...] = m_new

        @pl.when(step == last)
        def _():
            top_ref[...] = m_sc[...]
            total_ref[...] = l_sc[...]
            acc_ref[...] = acc_sc[...]
            ay_ref[...] = ay_sc[...]
            ax_ref[...] = ax_sc[...]

    col = pl.BlockSpec((block_q, 1), lambda i, j: (i, 0))
    extra = () if fresh else tuple(carry)
    outs = pl.pallas_call(
        kernel,
        grid=grid,
        in_specs=[
            pl.BlockSpec((block_q, width), lambda i, j: (i, 0)),
            pl.BlockSpec((block_k, width), lambda i, j: (j, 0)),
            pl.BlockSpec((1, block_k), lambda i, j: (0, j)),
            pl.BlockSpec((1, block_k), lambda i, j: (0, j)),
        ]
        + ([] if fresh else [col, col, pl.BlockSpec((block_q, width), lambda i, j: (i, 0)), col, col]),
        out_specs=[col, col, pl.BlockSpec((block_q, width), lambda i, j: (i, 0)), col, col],
        out_shape=[
            jax.ShapeDtypeStruct((nq, 1), jnp.float32),
            jax.ShapeDtypeStruct((nq, 1), jnp.float32),
            jax.ShapeDtypeStruct((nq, width), jnp.float32),
            jax.ShapeDtypeStruct((nq, 1), jnp.float32),
            jax.ShapeDtypeStruct((nq, 1), jnp.float32),
        ],
        scratch_shapes=[
            pltpu.VMEM((block_q, 1), jnp.float32),
            pltpu.VMEM((block_q, 1), jnp.float32),
            pltpu.VMEM((block_q, width), jnp.float32),
            pltpu.VMEM((block_q, 1), jnp.float32),
            pltpu.VMEM((block_q, 1), jnp.float32),
        ],
        compiler_params=pltpu.CompilerParams(dimension_semantics=("arbitrary", "arbitrary")),
        cost_estimate=pl.CostEstimate(
            flops=4 * nq * nk * width,
            transcendentals=nq * nk,
            bytes_accessed=2 * nq * width + 2 * nk * width * grid[0] + 8 * nq * width,
        ),
    )(queries, keys, key_y.reshape(1, nk), key_x.reshape(1, nk), *extra)
    return tuple(outs)


def body(feat1, feat2):
    rows, cols, width = feat1.shape
    ncol = lax.axis_size(COL)
    full_rows = rows * lax.axis_size(BLK)
    full_cols = cols * ncol
    row_start = lax.axis_index(BLK) * rows
    col_start = lax.axis_index(COL) * cols
    scale = 1.0 / math.sqrt(width)
    tokens = rows * cols
    parts = lax.axis_size(QUERY_AXES)
    queries = lax.all_gather(feat1.reshape(tokens, width), QUERY_AXES, axis=0, tiled=True)

    def norm_y(index):
        return (index.astype(jnp.float32) + 0.5) * (2.0 / full_rows) - 1.0

    def norm_x(index):
        return (index.astype(jnp.float32) + 0.5) * (2.0 / full_cols) - 1.0

    sz, sxl, sc, sxh, sy = (lax.axis_size(a) for a in FINE)
    blocks = [feat2]
    for shift in range(1, sz):
        ring = [(i, (i + shift) % sz) for i in range(sz)]
        blocks.append(lax.ppermute(feat2, "z", ring))
    zpiece = jnp.concatenate(blocks, axis=0)
    count = zpiece.shape[0]
    gathered = jnp.arange(count, dtype=jnp.int32)
    z_from = (lax.axis_index("z") - gathered // rows) % sz
    nx = sxl * sxh
    my_x = lax.axis_index("xh") * sxl + lax.axis_index("xl")
    carry = None
    for shift in range(nx):
        if shift == 0:
            keys = zpiece
        else:
            pairs = []
            for xl in range(sxl):
                for xh in range(sxh):
                    there = (xh * sxl + xl + shift) % nx
                    pairs.append((xl * sxh + xh, (there % sxl) * sxh + there // sxl))
            keys = lax.ppermute(zpiece, ("xl", "xh"), pairs)
        x_from = (my_x - shift) % nx
        blk_of = (z_from * sxl + x_from % sxl) * sc + lax.axis_index("c")
        col_of = (x_from // sxl) * sy + lax.axis_index("y")
        tile_y = blk_of * rows + gathered % rows
        grid_y = jnp.broadcast_to(tile_y[:, None], (count, cols))
        grid_x = col_of * cols + jnp.broadcast_to(jnp.arange(cols, dtype=jnp.int32)[None, :], (count, cols))
        carry = flash_partials(
            queries,
            keys.reshape(count * cols, width),
            norm_y(grid_y).reshape(-1),
            norm_x(grid_x).reshape(-1),
            carry,
            scale,
            BLOCK_Q,
            BLOCK_K,
        )
    top, total, acc, along_y, along_x = (part[:, 0] if part.shape[1] == 1 else part for part in carry)
    stats = jnp.stack([top, total, along_y, along_x]).reshape(4, parts, tokens)
    stats = jnp.pad(stats.transpose(1, 0, 2), ((0, 0), (0, 0), (0, width - tokens)))
    packed = jnp.concatenate([acc.reshape(parts, tokens, width), stats], axis=1)
    packed = lax.all_to_all(packed, QUERY_AXES, 0, 0, tiled=True)
    tops = packed[:, tokens, :tokens]
    peak = jnp.max(tops, axis=0)
    factor = jnp.exp(tops - peak[None])
    acc = jnp.sum(packed[:, :tokens, :] * factor[:, :, None], axis=0)
    total = jnp.sum(packed[:, tokens + 1, :tokens] * factor, axis=0)
    along_y = jnp.sum(packed[:, tokens + 2, :tokens] * factor, axis=0)
    along_x = jnp.sum(packed[:, tokens + 3, :tokens] * factor, axis=0)
    warped = (acc / total[:, None]).astype(jnp.bfloat16).reshape(rows, cols, width)
    own_y = norm_y(row_start + jnp.arange(rows, dtype=jnp.int32))
    own_x = norm_x(col_start + jnp.arange(cols, dtype=jnp.int32))
    flow = jnp.stack(
        [
            (along_y / total).reshape(rows, cols) - own_y[:, None],
            (along_x / total).reshape(rows, cols) - own_x[None, :],
        ]
    )
    xval = feat1.astype(jnp.float32)
    yval = warped.astype(jnp.float32)
    margin = 2
    xpad = with_halo(feat1, ((BLK, 0), (COL, 1)), margin).astype(jnp.float32)
    both = jnp.concatenate([yval, flow.transpose(1, 2, 0)], axis=2)
    both = with_halo(both, ((BLK, 0), (COL, 1)), margin)
    ypad = both[:, :, :width]
    flow_pad = both[margin - 1 : margin + rows + 1, margin - 1 : margin + cols + 1, width:].transpose(2, 0, 1)
    first, grad_var, grad_cov = local_terms(xpad, ypad)
    cell_y = row_start - 1 + jnp.arange(rows + 2, dtype=jnp.int32)
    cell_x = col_start - 1 + jnp.arange(cols + 2, dtype=jnp.int32)
    inside = ((cell_y >= 0) & (cell_y < full_rows))[:, None] & ((cell_x >= 0) & (cell_x < full_cols))[None, :]
    inside = inside[:, :, None]
    spread_first = box_valid(jnp.where(inside, first, 0.0))
    spread_var = box_valid(jnp.where(inside, grad_var, 0.0))
    spread_cov = box_valid(jnp.where(inside, grad_cov, 0.0))
    grad_warped = spread_first + 2.0 * yval * spread_var + xval * spread_cov
    x_rows = xpad[margin - 1 : margin + rows + 1, margin : margin + cols]
    x_cols = xpad[margin : margin + rows, margin - 1 : margin + cols + 1]
    edge_y = row_start - 1 + jnp.arange(rows + 1, dtype=jnp.int32)
    valid_y = (edge_y >= 0) & (edge_y <= full_rows - 2)
    edge_x = col_start - 1 + jnp.arange(cols + 1, dtype=jnp.int32)
    valid_x = (edge_x >= 0) & (edge_x <= full_cols - 2)
    delta_y = flow_pad[:, 1:, 1:-1] - flow_pad[:, :-1, 1:-1]
    push_y = jnp.where(
        valid_y[None, :, None],
        charbonnier(edge_weight(x_rows[:-1], x_rows[1:])[None], delta_y),
        0.0,
    )
    delta_x = flow_pad[:, 1:-1, 1:] - flow_pad[:, 1:-1, :-1]
    push_x = jnp.where(
        valid_x[None, None, :],
        charbonnier(edge_weight(x_cols[:, :-1], x_cols[:, 1:])[None], delta_x),
        0.0,
    )
    grad_flow = push_y[:, :rows] - push_y[:, 1:] + push_x[:, :, :cols] - push_x[:, :, 1:]
    return (flow, grad_flow, grad_warped)


def solution(mesh):
    blk, col = mesh.devices.shape
    fine = mesh.devices.reshape(blk // 4, 2, 2, 2, col // 2)
    fine_mesh = Mesh(fine, FINE)
    placed = (P(BLK, COL, None), P(BLK, COL, None))
    return jax.shard_map(
        body,
        mesh=fine_mesh,
        in_specs=placed,
        out_specs=(P(None, BLK, COL), P(None, BLK, COL), P(BLK, COL, None)),
        check_vma=False,
    )
```

```python
import math

import jax
import jax.numpy as jnp
from jax import lax
from jax.experimental import pallas as pl
from jax.experimental.pallas import tpu as pltpu
from jax.sharding import Mesh
from jax.sharding import PartitionSpec as P

ssim_one = 0.01
ssim_two = 0.03
charb_sq = 0.0001

FINE = ("z", "xl", "c", "xh", "y")
BLK = ("z", "xl", "c")
COL = ("xh", "y")
QUERY_AXES = ("c", "y")
BLOCK_Q = 512
BLOCK_K = 1536


def with_halo(value, sides, width):
    for axis, dim in sides:
        count, length = (lax.axis_size(axis), value.shape[dim])
        up = [(i, (i + 1) % count) for i in range(count - 1)]
        down = [(j, i) for i, j in up]
        last = lax.slice_in_dim(value, length - width, length, axis=dim)
        first = lax.slice_in_dim(value, 0, width, axis=dim)
        before = lax.ppermute(last, axis, up)
        after = lax.ppermute(first, axis, down)
        value = jnp.concatenate([before, value, after], axis=dim)
    return value


def box_valid(padded):
    rows_out = padded.shape[0] - 2
    cols_out = padded.shape[1] - 2
    total = jnp.zeros((rows_out, cols_out) + padded.shape[2:], padded.dtype)
    for offset_r in range(3):
        for offset_c in range(3):
            total = total + padded[offset_r : offset_r + rows_out, offset_c : offset_c + cols_out]
    return total / 9.0


def ssim_loss(mean_y, var_y, cov_xy, mean_x, var_x):
    top = (2.0 * mean_x * mean_y + ssim_one) * (2.0 * cov_xy + ssim_two)
    bottom = (mean_x * mean_x + mean_y * mean_y + ssim_one) * (var_x + var_y + ssim_two)
    return jnp.sum((1.0 - top / bottom) * 0.5)


def local_terms(xpad, ypad):
    mean_x = box_valid(xpad)
    mean_y = box_valid(ypad)
    var_x = box_valid(xpad * xpad) - mean_x * mean_x
    var_y = box_valid(ypad * ypad) - mean_y * mean_y
    cov_xy = box_valid(xpad * ypad) - mean_x * mean_y
    loss, pull = jax.vjp(
        lambda one, two, three: ssim_loss(one, two, three, mean_x, var_x), mean_y, var_y, cov_xy
    )
    grad_mean, grad_var, grad_cov = pull(jnp.ones_like(loss))
    first = grad_mean - 2.0 * grad_var * mean_y - grad_cov * mean_x
    return (first, grad_var, grad_cov)


def edge_weight(lower, upper):
    return jnp.exp(-jnp.mean(jnp.abs(upper - lower), axis=-1))


def charbonnier(weight, delta):
    return weight * delta / jnp.sqrt(delta * delta + charb_sq)


def flash_partials(queries, keys, key_y, key_x, carry, scale, block_q, block_k):
    nq, width = queries.shape
    nk = keys.shape[0]
    grid = (nq // block_q, nk // block_k)
    last = grid[1] - 1

    fresh = carry is None

    def kernel(q_ref, k_ref, y_ref, x_ref, *refs):
        if fresh:
            refs = (None,) * 5 + refs
        top_in, total_in, acc_in, ay_in, ax_in = refs[:5]
        top_ref, total_ref, acc_ref, ay_ref, ax_ref, m_sc, l_sc, acc_sc, ay_sc, ax_sc = refs[5:]
        step = pl.program_id(1)

        @pl.when(step == 0)
        def _():
            if fresh:
                m_sc[...] = jnp.full(m_sc.shape, -1e30, jnp.float32)
                l_sc[...] = jnp.zeros(l_sc.shape, jnp.float32)
                acc_sc[...] = jnp.zeros(acc_sc.shape, jnp.float32)
                ay_sc[...] = jnp.zeros(ay_sc.shape, jnp.float32)
                ax_sc[...] = jnp.zeros(ax_sc.shape, jnp.float32)
            else:
                m_sc[...] = top_in[...]
                l_sc[...] = total_in[...]
                acc_sc[...] = acc_in[...]
                ay_sc[...] = ay_in[...]
                ax_sc[...] = ax_in[...]

        k = k_ref[...]
        score = lax.dot_general(q_ref[...], k, (((1,), (1,)), ((), ())),
                                preferred_element_type=jnp.float32)
        m_prev = m_sc[...]
        m_new = jnp.maximum(m_prev, jnp.max(score, axis=1, keepdims=True))
        shrink = jnp.exp(m_prev - m_new)
        expo = jnp.exp(score - m_new)
        l_sc[...] = l_sc[...] * shrink + jnp.sum(expo, axis=1, keepdims=True)
        ay_sc[...] = ay_sc[...] * shrink + jnp.sum(expo * y_ref[...], axis=1, keepdims=True)
        ax_sc[...] = ax_sc[...] * shrink + jnp.sum(expo * x_ref[...], axis=1, keepdims=True)
        acc_sc[...] = acc_sc[...] * shrink + jnp.dot(expo.astype(jnp.bfloat16), k,
                                                     preferred_element_type=jnp.float32)
        m_sc[...] = m_new

        @pl.when(step == last)
        def _():
            top_ref[...] = m_sc[...]
            total_ref[...] = l_sc[...]
            acc_ref[...] = acc_sc[...]
            ay_ref[...] = ay_sc[...]
            ax_ref[...] = ax_sc[...]

    col = pl.BlockSpec((block_q, 1), lambda i, j: (i, 0))
    extra = () if fresh else tuple(carry)
    outs = pl.pallas_call(
        kernel,
        grid=grid,
        in_specs=[
            pl.BlockSpec((block_q, width), lambda i, j: (i, 0)),
            pl.BlockSpec((block_k, width), lambda i, j: (j, 0)),
            pl.BlockSpec((1, block_k), lambda i, j: (0, j)),
            pl.BlockSpec((1, block_k), lambda i, j: (0, j)),
        ]
        + ([] if fresh else [col, col, pl.BlockSpec((block_q, width), lambda i, j: (i, 0)), col, col]),
        out_specs=[col, col, pl.BlockSpec((block_q, width), lambda i, j: (i, 0)), col, col],
        out_shape=[
            jax.ShapeDtypeStruct((nq, 1), jnp.float32),
            jax.ShapeDtypeStruct((nq, 1), jnp.float32),
            jax.ShapeDtypeStruct((nq, width), jnp.float32),
            jax.ShapeDtypeStruct((nq, 1), jnp.float32),
            jax.ShapeDtypeStruct((nq, 1), jnp.float32),
        ],
        scratch_shapes=[
            pltpu.VMEM((block_q, 1), jnp.float32),
            pltpu.VMEM((block_q, 1), jnp.float32),
            pltpu.VMEM((block_q, width), jnp.float32),
            pltpu.VMEM((block_q, 1), jnp.float32),
            pltpu.VMEM((block_q, 1), jnp.float32),
        ],
        compiler_params=pltpu.CompilerParams(dimension_semantics=("arbitrary", "arbitrary")),
        cost_estimate=pl.CostEstimate(
            flops=4 * nq * nk * width,
            transcendentals=nq * nk,
            bytes_accessed=2 * nq * width + 2 * nk * width * grid[0] + 8 * nq * width,
        ),
    )(queries, keys, key_y.reshape(1, nk), key_x.reshape(1, nk), *extra)
    return tuple(outs)


def body(feat1, feat2):
    rows, cols, width = feat1.shape
    ncol = lax.axis_size(COL)
    full_rows = rows * lax.axis_size(BLK)
    full_cols = cols * ncol
    row_start = lax.axis_index(BLK) * rows
    col_start = lax.axis_index(COL) * cols
    scale = 1.0 / math.sqrt(width)
    tokens = rows * cols
    parts = lax.axis_size(QUERY_AXES)
    mine = feat1.reshape(tokens, width)
    arrived = [mine]
    for shift in range(1, parts):
        ring = [(i, (i + shift) % parts) for i in range(parts)]
        arrived.append(lax.ppermute(mine, QUERY_AXES, ring))
    order = (lax.axis_index(QUERY_AXES) - jnp.arange(parts, dtype=jnp.int32)) % parts
    queries = jnp.take(jnp.stack(arrived), order, axis=0).reshape(parts * tokens, width)

    def norm_y(index):
        return (index.astype(jnp.float32) + 0.5) * (2.0 / full_rows) - 1.0

    def norm_x(index):
        return (index.astype(jnp.float32) + 0.5) * (2.0 / full_cols) - 1.0

    sz, sxl, sc, sxh, sy = (lax.axis_size(a) for a in FINE)
    blocks = [feat2]
    for shift in range(1, sz):
        ring = [(i, (i + shift) % sz) for i in range(sz)]
        blocks.append(lax.ppermute(feat2, "z", ring))
    zpiece = jnp.concatenate(blocks, axis=0)
    count = zpiece.shape[0]
    gathered = jnp.arange(count, dtype=jnp.int32)
    z_from = (lax.axis_index("z") - gathered // rows) % sz
    nx = sxl * sxh
    my_x = lax.axis_index("xh") * sxl + lax.axis_index("xl")
    carry = None
    scaled = queries * jnp.asarray(scale, queries.dtype)
    for shift in range(nx):
        if shift == 0:
            keys = zpiece
        else:
            pairs = []
            for xl in range(sxl):
                for xh in range(sxh):
                    there = (xh * sxl + xl + shift) % nx
                    pairs.append((xl * sxh + xh, (there % sxl) * sxh + there // sxl))
            keys = lax.ppermute(zpiece, ("xl", "xh"), pairs)
        x_from = (my_x - shift) % nx
        blk_of = (z_from * sxl + x_from % sxl) * sc + lax.axis_index("c")
        col_of = (x_from // sxl) * sy + lax.axis_index("y")
        tile_y = blk_of * rows + gathered % rows
        grid_y = jnp.broadcast_to(tile_y[:, None], (count, cols))
        grid_x = col_of * cols + jnp.broadcast_to(jnp.arange(cols, dtype=jnp.int32)[None, :], (count, cols))
        carry = flash_partials(
            scaled,
            keys.reshape(count * cols, width),
            norm_y(grid_y).reshape(-1),
            norm_x(grid_x).reshape(-1),
            carry,
            scale,
            BLOCK_Q,
            BLOCK_K,
        )
    top, total, acc, along_y, along_x = (part[:, 0] if part.shape[1] == 1 else part for part in carry)
    stats = jnp.stack([top, total, along_y, along_x]).reshape(4, parts, tokens)
    stats = jnp.pad(stats.transpose(1, 0, 2), ((0, 0), (0, 0), (0, width - tokens)))
    packed = jnp.concatenate([acc.reshape(parts, tokens, width), stats], axis=1)
    packed = lax.all_to_all(packed, QUERY_AXES, 0, 0, tiled=True)
    tops = packed[:, tokens, :tokens]
    peak = jnp.max(tops, axis=0)
    factor = jnp.exp(tops - peak[None])
    acc = jnp.sum(packed[:, :tokens, :] * factor[:, :, None], axis=0)
    total = jnp.sum(packed[:, tokens + 1, :tokens] * factor, axis=0)
    along_y = jnp.sum(packed[:, tokens + 2, :tokens] * factor, axis=0)
    along_x = jnp.sum(packed[:, tokens + 3, :tokens] * factor, axis=0)
    warped = (acc / total[:, None]).astype(jnp.bfloat16).reshape(rows, cols, width)
    own_y = norm_y(row_start + jnp.arange(rows, dtype=jnp.int32))
    own_x = norm_x(col_start + jnp.arange(cols, dtype=jnp.int32))
    flow = jnp.stack(
        [
            (along_y / total).reshape(rows, cols) - own_y[:, None],
            (along_x / total).reshape(rows, cols) - own_x[None, :],
        ]
    )
    xval = feat1.astype(jnp.float32)
    yval = warped.astype(jnp.float32)
    margin = 2
    xpad = with_halo(feat1, ((BLK, 0), (COL, 1)), margin).astype(jnp.float32)
    both = jnp.concatenate([yval, flow.transpose(1, 2, 0)], axis=2)
    both = with_halo(both, ((BLK, 0), (COL, 1)), margin)
    ypad = both[:, :, :width]
    flow_pad = both[margin - 1 : margin + rows + 1, margin - 1 : margin + cols + 1, width:].transpose(2, 0, 1)
    first, grad_var, grad_cov = local_terms(xpad, ypad)
    cell_y = row_start - 1 + jnp.arange(rows + 2, dtype=jnp.int32)
    cell_x = col_start - 1 + jnp.arange(cols + 2, dtype=jnp.int32)
    inside = ((cell_y >= 0) & (cell_y < full_rows))[:, None] & ((cell_x >= 0) & (cell_x < full_cols))[None, :]
    inside = inside[:, :, None]
    spread_first = box_valid(jnp.where(inside, first, 0.0))
    spread_var = box_valid(jnp.where(inside, grad_var, 0.0))
    spread_cov = box_valid(jnp.where(inside, grad_cov, 0.0))
    grad_warped = spread_first + 2.0 * yval * spread_var + xval * spread_cov
    x_rows = xpad[margin - 1 : margin + rows + 1, margin : margin + cols]
    x_cols = xpad[margin : margin + rows, margin - 1 : margin + cols + 1]
    edge_y = row_start - 1 + jnp.arange(rows + 1, dtype=jnp.int32)
    valid_y = (edge_y >= 0) & (edge_y <= full_rows - 2)
    edge_x = col_start - 1 + jnp.arange(cols + 1, dtype=jnp.int32)
    valid_x = (edge_x >= 0) & (edge_x <= full_cols - 2)
    delta_y = flow_pad[:, 1:, 1:-1] - flow_pad[:, :-1, 1:-1]
    push_y = jnp.where(
        valid_y[None, :, None],
        charbonnier(edge_weight(x_rows[:-1], x_rows[1:])[None], delta_y),
        0.0,
    )
    delta_x = flow_pad[:, 1:-1, 1:] - flow_pad[:, 1:-1, :-1]
    push_x = jnp.where(
        valid_x[None, None, :],
        charbonnier(edge_weight(x_cols[:, :-1], x_cols[:, 1:])[None], delta_x),
        0.0,
    )
    grad_flow = push_y[:, :rows] - push_y[:, 1:] + push_x[:, :, :cols] - push_x[:, :, 1:]
    return (flow, grad_flow, grad_warped)


def solution(mesh):
    blk, col = mesh.devices.shape
    fine = mesh.devices.reshape(blk // 4, 2, 2, 2, col // 2)
    fine_mesh = Mesh(fine, FINE)
    placed = (P(BLK, COL, None), P(BLK, COL, None))
    return jax.shard_map(
        body,
        mesh=fine_mesh,
        in_specs=placed,
        out_specs=(P(None, BLK, COL), P(None, BLK, COL), P(BLK, COL, None)),
        check_vma=False,
    )
```

```python
import math

import jax
import jax.numpy as jnp
from jax import lax
from jax.experimental import pallas as pl
from jax.experimental.pallas import tpu as pltpu
from jax.sharding import Mesh
from jax.sharding import PartitionSpec as P

ssim_one = 0.01
ssim_two = 0.03
charb_sq = 0.0001

FINE = ("z", "xl", "c", "xh", "y")
BLK = ("z", "xl", "c")
COL = ("xh", "y")
QUERY_AXES = ("c", "y")
BLOCK_Q = 512
BLOCK_K = 1536
CALL_GROUPS = ((0,), (1,), (2, 3))


def with_halo(value, sides, width):
    for axis, dim in sides:
        count, length = (lax.axis_size(axis), value.shape[dim])
        up = [(i, (i + 1) % count) for i in range(count - 1)]
        down = [(j, i) for i, j in up]
        last = lax.slice_in_dim(value, length - width, length, axis=dim)
        first = lax.slice_in_dim(value, 0, width, axis=dim)
        before = lax.ppermute(last, axis, up)
        after = lax.ppermute(first, axis, down)
        value = jnp.concatenate([before, value, after], axis=dim)
    return value


def box_valid(padded):
    rows_out = padded.shape[0] - 2
    cols_out = padded.shape[1] - 2
    total = jnp.zeros((rows_out, cols_out) + padded.shape[2:], padded.dtype)
    for offset_r in range(3):
        for offset_c in range(3):
            total = total + padded[offset_r : offset_r + rows_out, offset_c : offset_c + cols_out]
    return total / 9.0


def ssim_loss(mean_y, var_y, cov_xy, mean_x, var_x):
    top = (2.0 * mean_x * mean_y + ssim_one) * (2.0 * cov_xy + ssim_two)
    bottom = (mean_x * mean_x + mean_y * mean_y + ssim_one) * (var_x + var_y + ssim_two)
    return jnp.sum((1.0 - top / bottom) * 0.5)


def local_terms(xpad, ypad):
    mean_x = box_valid(xpad)
    mean_y = box_valid(ypad)
    var_x = box_valid(xpad * xpad) - mean_x * mean_x
    var_y = box_valid(ypad * ypad) - mean_y * mean_y
    cov_xy = box_valid(xpad * ypad) - mean_x * mean_y
    loss, pull = jax.vjp(
        lambda one, two, three: ssim_loss(one, two, three, mean_x, var_x), mean_y, var_y, cov_xy
    )
    grad_mean, grad_var, grad_cov = pull(jnp.ones_like(loss))
    first = grad_mean - 2.0 * grad_var * mean_y - grad_cov * mean_x
    return (first, grad_var, grad_cov)


def edge_weight(lower, upper):
    return jnp.exp(-jnp.mean(jnp.abs(upper - lower), axis=-1))


def charbonnier(weight, delta):
    return weight * delta / jnp.sqrt(delta * delta + charb_sq)


def flash_partials(queries, keys, key_y, key_x, carry, scale, block_q, block_k):
    nq, width = queries.shape
    nk = keys.shape[0]
    grid = (nq // block_q, nk // block_k)
    last = grid[1] - 1

    fresh = carry is None

    def kernel(q_ref, k_ref, y_ref, x_ref, *refs):
        if fresh:
            refs = (None,) * 5 + refs
        top_in, total_in, acc_in, ay_in, ax_in = refs[:5]
        top_ref, total_ref, acc_ref, ay_ref, ax_ref, m_sc, l_sc, acc_sc, ay_sc, ax_sc = refs[5:]
        step = pl.program_id(1)

        @pl.when(step == 0)
        def _():
            if fresh:
                m_sc[...] = jnp.full(m_sc.shape, -1e30, jnp.float32)
                l_sc[...] = jnp.zeros(l_sc.shape, jnp.float32)
                acc_sc[...] = jnp.zeros(acc_sc.shape, jnp.float32)
                ay_sc[...] = jnp.zeros(ay_sc.shape, jnp.float32)
                ax_sc[...] = jnp.zeros(ax_sc.shape, jnp.float32)
            else:
                m_sc[...] = top_in[...]
                l_sc[...] = total_in[...]
                acc_sc[...] = acc_in[...]
                ay_sc[...] = ay_in[...]
                ax_sc[...] = ax_in[...]

        k = k_ref[...]
        score = lax.dot_general(q_ref[...], k, (((1,), (1,)), ((), ())),
                                preferred_element_type=jnp.float32)
        m_prev = m_sc[...]
        m_new = jnp.maximum(m_prev, jnp.max(score, axis=1, keepdims=True))
        shrink = jnp.exp(m_prev - m_new)
        expo = jnp.exp(score - m_new)
        l_sc[...] = l_sc[...] * shrink + jnp.sum(expo, axis=1, keepdims=True)
        ay_sc[...] = ay_sc[...] * shrink + jnp.sum(expo * y_ref[...], axis=1, keepdims=True)
        ax_sc[...] = ax_sc[...] * shrink + jnp.sum(expo * x_ref[...], axis=1, keepdims=True)
        acc_sc[...] = acc_sc[...] * shrink + jnp.dot(expo.astype(jnp.bfloat16), k,
                                                     preferred_element_type=jnp.float32)
        m_sc[...] = m_new

        @pl.when(step == last)
        def _():
            top_ref[...] = m_sc[...]
            total_ref[...] = l_sc[...]
            acc_ref[...] = acc_sc[...]
            ay_ref[...] = ay_sc[...]
            ax_ref[...] = ax_sc[...]

    col = pl.BlockSpec((block_q, 1), lambda i, j: (i, 0))
    extra = () if fresh else tuple(carry)
    outs = pl.pallas_call(
        kernel,
        grid=grid,
        in_specs=[
            pl.BlockSpec((block_q, width), lambda i, j: (i, 0)),
            pl.BlockSpec((block_k, width), lambda i, j: (j, 0)),
            pl.BlockSpec((1, block_k), lambda i, j: (0, j)),
            pl.BlockSpec((1, block_k), lambda i, j: (0, j)),
        ]
        + ([] if fresh else [col, col, pl.BlockSpec((block_q, width), lambda i, j: (i, 0)), col, col]),
        out_specs=[col, col, pl.BlockSpec((block_q, width), lambda i, j: (i, 0)), col, col],
        out_shape=[
            jax.ShapeDtypeStruct((nq, 1), jnp.float32),
            jax.ShapeDtypeStruct((nq, 1), jnp.float32),
            jax.ShapeDtypeStruct((nq, width), jnp.float32),
            jax.ShapeDtypeStruct((nq, 1), jnp.float32),
            jax.ShapeDtypeStruct((nq, 1), jnp.float32),
        ],
        scratch_shapes=[
            pltpu.VMEM((block_q, 1), jnp.float32),
            pltpu.VMEM((block_q, 1), jnp.float32),
            pltpu.VMEM((block_q, width), jnp.float32),
            pltpu.VMEM((block_q, 1), jnp.float32),
            pltpu.VMEM((block_q, 1), jnp.float32),
        ],
        compiler_params=pltpu.CompilerParams(dimension_semantics=("arbitrary", "arbitrary")),
        cost_estimate=pl.CostEstimate(
            flops=4 * nq * nk * width,
            transcendentals=nq * nk,
            bytes_accessed=2 * nq * width + 2 * nk * width * grid[0] + 8 * nq * width,
        ),
    )(queries, keys, key_y.reshape(1, nk), key_x.reshape(1, nk), *extra)
    return tuple(outs)


def body(feat1, feat2):
    rows, cols, width = feat1.shape
    ncol = lax.axis_size(COL)
    full_rows = rows * lax.axis_size(BLK)
    full_cols = cols * ncol
    row_start = lax.axis_index(BLK) * rows
    col_start = lax.axis_index(COL) * cols
    scale = 1.0 / math.sqrt(width)
    tokens = rows * cols
    parts = lax.axis_size(QUERY_AXES)
    mine = feat1.reshape(tokens, width)
    arrived = [mine]
    for shift in range(1, parts):
        ring = [(i, (i + shift) % parts) for i in range(parts)]
        arrived.append(lax.ppermute(mine, QUERY_AXES, ring))
    order = (lax.axis_index(QUERY_AXES) - jnp.arange(parts, dtype=jnp.int32)) % parts
    queries = jnp.take(jnp.stack(arrived), order, axis=0).reshape(parts * tokens, width)

    def norm_y(index):
        return (index.astype(jnp.float32) + 0.5) * (2.0 / full_rows) - 1.0

    def norm_x(index):
        return (index.astype(jnp.float32) + 0.5) * (2.0 / full_cols) - 1.0

    sz, sxl, sc, sxh, sy = (lax.axis_size(a) for a in FINE)
    blocks = [feat2]
    for shift in range(1, sz):
        ring = [(i, (i + shift) % sz) for i in range(sz)]
        blocks.append(lax.ppermute(feat2, "z", ring))
    zpiece = jnp.concatenate(blocks, axis=0)
    count = zpiece.shape[0]
    gathered = jnp.arange(count, dtype=jnp.int32)
    z_from = (lax.axis_index("z") - gathered // rows) % sz
    nx = sxl * sxh
    my_x = lax.axis_index("xh") * sxl + lax.axis_index("xl")
    carry = None
    scaled = queries * jnp.asarray(scale, queries.dtype)
    staged = []
    for shift in range(nx):
        if shift == 0:
            keys = zpiece
        else:
            pairs = []
            for xl in range(sxl):
                for xh in range(sxh):
                    there = (xh * sxl + xl + shift) % nx
                    pairs.append((xl * sxh + xh, (there % sxl) * sxh + there // sxl))
            keys = lax.ppermute(zpiece, ("xl", "xh"), pairs)
        x_from = (my_x - shift) % nx
        blk_of = (z_from * sxl + x_from % sxl) * sc + lax.axis_index("c")
        col_of = (x_from // sxl) * sy + lax.axis_index("y")
        tile_y = blk_of * rows + gathered % rows
        grid_y = jnp.broadcast_to(tile_y[:, None], (count, cols))
        grid_x = col_of * cols + jnp.broadcast_to(jnp.arange(cols, dtype=jnp.int32)[None, :], (count, cols))
        staged.append((keys.reshape(count * cols, width), norm_y(grid_y).reshape(-1), norm_x(grid_x).reshape(-1)))
    for group in CALL_GROUPS:
        carry = flash_partials(
            scaled,
            jnp.concatenate([staged[s][0] for s in group], axis=0),
            jnp.concatenate([staged[s][1] for s in group], axis=0),
            jnp.concatenate([staged[s][2] for s in group], axis=0),
            carry,
            scale,
            BLOCK_Q,
            BLOCK_K,
        )
    top, total, acc, along_y, along_x = (part[:, 0] if part.shape[1] == 1 else part for part in carry)
    stats = jnp.stack([top, total, along_y, along_x]).reshape(4, parts, tokens)
    stats = jnp.pad(stats.transpose(1, 0, 2), ((0, 0), (0, 0), (0, width - tokens)))
    packed = jnp.concatenate([acc.reshape(parts, tokens, width), stats], axis=1)
    packed = lax.all_to_all(packed, QUERY_AXES, 0, 0, tiled=True)
    tops = packed[:, tokens, :tokens]
    peak = jnp.max(tops, axis=0)
    factor = jnp.exp(tops - peak[None])
    acc = jnp.sum(packed[:, :tokens, :] * factor[:, :, None], axis=0)
    total = jnp.sum(packed[:, tokens + 1, :tokens] * factor, axis=0)
    along_y = jnp.sum(packed[:, tokens + 2, :tokens] * factor, axis=0)
    along_x = jnp.sum(packed[:, tokens + 3, :tokens] * factor, axis=0)
    warped = (acc / total[:, None]).astype(jnp.bfloat16).reshape(rows, cols, width)
    own_y = norm_y(row_start + jnp.arange(rows, dtype=jnp.int32))
    own_x = norm_x(col_start + jnp.arange(cols, dtype=jnp.int32))
    flow = jnp.stack(
        [
            (along_y / total).reshape(rows, cols) - own_y[:, None],
            (along_x / total).reshape(rows, cols) - own_x[None, :],
        ]
    )
    xval = feat1.astype(jnp.float32)
    yval = warped.astype(jnp.float32)
    margin = 2
    xpad = with_halo(feat1, ((BLK, 0), (COL, 1)), margin).astype(jnp.float32)
    both = jnp.concatenate([yval, flow.transpose(1, 2, 0)], axis=2)
    both = with_halo(both, ((BLK, 0), (COL, 1)), margin)
    ypad = both[:, :, :width]
    flow_pad = both[margin - 1 : margin + rows + 1, margin - 1 : margin + cols + 1, width:].transpose(2, 0, 1)
    first, grad_var, grad_cov = local_terms(xpad, ypad)
    cell_y = row_start - 1 + jnp.arange(rows + 2, dtype=jnp.int32)
    cell_x = col_start - 1 + jnp.arange(cols + 2, dtype=jnp.int32)
    inside = ((cell_y >= 0) & (cell_y < full_rows))[:, None] & ((cell_x >= 0) & (cell_x < full_cols))[None, :]
    inside = inside[:, :, None]
    spread_first = box_valid(jnp.where(inside, first, 0.0))
    spread_var = box_valid(jnp.where(inside, grad_var, 0.0))
    spread_cov = box_valid(jnp.where(inside, grad_cov, 0.0))
    grad_warped = spread_first + 2.0 * yval * spread_var + xval * spread_cov
    x_rows = xpad[margin - 1 : margin + rows + 1, margin : margin + cols]
    x_cols = xpad[margin : margin + rows, margin - 1 : margin + cols + 1]
    edge_y = row_start - 1 + jnp.arange(rows + 1, dtype=jnp.int32)
    valid_y = (edge_y >= 0) & (edge_y <= full_rows - 2)
    edge_x = col_start - 1 + jnp.arange(cols + 1, dtype=jnp.int32)
    valid_x = (edge_x >= 0) & (edge_x <= full_cols - 2)
    delta_y = flow_pad[:, 1:, 1:-1] - flow_pad[:, :-1, 1:-1]
    push_y = jnp.where(
        valid_y[None, :, None],
        charbonnier(edge_weight(x_rows[:-1], x_rows[1:])[None], delta_y),
        0.0,
    )
    delta_x = flow_pad[:, 1:-1, 1:] - flow_pad[:, 1:-1, :-1]
    push_x = jnp.where(
        valid_x[None, None, :],
        charbonnier(edge_weight(x_cols[:, :-1], x_cols[:, 1:])[None], delta_x),
        0.0,
    )
    grad_flow = push_y[:, :rows] - push_y[:, 1:] + push_x[:, :, :cols] - push_x[:, :, 1:]
    return (flow, grad_flow, grad_warped)


def solution(mesh):
    blk, col = mesh.devices.shape
    fine = mesh.devices.reshape(blk // 4, 2, 2, 2, col // 2)
    fine_mesh = Mesh(fine, FINE)
    placed = (P(BLK, COL, None), P(BLK, COL, None))
    return jax.shard_map(
        body,
        mesh=fine_mesh,
        in_specs=placed,
        out_specs=(P(None, BLK, COL), P(None, BLK, COL), P(BLK, COL, None)),
        check_vma=False,
    )
```
